512 devices in a mesh: wide: 128 (over y, z, core), narrow: 4 (over x).
Axes of the slice: x: 4, y: 4, z: 16, core: 2. Of those that a mesh axis runs over, the one named last changes fastest.
Arguments:
- raw_echo: bfloat16 [2, 4, 1024, 16384], P(None, 'narrow', 'wide'), may hold values from -6 to 6
- range_replica: bfloat16 [2, 4096], replicated, may hold values from -0.0625 to 0.0625
- interp_weight: float32 [8, 1024], replicated, may hold values from -2.5 to 2.5
- band_offset: int32 [16384], P('wide'), may hold values from 0 to 24, as said below
- azimuth_rate: float32 [16384], P('wide'), may hold values from 0.01 to 0.1
- tile_owner: int32 [4, 16], replicated, may hold values from 0 to 3, as said below
Outputs:
- tile_mean: float32 [4, 64, 16384], P('narrow', None, 'wide')
The draws below stay inside these ranges and needn't reach their ends.
Inputs may be any that keep to these rules, and one draw needn't show every extreme that they name: band_offset reaches 24 in every draw. `tile_owner`: every tile owns at least one block of every group. One tile, the same for every group, owns exactly 8 blocks of every group; no tile owns more than 8 blocks of one group.
All inputs are finite; a program needn't handle non-finite values.
Results may differ from the reference program's by a relative error of at most 0.011.
Values may be sent and summed in bfloat16 or wider, within the bound.
No kernel may reach another device: no remote copies, remote signals or barrier semaphores. Data moves between devices by JAX's collectives and lax.ppermute only.
A program may use at most 64 MiB of HBM per device.

```python
import math
import jax
import jax.numpy as jnp
from jax import lax

NR = 16384
RSPLIT = 128
FTAPS = 4096
PUL_DEV = 8
TAPS = 8
MAXOFF = 24
BLOCKS = 16
CAP = 8
PULSE_GROUP = 1024
TILES = 4
BROWS = 64
HALO = 31


def draw_band_offset(key, part):
    values = jax.random.randint(key, (NR,), 0, MAXOFF + 1, dtype=jnp.int32)
    place = jnp.arange(NR, dtype=jnp.int32)
    return jnp.where(place % 64 == 0, MAXOFF, values).astype(jnp.int32)


def shuffle_row(row_key, row):
    return jax.random.permutation(row_key, row)


def draw_tile_owner(key, part):
    heavy_key, extra_key, order_key = jax.random.split(jax.random.fold_in(key, 7), 3)
    heavy = jax.random.randint(heavy_key, (), 0, TILES, dtype=jnp.int32)
    others = TILES - 1
    spare = BLOCKS - CAP - others
    loaded = jnp.zeros((TILES, CAP), jnp.int32) + heavy
    cover = (heavy + 1 + jnp.arange(others, dtype=jnp.int32)) % TILES
    cover = jnp.zeros((TILES, others), jnp.int32) + cover[None, :]
    extra = (heavy + 1 + jax.random.randint(extra_key, (TILES, spare), 0, others, dtype=jnp.int32)) % TILES
    whole = jnp.concatenate([loaded, cover, extra], axis=1).astype(jnp.int32)
    row_keys = jax.random.split(order_key, TILES)
    return jax.vmap(shuffle_row)(row_keys, whole).astype(jnp.int32)


def block_levels(own_key, shape, cuts, low, top_value):
    def one(position, parts):
        steps = jax.random.uniform(jax.random.fold_in(jax.random.fold_in(own_key, 6), position), (parts,), jnp.float32, low / len(cuts), top_value / len(cuts))
        return jnp.repeat(jnp.exp(steps), shape[position] // parts).reshape((-1,) + (1,) * (len(shape) - position - 1))

    level = one(*cuts[0])
    for cut in cuts[1:]:
        level = level * one(*cut)
    return level


def scatter_about(rng, extent, scale, reach, shards=(), held_as=jnp.bfloat16):
    loudness = block_levels(rng, extent, shards, -0.22, 0.18) if shards else 1.0
    result = jax.random.normal(rng, extent, jnp.float32) * scale * loudness
    return jnp.minimum(jnp.maximum(result, -reach), reach).astype(held_as)


def setup_inputs(seed: int = 0) -> dict:
    arg_keys = jax.random.split(jax.random.key(seed), 7)
    return {
        "raw_echo": scatter_about(arg_keys[0], (2, TILES, PULSE_GROUP, NR), 1.0, 6.0, ((1, 4), (2, 128))),
        "range_replica": scatter_about(arg_keys[1], (2, FTAPS), (2 * FTAPS) ** -0.5, 0.0625),
        "interp_weight": scatter_about(arg_keys[2], (TAPS, PULSE_GROUP), 0.35, 2.5, (), jnp.float32),
        "band_offset": draw_band_offset(jax.random.fold_in(arg_keys[6], 71), 0),
        "azimuth_rate": jnp.clip(jnp.exp(math.log(0.1) - 2.3025851 * jax.random.uniform(arg_keys[4], (NR,), jnp.float32) ** block_levels(arg_keys[4], (NR,), ((0, 128),), -0.2, 0.2)), 0.01, 0.1),
        "tile_owner": draw_tile_owner(jax.random.fold_in(arg_keys[6], 71), 0),
    }


def contract(form, left, right):
    return jnp.einsum(form, left.astype(jnp.float32), right.astype(jnp.float32), precision=lax.Precision.HIGHEST)

def make_table(size, sign):
    index = jnp.arange(size, dtype=jnp.int32)
    product = index[:, None] * index[None, :] % size
    angle = sign * 2.0 * math.pi / size * product.astype(jnp.float32)
    norm = 1.0 / math.sqrt(size)
    return ((jnp.cos(angle) * norm).astype(jnp.bfloat16), (jnp.sin(angle) * norm).astype(jnp.bfloat16))

def make_twiddle(first, second, sign):
    heads = jnp.arange(first, dtype=jnp.int32)
    tails = jnp.arange(second, dtype=jnp.int32)
    product = heads[:, None] * tails[None, :] % (first * second)
    angle = sign * 2.0 * math.pi / (first * second) * product.astype(jnp.float32)
    return (jnp.cos(angle), jnp.sin(angle))

def range_transform(real_part, imag_part, first, sign):
    count = real_part.shape[0]
    length = real_part.shape[1]
    second = length // first
    head_cos, head_sin = make_table(first, sign)
    tail_cos, tail_sin = make_table(second, sign)
    twist_cos, twist_sin = make_twiddle(first, second, sign)
    split_real = real_part.reshape(count, first, second)
    split_imag = imag_part.reshape(count, first, second)

    def section_one(table, values):
        return contract('kn,pnm->pkm', table, values)
    mid_real = section_one(head_cos, split_real) - section_one(head_sin, split_imag)
    mid_imag = section_one(head_cos, split_imag) + section_one(head_sin, split_real)
    turn_real = (mid_real * twist_cos - mid_imag * twist_sin).astype(jnp.bfloat16)
    turn_imag = (mid_real * twist_sin + mid_imag * twist_cos).astype(jnp.bfloat16)

    def section_two(table, values):
        return contract('pam,km->pka', values, table)
    out_real = section_two(tail_cos, turn_real) - section_two(tail_sin, turn_imag)
    out_imag = section_two(tail_cos, turn_imag) + section_two(tail_sin, turn_real)
    return (out_real.reshape(count, length), out_imag.reshape(count, length))

def pulse_transform(real_part, imag_part, first, sign):
    length = real_part.shape[0]
    width = real_part.shape[1]
    second = length // first
    head_cos, head_sin = make_table(first, sign)
    tail_cos, tail_sin = make_table(second, sign)
    twist_cos, twist_sin = make_twiddle(first, second, sign)
    twist_cos = twist_cos[:, :, None]
    twist_sin = twist_sin[:, :, None]
    split_real = real_part.reshape(first, second, width)
    split_imag = imag_part.reshape(first, second, width)

    def section_one(table, values):
        return contract('kn,nmc->kmc', table, values)
    mid_real = section_one(head_cos, split_real) - section_one(head_sin, split_imag)
    mid_imag = section_one(head_cos, split_imag) + section_one(head_sin, split_real)
    turn_real = (mid_real * twist_cos - mid_imag * twist_sin).astype(jnp.bfloat16)
    turn_imag = (mid_real * twist_sin + mid_imag * twist_cos).astype(jnp.bfloat16)

    def section_two(table, values):
        return contract('kmc,jm->jkc', values, table)
    out_real = section_two(tail_cos, turn_real) - section_two(tail_sin, turn_imag)
    out_imag = section_two(tail_cos, turn_imag) + section_two(tail_sin, turn_real)
    return (out_real.reshape(length, width), out_imag.reshape(length, width))

def reference(raw_echo, range_replica, interp_weight, band_offset, azimuth_rate, tile_owner):
    padded = jnp.pad(range_replica, ((0, 0), (0, NR - FTAPS)))
    replica_real, replica_imag = range_transform(padded[0:1], padded[1:2], RSPLIT, -1)
    scale = math.sqrt(NR)
    replica_real = replica_real[0] * scale
    replica_imag = replica_imag[0] * scale
    bins = jnp.arange(NR, dtype=jnp.int32) + band_offset.astype(jnp.int32)
    freq = jnp.arange(PULSE_GROUP, dtype=jnp.int32)
    shifted = ((freq + PULSE_GROUP // 2) % PULSE_GROUP - PULSE_GROUP // 2).astype(jnp.float32) / PULSE_GROUP
    phase = math.pi * (shifted * shifted)[:, None] / azimuth_rate[None, :]
    phase_cos = jnp.cos(phase)
    phase_sin = jnp.sin(phase)

    def focus(group_echo):
        spec_real, spec_imag = range_transform(group_echo[0], group_echo[1], RSPLIT, -1)
        match_real = (spec_real * replica_real + spec_imag * replica_imag).astype(jnp.bfloat16)
        match_imag = (spec_imag * replica_real - spec_real * replica_imag).astype(jnp.bfloat16)
        comp_real, comp_imag = range_transform(match_real, match_imag, RSPLIT, 1)
        comp_real = comp_real.astype(jnp.bfloat16)
        comp_imag = comp_imag.astype(jnp.bfloat16)
        dop_real, dop_imag = pulse_transform(comp_real, comp_imag, PUL_DEV, -1)
        dop_real = jnp.pad(dop_real.astype(jnp.bfloat16), ((0, 0), (0, HALO)))
        dop_imag = jnp.pad(dop_imag.astype(jnp.bfloat16), ((0, 0), (0, HALO)))
        moved_real = jnp.zeros((PULSE_GROUP, NR), jnp.float32)
        moved_imag = jnp.zeros((PULSE_GROUP, NR), jnp.float32)
        for tap_index in range(TAPS):
            weight = interp_weight[tap_index][:, None]
            moved_real = moved_real + weight * jnp.take(dop_real, bins + tap_index, axis=1).astype(jnp.float32)
            moved_imag = moved_imag + weight * jnp.take(dop_imag, bins + tap_index, axis=1).astype(jnp.float32)
        focus_real = (moved_real * phase_cos - moved_imag * phase_sin).astype(jnp.bfloat16)
        focus_imag = (moved_real * phase_sin + moved_imag * phase_cos).astype(jnp.bfloat16)
        image_real, image_imag = pulse_transform(focus_real, focus_imag, PUL_DEV, 1)
        return (image_real * image_real + image_imag * image_imag).astype(jnp.bfloat16)
    intensity = lax.map(focus, jnp.transpose(raw_echo, (1, 0, 2, 3)))
    blocks = intensity.reshape(TILES, BLOCKS, BROWS, NR)
    onehot = (tile_owner[:, :, None] == jnp.arange(TILES, dtype=jnp.int32)[None, None, :]).astype(jnp.float32)
    totals = jnp.einsum('gbt,gbir->tir', onehot, blocks.astype(jnp.float32), precision=lax.Precision.HIGHEST)
    counts = lax.optimization_barrier(jnp.sum(onehot, axis=(0, 1)))
    return totals / counts[:, None, None]
```

```python
import math

import jax
import jax.numpy as jnp
import ml_dtypes
import numpy as np
from jax import lax
from jax.experimental import pallas as pl
from jax.experimental.pallas import tpu as pltpu
from jax.sharding import PartitionSpec as P

RSPLIT = 128
PUL_DEV = 8
CAP = 8
HALO = 31


def passed_along(shard, axis, by):
    devices = lax.axis_size(axis)
    pairs = [(i, i + by) for i in range(devices) if 0 <= i + by < devices]
    return lax.ppermute(shard, axis, pairs)


def make_table(size, sign):
    index = jnp.arange(size, dtype=jnp.int32)
    product = index[:, None] * index[None, :] % size
    angle = sign * 2.0 * math.pi / size * product.astype(jnp.float32)
    norm = 1.0 / math.sqrt(size)
    return (
        (jnp.cos(angle) * norm).astype(jnp.bfloat16),
        (jnp.sin(angle) * norm).astype(jnp.bfloat16),
    )


def make_twiddle(first, second, sign):
    heads = jnp.arange(first, dtype=jnp.int32)
    tails = jnp.arange(second, dtype=jnp.int32)
    product = heads[:, None] * tails[None, :] % (first * second)
    angle = sign * 2.0 * math.pi / (first * second) * product.astype(jnp.float32)
    return (jnp.cos(angle), jnp.sin(angle))


def host_block_table(size, sign):
    index = np.arange(size, dtype=np.int64)
    product = (index[:, None] * index[None, :] % size).astype(np.float32)
    angle = np.float32(sign * 2.0 * math.pi / size) * product
    norm = np.float32(1.0 / math.sqrt(size))
    cos = (np.cos(angle) * norm).astype(ml_dtypes.bfloat16)
    sin = (np.sin(angle) * norm).astype(ml_dtypes.bfloat16)
    top = np.concatenate([cos, -sin], axis=1)
    bottom = np.concatenate([sin, cos], axis=1)
    return np.concatenate([top, bottom], axis=0)


def host_twiddle(first, second, sign):
    heads = np.arange(first, dtype=np.int64)
    tails = np.arange(second, dtype=np.int64)
    product = (heads[:, None] * tails[None, :] % (first * second)).astype(np.float32)
    angle = np.float32(sign * 2.0 * math.pi / (first * second)) * product
    return np.stack([np.cos(angle), np.sin(angle)]).astype(np.float32)


def square_transform(stacked, table, twiddle):
    half = stacked.shape[0] // 2
    mid = jnp.dot(table, stacked, preferred_element_type=jnp.float32)
    mid_real, mid_imag = mid[:half], mid[half:]
    twist_cos, twist_sin = twiddle[0], twiddle[1]
    turn_real = (mid_real * twist_cos - mid_imag * twist_sin).astype(jnp.bfloat16)
    turn_imag = (mid_real * twist_sin + mid_imag * twist_cos).astype(jnp.bfloat16)
    turned = jnp.concatenate([turn_real, turn_imag], axis=1)
    out = lax.dot_general(
        table, turned, (((1,), (1,)), ((), ())), preferred_element_type=jnp.float32
    )
    return out[:half], out[half:]


def range_kernel(echo_ref, replica_ref, fwd_ref, inv_ref, fwd_tw_ref, inv_tw_ref, out_ref, rep_ref):
    fwd = fwd_ref[...]
    fwd_tw = fwd_tw_ref[...]

    @pl.when(pl.program_id(0) == 0)
    def _():
        rep_real, rep_imag = square_transform(replica_ref[...], fwd, fwd_tw)
        rep_ref[0] = rep_real * 128.0
        rep_ref[1] = rep_imag * 128.0

    pulse = echo_ref[:, 0]
    stacked = jnp.concatenate([pulse[0], pulse[1]], axis=0)
    spec_real, spec_imag = square_transform(stacked, fwd, fwd_tw)
    rep_real = rep_ref[0]
    rep_imag = rep_ref[1]
    match_real = (spec_real * rep_real + spec_imag * rep_imag).astype(jnp.bfloat16)
    match_imag = (spec_imag * rep_real - spec_real * rep_imag).astype(jnp.bfloat16)
    matched = jnp.concatenate([match_real, match_imag], axis=0)
    comp_real, comp_imag = square_transform(matched, inv_ref[...], inv_tw_ref[...])
    out_ref[0, 0] = comp_real.astype(jnp.bfloat16)
    out_ref[1, 0] = comp_imag.astype(jnp.bfloat16)


def range_compress(echo, range_replica):
    pulses, length = echo.shape[1], echo.shape[2]
    side = RSPLIT
    assert length == side * side
    padded = jnp.pad(range_replica, ((0, 0), (0, length - range_replica.shape[1])))
    replica = padded.reshape(2 * side, side)
    fwd = jnp.asarray(host_block_table(side, -1))
    inv = jnp.asarray(host_block_table(side, 1))
    fwd_tw = jnp.asarray(host_twiddle(side, side, -1))
    inv_tw = jnp.asarray(host_twiddle(side, side, 1))
    full = lambda shape: pl.BlockSpec(shape, lambda p: (0,) * len(shape))
    out = pl.pallas_call(
        range_kernel,
        grid=(pulses,),
        in_specs=[
            pl.BlockSpec((2, 1, side, side), lambda p: (0, p, 0, 0)),
            full((2 * side, side)),
            full((2 * side, 2 * side)),
            full((2 * side, 2 * side)),
            full((2, side, side)),
            full((2, side, side)),
        ],
        out_specs=pl.BlockSpec((2, 1, side, side), lambda p: (0, p, 0, 0)),
        out_shape=jax.ShapeDtypeStruct((2, pulses, side, side), jnp.bfloat16),
        scratch_shapes=[pltpu.VMEM((2, side, side), jnp.float32)],
        compiler_params=pltpu.CompilerParams(dimension_semantics=("arbitrary",)),
        cost_estimate=pl.CostEstimate(
            flops=pulses * 4 * 2 * (2 * side) ** 2 * side,
            bytes_accessed=pulses * 2 * 2 * length * 2,
            transcendentals=0,
        ),
    )(echo.reshape(2, pulses, side, side), replica, fwd, inv, fwd_tw, inv_tw)
    return out.reshape(2, pulses, length)


def pulse_transform(real_part, imag_part, first, sign):
    length = real_part.shape[0]
    width = real_part.shape[1]
    second = length // first
    head_cos, head_sin = make_table(first, sign)
    tail_cos, tail_sin = make_table(second, sign)
    twist_cos, twist_sin = make_twiddle(first, second, sign)
    twist_cos = twist_cos[:, :, None]
    twist_sin = twist_sin[:, :, None]
    split_real = real_part.reshape(first, second, width)
    split_imag = imag_part.reshape(first, second, width)

    def section_one(table, values):
        return jnp.einsum("kn,nmc->kmc", table, values, preferred_element_type=jnp.float32)

    mid_real = section_one(head_cos, split_real) - section_one(head_sin, split_imag)
    mid_imag = section_one(head_cos, split_imag) + section_one(head_sin, split_real)
    turn_real = (mid_real * twist_cos - mid_imag * twist_sin).astype(jnp.bfloat16)
    turn_imag = (mid_real * twist_sin + mid_imag * twist_cos).astype(jnp.bfloat16)

    def section_two(table, values):
        return jnp.einsum("kmc,jm->jkc", values, table, preferred_element_type=jnp.float32)

    out_real = section_two(tail_cos, turn_real) - section_two(tail_sin, turn_imag)
    out_imag = section_two(tail_cos, turn_imag) + section_two(tail_sin, turn_real)
    return (out_real.reshape(length, width), out_imag.reshape(length, width))


def azimuth_spectra(values):
    first_real, first_imag = pulse_transform(values[0, :, 0], values[1, :, 0], PUL_DEV, -1)
    return jnp.stack([first_real.astype(jnp.bfloat16), first_imag.astype(jnp.bfloat16)])[
        :, :, None, :
    ]


def per_device(raw_echo, range_replica, interp_weight, band_offset, azimuth_rate, tile_owner):
    echo = raw_echo[:, 0]
    length = echo.shape[2]
    compressed = range_compress(echo, range_replica)
    devices = lax.axis_size("wide")
    width = length // devices
    local_pulses = compressed.shape[1]
    split_bins = compressed.reshape(2, local_pulses, devices, width)
    doppler = azimuth_spectra(
        lax.all_to_all(split_bins, "wide", split_axis=2, concat_axis=1, tiled=True)
    )[:, :, 0]
    rim = passed_along(doppler[:, :, :HALO], "wide", -1)
    extended = jnp.concatenate([doppler, rim], axis=2)
    pulses = extended.shape[1]
    columns = jnp.arange(width + HALO, dtype=jnp.int32)
    bins = jnp.arange(width, dtype=jnp.int32) + band_offset
    moved_real = jnp.zeros((pulses, width), jnp.float32)
    moved_imag = jnp.zeros((pulses, width), jnp.float32)
    for tap_index in range(interp_weight.shape[0]):
        select = (columns[:, None] == (bins + tap_index)[None, :]).astype(jnp.bfloat16)
        picked = jnp.einsum("xpc,cr->xpr", extended, select, preferred_element_type=jnp.float32)
        weight = interp_weight[tap_index][:, None]
        moved_real = moved_real + weight * picked[0]
        moved_imag = moved_imag + weight * picked[1]
    half = pulses // 2
    freq = jnp.arange(half + 1, dtype=jnp.int32)
    shifted = ((freq + half) % pulses - half).astype(jnp.float32) / pulses
    phase = math.pi * (shifted * shifted)[:, None] / azimuth_rate[None, :]
    half_cos = jnp.cos(phase)
    half_sin = jnp.sin(phase)
    phase_cos = jnp.concatenate([half_cos, jnp.flip(half_cos[1:half], 0)], axis=0)
    phase_sin = jnp.concatenate([half_sin, jnp.flip(half_sin[1:half], 0)], axis=0)
    focus_real = (moved_real * phase_cos - moved_imag * phase_sin).astype(jnp.bfloat16)
    focus_imag = (moved_real * phase_sin + moved_imag * phase_cos).astype(jnp.bfloat16)
    image_real, image_imag = pulse_transform(focus_real, focus_imag, PUL_DEV, 1)
    intensity = (image_real * image_real + image_imag * image_imag).astype(jnp.bfloat16)
    block_count = tile_owner.shape[1]
    block_rows = pulses // block_count
    blocks = intensity.reshape(block_count, block_rows * width)
    tiles = lax.axis_size("narrow")
    group = lax.axis_index("narrow")
    tile_ids = jnp.arange(tiles, dtype=jnp.int32)
    own_row = lax.dynamic_slice_in_dim(tile_owner, group, 1, 0)[0]
    member = (own_row[None, :] == tile_ids[:, None]).astype(jnp.bfloat16)
    counts = jnp.sum(
        (tile_owner[:, :, None] == tile_ids[None, None, :]).astype(jnp.int32), axis=(0, 1)
    )
    own_count = jnp.sum(jnp.where(tile_ids == group, counts, 0)).astype(jnp.float32)
    partial = jnp.dot(member, blocks, preferred_element_type=jnp.float32)
    partial = partial.reshape(tiles, block_rows, width)
    incoming = lax.all_to_all(partial, "narrow", split_axis=0, concat_axis=0, tiled=True)
    summed = jnp.sum(incoming, axis=0)[None]
    return summed / own_count


def solution(mesh):
    return jax.shard_map(
        per_device,
        mesh=mesh,
        in_specs=(P(None, "narrow", "wide", None), P(), P(), P("wide"), P("wide"), P()),
        out_specs=P("narrow", None, "wide"),
        check_vma=False,
    )
```

```python
import math

import jax
import jax.numpy as jnp
import ml_dtypes
import numpy as np
from jax import lax
from jax.experimental import pallas as pl
from jax.experimental.pallas import tpu as pltpu
from jax.sharding import PartitionSpec as P

RSPLIT = 128
PUL_DEV = 8
CAP = 8
HALO = 31


def passed_along(shard, axis, by):
    devices = lax.axis_size(axis)
    pairs = [(i, i + by) for i in range(devices) if 0 <= i + by < devices]
    return lax.ppermute(shard, axis, pairs)


def make_table(size, sign):
    index = jnp.arange(size, dtype=jnp.int32)
    product = index[:, None] * index[None, :] % size
    angle = sign * 2.0 * math.pi / size * product.astype(jnp.float32)
    norm = 1.0 / math.sqrt(size)
    return (
        (jnp.cos(angle) * norm).astype(jnp.bfloat16),
        (jnp.sin(angle) * norm).astype(jnp.bfloat16),
    )


def make_twiddle(first, second, sign):
    heads = jnp.arange(first, dtype=jnp.int32)
    tails = jnp.arange(second, dtype=jnp.int32)
    product = heads[:, None] * tails[None, :] % (first * second)
    angle = sign * 2.0 * math.pi / (first * second) * product.astype(jnp.float32)
    return (jnp.cos(angle), jnp.sin(angle))


def host_twiddle(first, second, sign):
    heads = np.arange(first, dtype=np.int64)
    tails = np.arange(second, dtype=np.int64)
    product = (heads[:, None] * tails[None, :] % (first * second)).astype(np.float32)
    angle = np.float32(sign * 2.0 * math.pi / (first * second)) * product
    return np.stack([np.cos(angle), np.sin(angle)]).astype(np.float32)


def host_tables(size, sign):
    index = np.arange(size, dtype=np.int64)
    product = (index[:, None] * index[None, :] % size).astype(np.float32)
    angle = np.float32(sign * 2.0 * math.pi / size) * product
    norm = np.float32(1.0 / math.sqrt(size))
    cos = (np.cos(angle) * norm).astype(ml_dtypes.bfloat16)
    sin = (np.sin(angle) * norm).astype(ml_dtypes.bfloat16)
    table = np.block([[cos, -sin], [sin, cos]])
    return table, np.ascontiguousarray(table.T)


def twist(mid_real, mid_imag, twiddle):
    twist_cos, twist_sin = twiddle[0], twiddle[1]
    turn_real = (mid_real * twist_cos - mid_imag * twist_sin).astype(jnp.bfloat16)
    turn_imag = (mid_real * twist_sin + mid_imag * twist_cos).astype(jnp.bfloat16)
    return turn_real, turn_imag


def forward_transposed(stacked, table, table_t, twiddle):
    half = stacked.shape[0] // 2
    mid = jnp.dot(table, stacked, preferred_element_type=jnp.float32)
    turn_real, turn_imag = twist(mid[:half], mid[half:], twiddle)
    spec = jnp.dot(
        jnp.concatenate([turn_real, turn_imag], axis=1), table_t, preferred_element_type=jnp.float32
    )
    return spec[:, :half], spec[:, half:]


def inverse_from_transposed(real_t, imag_t, table, table_t, twiddle):
    half = real_t.shape[0]
    mid = jnp.dot(
        jnp.concatenate([real_t, imag_t], axis=1), table_t, preferred_element_type=jnp.float32
    )
    turn_real, turn_imag = twist(mid[:, :half], mid[:, half:], twiddle)
    out = jnp.dot(
        table, jnp.concatenate([turn_real, turn_imag], axis=0), preferred_element_type=jnp.float32
    )
    return out[:half], out[half:]


def range_kernel(
    echo_ref, replica_ref, fwd_ref, fwd_t_ref, inv_ref, inv_t_ref, fwd_tw_ref, inv_tw_ref, out_ref, wide_ref
):
    pulses = echo_ref.shape[1] // echo_ref.shape[2]
    side = echo_ref.shape[2]
    fwd, fwd_t = fwd_ref[...], fwd_t_ref[...]
    inv, inv_t = inv_ref[...], inv_t_ref[...]
    fwd_tw, inv_tw = fwd_tw_ref[...], inv_tw_ref[...]
    rep_real, rep_imag = forward_transposed(replica_ref[...], fwd, fwd_t, fwd_tw)
    rep_real = rep_real * 128.0
    rep_imag = rep_imag * 128.0
    for pulse in range(pulses):
        rows = pl.ds(pulse, side, stride=pulses)
        stacked = jnp.concatenate([echo_ref[0, rows, :], echo_ref[1, rows, :]], axis=0)
        spec_real, spec_imag = forward_transposed(stacked, fwd, fwd_t, fwd_tw)
        match_real = (spec_real * rep_real + spec_imag * rep_imag).astype(jnp.bfloat16)
        match_imag = (spec_imag * rep_real - spec_real * rep_imag).astype(jnp.bfloat16)
        comp_real, comp_imag = inverse_from_transposed(match_real, match_imag, inv, inv_t, inv_tw)
        wide_ref[pl.ds(pulse, side, stride=2 * pulses), :] = comp_real
        wide_ref[pl.ds(pulses + pulse, side, stride=2 * pulses), :] = comp_imag
    out_ref[...] = wide_ref[...].astype(jnp.bfloat16)


def range_compress(echo, range_replica):
    pulses, length = echo.shape[1], echo.shape[2]
    side = RSPLIT
    assert length == side * side
    padded = jnp.pad(range_replica, ((0, 0), (0, length - range_replica.shape[1])))
    replica = padded.reshape(2 * side, side)
    rows = echo.reshape(2, pulses, side, side).transpose(0, 2, 1, 3).reshape(2, side * pulses, side)
    fwd, fwd_t = host_tables(side, -1)
    inv, inv_t = host_tables(side, 1)
    fwd_tw = host_twiddle(side, side, -1)
    inv_tw = host_twiddle(side, side, 1)
    whole = pl.BlockSpec(memory_space=pltpu.VMEM)
    out = pl.pallas_call(
        range_kernel,
        in_specs=[whole] * 8,
        out_specs=whole,
        out_shape=jax.ShapeDtypeStruct((side * 2 * pulses, side), jnp.bfloat16),
        scratch_shapes=[pltpu.VMEM((side * 2 * pulses, side), jnp.float32)],
        cost_estimate=pl.CostEstimate(
            flops=(pulses + 1) * 4 * 2 * (2 * side) ** 2 * side,
            bytes_accessed=pulses * 2 * 2 * length * 2,
            transcendentals=0,
        ),
    )(
        rows,
        replica,
        jnp.asarray(fwd),
        jnp.asarray(fwd_t),
        jnp.asarray(inv),
        jnp.asarray(inv_t),
        jnp.asarray(fwd_tw),
        jnp.asarray(inv_tw),
    )
    return out.reshape(side, 2, pulses, side)


def pulse_transform(real_part, imag_part, first, sign):
    length = real_part.shape[0]
    width = real_part.shape[1]
    second = length // first
    head_cos, head_sin = make_table(first, sign)
    tail_cos, tail_sin = make_table(second, sign)
    twist_cos, twist_sin = make_twiddle(first, second, sign)
    twist_cos = twist_cos[:, :, None]
    twist_sin = twist_sin[:, :, None]
    split_real = real_part.reshape(first, second, width)
    split_imag = imag_part.reshape(first, second, width)

    def section_one(table, values):
        return jnp.einsum("kn,nmc->kmc", table, values, preferred_element_type=jnp.float32)

    mid_real = section_one(head_cos, split_real) - section_one(head_sin, split_imag)
    mid_imag = section_one(head_cos, split_imag) + section_one(head_sin, split_real)
    turn_real = (mid_real * twist_cos - mid_imag * twist_sin).astype(jnp.bfloat16)
    turn_imag = (mid_real * twist_sin + mid_imag * twist_cos).astype(jnp.bfloat16)

    def section_two(table, values):
        return jnp.einsum("kmc,jm->jkc", values, table, preferred_element_type=jnp.float32)

    out_real = section_two(tail_cos, turn_real) - section_two(tail_sin, turn_imag)
    out_imag = section_two(tail_cos, turn_imag) + section_two(tail_sin, turn_real)
    return (out_real.reshape(length, width), out_imag.reshape(length, width))


def azimuth_spectra(values):
    first_real, first_imag = pulse_transform(values[0, :, 0], values[1, :, 0], PUL_DEV, -1)
    return jnp.stack([first_real.astype(jnp.bfloat16), first_imag.astype(jnp.bfloat16)])[
        :, :, None, :
    ]


def per_device(raw_echo, range_replica, interp_weight, band_offset, azimuth_rate, tile_owner):
    echo = raw_echo[:, 0]
    length = echo.shape[2]
    compressed = range_compress(echo, range_replica)
    devices = lax.axis_size("wide")
    width = length // devices
    assert compressed.shape[0] == devices and compressed.shape[3] == width
    turned = lax.all_to_all(compressed, "wide", split_axis=0, concat_axis=2, tiled=True)[0]
    doppler = azimuth_spectra(turned[:, :, None, :])[:, :, 0]
    rim = passed_along(doppler[:, :, :HALO], "wide", -1)
    extended = jnp.concatenate([doppler, rim], axis=2)
    pulses = extended.shape[1]
    columns = jnp.arange(width + HALO, dtype=jnp.int32)
    bins = jnp.arange(width, dtype=jnp.int32) + band_offset
    moved_real = jnp.zeros((pulses, width), jnp.float32)
    moved_imag = jnp.zeros((pulses, width), jnp.float32)
    for tap_index in range(interp_weight.shape[0]):
        select = (columns[:, None] == (bins + tap_index)[None, :]).astype(jnp.bfloat16)
        picked = jnp.einsum("xpc,cr->xpr", extended, select, preferred_element_type=jnp.float32)
        weight = interp_weight[tap_index][:, None]
        moved_real = moved_real + weight * picked[0]
        moved_imag = moved_imag + weight * picked[1]
    half = pulses // 2
    freq = jnp.arange(half + 1, dtype=jnp.int32)
    shifted = ((freq + half) % pulses - half).astype(jnp.float32) / pulses
    phase = math.pi * (shifted * shifted)[:, None] / azimuth_rate[None, :]
    half_cos = jnp.cos(phase)
    half_sin = jnp.sin(phase)
    phase_cos = jnp.concatenate([half_cos, jnp.flip(half_cos[1:half], 0)], axis=0)
    phase_sin = jnp.concatenate([half_sin, jnp.flip(half_sin[1:half], 0)], axis=0)
    focus_real = (moved_real * phase_cos - moved_imag * phase_sin).astype(jnp.bfloat16)
    focus_imag = (moved_real * phase_sin + moved_imag * phase_cos).astype(jnp.bfloat16)
    image_real, image_imag = pulse_transform(focus_real, focus_imag, PUL_DEV, 1)
    intensity = (image_real * image_real + image_imag * image_imag).astype(jnp.bfloat16)
    block_count = tile_owner.shape[1]
    block_rows = pulses // block_count
    blocks = intensity.reshape(block_count, block_rows * width)
    tiles = lax.axis_size("narrow")
    group = lax.axis_index("narrow")
    tile_ids = jnp.arange(tiles, dtype=jnp.int32)
    own_row = lax.dynamic_slice_in_dim(tile_owner, group, 1, 0)[0]
    member = (own_row[None, :] == tile_ids[:, None]).astype(jnp.bfloat16)
    counts = jnp.sum(
        (tile_owner[:, :, None] == tile_ids[None, None, :]).astype(jnp.int32), axis=(0, 1)
    )
    own_count = jnp.sum(jnp.where(tile_ids == group, counts, 0)).astype(jnp.float32)
    partial = jnp.dot(member, blocks, preferred_element_type=jnp.float32)
    partial = partial.reshape(tiles, block_rows, width)
    incoming = lax.all_to_all(partial, "narrow", split_axis=0, concat_axis=0, tiled=True)
    summed = jnp.sum(incoming, axis=0)[None]
    return summed / own_count


def solution(mesh):
    return jax.shard_map(
        per_device,
        mesh=mesh,
        in_specs=(P(None, "narrow", "wide", None), P(), P(), P("wide"), P("wide"), P()),
        out_specs=P("narrow", None, "wide"),
        check_vma=False,
    )
```

```python
import math

import jax
import jax.numpy as jnp
import ml_dtypes
import numpy as np
from jax import lax
from jax.experimental import pallas as pl
from jax.experimental.pallas import tpu as pltpu
from jax.sharding import PartitionSpec as P

RSPLIT = 128
PUL_DEV = 8
CAP = 8
HALO = 31


def passed_along(shard, axis, by):
    devices = lax.axis_size(axis)
    pairs = [(i, i + by) for i in range(devices) if 0 <= i + by < devices]
    return lax.ppermute(shard, axis, pairs)


def make_table(size, sign):
    index = jnp.arange(size, dtype=jnp.int32)
    product = index[:, None] * index[None, :] % size
    angle = sign * 2.0 * math.pi / size * product.astype(jnp.float32)
    norm = 1.0 / math.sqrt(size)
    return (
        (jnp.cos(angle) * norm).astype(jnp.bfloat16),
        (jnp.sin(angle) * norm).astype(jnp.bfloat16),
    )


def make_twiddle(first, second, sign):
    heads = jnp.arange(first, dtype=jnp.int32)
    tails = jnp.arange(second, dtype=jnp.int32)
    product = heads[:, None] * tails[None, :] % (first * second)
    angle = sign * 2.0 * math.pi / (first * second) * product.astype(jnp.float32)
    return (jnp.cos(angle), jnp.sin(angle))


def host_twiddle(first, second, sign):
    heads = np.arange(first, dtype=np.int64)
    tails = np.arange(second, dtype=np.int64)
    product = (heads[:, None] * tails[None, :] % (first * second)).astype(np.float32)
    angle = np.float32(sign * 2.0 * math.pi / (first * second)) * product
    return np.stack([np.cos(angle), np.sin(angle)]).astype(np.float32)


def host_tables(size, sign):
    index = np.arange(size, dtype=np.int64)
    product = (index[:, None] * index[None, :] % size).astype(np.float32)
    angle = np.float32(sign * 2.0 * math.pi / size) * product
    norm = np.float32(1.0 / math.sqrt(size))
    cos = (np.cos(angle) * norm).astype(ml_dtypes.bfloat16)
    sin = (np.sin(angle) * norm).astype(ml_dtypes.bfloat16)
    table = np.block([[cos, -sin], [sin, cos]])
    return table, np.ascontiguousarray(table.T)


def twist(mid_real, mid_imag, twiddle):
    twist_cos, twist_sin = twiddle[0], twiddle[1]
    turn_real = (mid_real * twist_cos - mid_imag * twist_sin).astype(jnp.bfloat16)
    turn_imag = (mid_real * twist_sin + mid_imag * twist_cos).astype(jnp.bfloat16)
    return turn_real, turn_imag


def forward_transposed(stacked, table, table_t, twiddle):
    half = stacked.shape[0] // 2
    mid = jnp.dot(table, stacked, preferred_element_type=jnp.float32)
    turn_real, turn_imag = twist(mid[:half], mid[half:], twiddle)
    spec = jnp.dot(
        jnp.concatenate([turn_real, turn_imag], axis=1), table_t, preferred_element_type=jnp.float32
    )
    return spec[:, :half], spec[:, half:]


def inverse_from_transposed(real_t, imag_t, table, table_t, twiddle):
    half = real_t.shape[0]
    mid = jnp.dot(
        jnp.concatenate([real_t, imag_t], axis=1), table_t, preferred_element_type=jnp.float32
    )
    turn_real, turn_imag = twist(mid[:, :half], mid[:, half:], twiddle)
    out = jnp.dot(
        table, jnp.concatenate([turn_real, turn_imag], axis=0), preferred_element_type=jnp.float32
    )
    return out[:half], out[half:]


def range_kernel(
    echo_ref, replica_ref, fwd_ref, fwd_t_ref, inv_ref, inv_t_ref, fwd_tw_ref, inv_tw_ref, out_ref, wide_ref
):
    pulses = echo_ref.shape[1] // echo_ref.shape[2]
    side = echo_ref.shape[2]
    fwd, fwd_t = fwd_ref[...], fwd_t_ref[...]
    inv, inv_t = inv_ref[...], inv_t_ref[...]
    fwd_tw, inv_tw = fwd_tw_ref[...], inv_tw_ref[...]
    rep_real, rep_imag = forward_transposed(replica_ref[...], fwd, fwd_t, fwd_tw)
    rep_real = rep_real * 128.0
    rep_imag = rep_imag * 128.0
    for pulse in range(pulses):
        rows = pl.ds(pulse, side, stride=pulses)
        stacked = jnp.concatenate([echo_ref[0, rows, :], echo_ref[1, rows, :]], axis=0)
        spec_real, spec_imag = forward_transposed(stacked, fwd, fwd_t, fwd_tw)
        match_real = (spec_real * rep_real + spec_imag * rep_imag).astype(jnp.bfloat16)
        match_imag = (spec_imag * rep_real - spec_real * rep_imag).astype(jnp.bfloat16)
        comp_real, comp_imag = inverse_from_transposed(match_real, match_imag, inv, inv_t, inv_tw)
        wide_ref[pl.ds(pulse, side, stride=2 * pulses), :] = comp_real
        wide_ref[pl.ds(pulses + pulse, side, stride=2 * pulses), :] = comp_imag
    out_ref[...] = wide_ref[...].astype(jnp.bfloat16)


def range_compress(echo, range_replica):
    pulses, length = echo.shape[1], echo.shape[2]
    side = RSPLIT
    assert length == side * side
    padded = jnp.pad(range_replica, ((0, 0), (0, length - range_replica.shape[1])))
    replica = padded.reshape(2 * side, side)
    rows = echo.reshape(2, pulses, side, side).transpose(0, 2, 1, 3).reshape(2, side * pulses, side)
    fwd, fwd_t = host_tables(side, -1)
    inv, inv_t = host_tables(side, 1)
    fwd_tw = host_twiddle(side, side, -1)
    inv_tw = host_twiddle(side, side, 1)
    whole = pl.BlockSpec(memory_space=pltpu.VMEM)
    out = pl.pallas_call(
        range_kernel,
        in_specs=[whole] * 8,
        out_specs=whole,
        out_shape=jax.ShapeDtypeStruct((side * 2 * pulses, side), jnp.bfloat16),
        scratch_shapes=[pltpu.VMEM((side * 2 * pulses, side), jnp.float32)],
        cost_estimate=pl.CostEstimate(
            flops=(pulses + 1) * 4 * 2 * (2 * side) ** 2 * side,
            bytes_accessed=pulses * 2 * 2 * length * 2,
            transcendentals=0,
        ),
    )(
        rows,
        replica,
        jnp.asarray(fwd),
        jnp.asarray(fwd_t),
        jnp.asarray(inv),
        jnp.asarray(inv_t),
        jnp.asarray(fwd_tw),
        jnp.asarray(inv_tw),
    )
    return out.reshape(side, 2, pulses, side)


def pulse_transform(real_part, imag_part, first, sign):
    length = real_part.shape[0]
    width = real_part.shape[1]
    second = length // first
    head_cos, head_sin = make_table(first, sign)
    tail_cos, tail_sin = make_table(second, sign)
    twist_cos, twist_sin = make_twiddle(first, second, sign)
    twist_cos = twist_cos[:, :, None]
    twist_sin = twist_sin[:, :, None]
    split_real = real_part.reshape(first, second, width)
    split_imag = imag_part.reshape(first, second, width)

    def section_one(table, values):
        return jnp.einsum("kn,nmc->kmc", table, values, preferred_element_type=jnp.float32)

    mid_real = section_one(head_cos, split_real) - section_one(head_sin, split_imag)
    mid_imag = section_one(head_cos, split_imag) + section_one(head_sin, split_real)
    turn_real = (mid_real * twist_cos - mid_imag * twist_sin).astype(jnp.bfloat16)
    turn_imag = (mid_real * twist_sin + mid_imag * twist_cos).astype(jnp.bfloat16)

    def section_two(table, values):
        return jnp.einsum("kmc,jm->jkc", values, table, preferred_element_type=jnp.float32)

    out_real = section_two(tail_cos, turn_real) - section_two(tail_sin, turn_imag)
    out_imag = section_two(tail_cos, turn_imag) + section_two(tail_sin, turn_real)
    return (out_real.reshape(length, width), out_imag.reshape(length, width))


def azimuth_spectra(values):
    first_real, first_imag = pulse_transform(values[0, :, 0], values[1, :, 0], PUL_DEV, -1)
    return jnp.stack([first_real.astype(jnp.bfloat16), first_imag.astype(jnp.bfloat16)])[
        :, :, None, :
    ]


def per_device(raw_echo, range_replica, interp_weight, band_offset, azimuth_rate, tile_owner):
    echo = raw_echo[:, 0]
    length = echo.shape[2]
    compressed = range_compress(echo, range_replica)
    devices = lax.axis_size("wide")
    width = length // devices
    assert compressed.shape[0] == devices and compressed.shape[3] == width
    turned = lax.all_to_all(compressed, "wide", split_axis=0, concat_axis=2, tiled=True)[0]
    doppler = azimuth_spectra(turned[:, :, None, :])[:, :, 0]
    rim = passed_along(doppler[:, :, :HALO], "wide", -1)
    extended = jnp.concatenate([doppler, rim], axis=2)
    pulses = extended.shape[1]
    columns = jnp.arange(width + HALO, dtype=jnp.int32)
    bins = jnp.arange(width, dtype=jnp.int32) + band_offset
    moved_real = jnp.zeros((pulses, width), jnp.float32)
    moved_imag = jnp.zeros((pulses, width), jnp.float32)
    for tap_index in range(interp_weight.shape[0]):
        select = (columns[:, None] == (bins + tap_index)[None, :]).astype(jnp.bfloat16)
        picked = jnp.einsum("xpc,cr->xpr", extended, select, preferred_element_type=jnp.float32)
        weight = interp_weight[tap_index][:, None]
        moved_real = moved_real + weight * picked[0]
        moved_imag = moved_imag + weight * picked[1]
    half = pulses // 2
    freq = jnp.arange(half + 1, dtype=jnp.int32)
    shifted = ((freq + half) % pulses - half).astype(jnp.float32) / pulses
    phase = math.pi * (shifted * shifted)[:, None] / azimuth_rate[None, :]
    half_cos = jnp.cos(phase)
    half_sin = jnp.sin(phase)
    phase_cos = jnp.concatenate([half_cos, jnp.flip(half_cos[1:half], 0)], axis=0)
    phase_sin = jnp.concatenate([half_sin, jnp.flip(half_sin[1:half], 0)], axis=0)
    focus_real = (moved_real * phase_cos - moved_imag * phase_sin).astype(jnp.bfloat16)
    focus_imag = (moved_real * phase_sin + moved_imag * phase_cos).astype(jnp.bfloat16)
    image_real, image_imag = pulse_transform(focus_real, focus_imag, PUL_DEV, 1)
    intensity = (image_real * image_real + image_imag * image_imag).astype(jnp.bfloat16)
    block_count = tile_owner.shape[1]
    block_rows = pulses // block_count
    blocks = intensity.reshape(block_count, block_rows * width)
    tiles = lax.axis_size("narrow")
    group = lax.axis_index("narrow")
    tile_ids = jnp.arange(tiles, dtype=jnp.int32)
    own_row = lax.dynamic_slice_in_dim(tile_owner, group, 1, 0)[0]
    member = (own_row[None, :] == tile_ids[:, None]).astype(jnp.bfloat16)
    counts = jnp.sum(
        (tile_owner[:, :, None] == tile_ids[None, None, :]).astype(jnp.int32), axis=(0, 1)
    )
    own_count = jnp.sum(jnp.where(tile_ids == group, counts, 0)).astype(jnp.float32)
    partial = jnp.dot(member, blocks, preferred_element_type=jnp.float32)
    partial = partial.reshape(tiles, block_rows, width)
    summed = lax.dynamic_index_in_dim(partial, group, 0, keepdims=False)
    for shift in range(1, tiles):
        outgoing = lax.dynamic_index_in_dim(partial, (group + shift) % tiles, 0, keepdims=False)
        summed = summed + lax.ppermute(
            outgoing, "narrow", [(i, (i + shift) % tiles) for i in range(tiles)]
        )
    return summed[None] / own_count


def solution(mesh):
    return jax.shard_map(
        per_device,
        mesh=mesh,
        in_specs=(P(None, "narrow", "wide", None), P(), P(), P("wide"), P("wide"), P()),
        out_specs=P("narrow", None, "wide"),
        check_vma=False,
    )
```

```python
import math

import jax
import jax.numpy as jnp
import ml_dtypes
import numpy as np
from jax import lax
from jax.experimental import pallas as pl
from jax.experimental.pallas import tpu as pltpu
from jax.sharding import PartitionSpec as P

RSPLIT = 128
PUL_DEV = 8
CAP = 8
HALO = 31


def passed_along(shard, axis, by):
    devices = lax.axis_size(axis)
    pairs = [(i, i + by) for i in range(devices) if 0 <= i + by < devices]
    return lax.ppermute(shard, axis, pairs)


def host_twiddle(first, second, sign):
    heads = np.arange(first, dtype=np.int64)
    tails = np.arange(second, dtype=np.int64)
    product = (heads[:, None] * tails[None, :] % (first * second)).astype(np.float32)
    angle = np.float32(sign * 2.0 * math.pi / (first * second)) * product
    return np.stack([np.cos(angle), np.sin(angle)]).astype(np.float32)


def host_tables(size, sign):
    index = np.arange(size, dtype=np.int64)
    product = (index[:, None] * index[None, :] % size).astype(np.float32)
    angle = np.float32(sign * 2.0 * math.pi / size) * product
    norm = np.float32(1.0 / math.sqrt(size))
    cos = (np.cos(angle) * norm).astype(ml_dtypes.bfloat16)
    sin = (np.sin(angle) * norm).astype(ml_dtypes.bfloat16)
    table = np.block([[cos, -sin], [sin, cos]])
    return table, np.ascontiguousarray(table.T)


def twist(mid_real, mid_imag, twiddle):
    twist_cos, twist_sin = twiddle[0], twiddle[1]
    turn_real = (mid_real * twist_cos - mid_imag * twist_sin).astype(jnp.bfloat16)
    turn_imag = (mid_real * twist_sin + mid_imag * twist_cos).astype(jnp.bfloat16)
    return turn_real, turn_imag


def forward_transposed(stacked, table, table_t, twiddle):
    half = stacked.shape[0] // 2
    mid = jnp.dot(table, stacked, preferred_element_type=jnp.float32)
    turn_real, turn_imag = twist(mid[:half], mid[half:], twiddle)
    spec = jnp.dot(
        jnp.concatenate([turn_real, turn_imag], axis=1), table_t, preferred_element_type=jnp.float32
    )
    return spec[:, :half], spec[:, half:]


def inverse_from_transposed(real_t, imag_t, table, table_t, twiddle):
    half = real_t.shape[0]
    mid = jnp.dot(
        jnp.concatenate([real_t, imag_t], axis=1), table_t, preferred_element_type=jnp.float32
    )
    turn_real, turn_imag = twist(mid[:, :half], mid[:, half:], twiddle)
    out = jnp.dot(
        table, jnp.concatenate([turn_real, turn_imag], axis=0), preferred_element_type=jnp.float32
    )
    return out[:half], out[half:]


def range_kernel(
    echo_ref, replica_ref, fwd_ref, fwd_t_ref, inv_ref, inv_t_ref, fwd_tw_ref, inv_tw_ref, out_ref, wide_ref
):
    pulses = echo_ref.shape[1] // echo_ref.shape[2]
    side = echo_ref.shape[2]
    fwd, fwd_t = fwd_ref[...], fwd_t_ref[...]
    inv, inv_t = inv_ref[...], inv_t_ref[...]
    fwd_tw, inv_tw = fwd_tw_ref[...], inv_tw_ref[...]
    rep_real, rep_imag = forward_transposed(replica_ref[...], fwd, fwd_t, fwd_tw)
    rep_real = rep_real * 128.0
    rep_imag = rep_imag * 128.0
    for pulse in range(pulses):
        rows = pl.ds(pulse, side, stride=pulses)
        stacked = jnp.concatenate([echo_ref[0, rows, :], echo_ref[1, rows, :]], axis=0)
        spec_real, spec_imag = forward_transposed(stacked, fwd, fwd_t, fwd_tw)
        match_real = (spec_real * rep_real + spec_imag * rep_imag).astype(jnp.bfloat16)
        match_imag = (spec_imag * rep_real - spec_real * rep_imag).astype(jnp.bfloat16)
        comp_real, comp_imag = inverse_from_transposed(match_real, match_imag, inv, inv_t, inv_tw)
        wide_ref[pl.ds(pulse, side, stride=2 * pulses), :] = comp_real
        wide_ref[pl.ds(pulses + pulse, side, stride=2 * pulses), :] = comp_imag
    out_ref[...] = wide_ref[...].astype(jnp.bfloat16)


def range_compress(echo, range_replica):
    pulses, length = echo.shape[1], echo.shape[2]
    side = RSPLIT
    assert length == side * side
    padded = jnp.pad(range_replica, ((0, 0), (0, length - range_replica.shape[1])))
    replica = padded.reshape(2 * side, side)
    rows = echo.reshape(2, pulses, side, side).transpose(0, 2, 1, 3).reshape(2, side * pulses, side)
    fwd, fwd_t = host_tables(side, -1)
    inv, inv_t = host_tables(side, 1)
    fwd_tw = host_twiddle(side, side, -1)
    inv_tw = host_twiddle(side, side, 1)
    whole = pl.BlockSpec(memory_space=pltpu.VMEM)
    out = pl.pallas_call(
        range_kernel,
        in_specs=[whole] * 8,
        out_specs=whole,
        out_shape=jax.ShapeDtypeStruct((side * 2 * pulses, side), jnp.bfloat16),
        scratch_shapes=[pltpu.VMEM((side * 2 * pulses, side), jnp.float32)],
        cost_estimate=pl.CostEstimate(
            flops=(pulses + 1) * 4 * 2 * (2 * side) ** 2 * side,
            bytes_accessed=pulses * 2 * 2 * length * 2,
            transcendentals=0,
        ),
    )(
        rows,
        replica,
        jnp.asarray(fwd),
        jnp.asarray(fwd_t),
        jnp.asarray(inv),
        jnp.asarray(inv_t),
        jnp.asarray(fwd_tw),
        jnp.asarray(inv_tw),
    )
    return out.reshape(side, 2, pulses, side)


def host_block_table4(size, sign):
    index = np.arange(size, dtype=np.int64)
    product = (index[:, None] * index[None, :] % size).astype(np.float32)
    angle = np.float32(sign * 2.0 * math.pi / size) * product
    norm = np.float32(1.0 / math.sqrt(size))
    cos = (np.cos(angle) * norm).astype(ml_dtypes.bfloat16)
    sin = (np.sin(angle) * norm).astype(ml_dtypes.bfloat16)
    return np.stack([np.stack([cos, -sin], axis=1), np.stack([sin, cos], axis=1)])


def pulse_transform(values, first, sign):
    length, width = values.shape[1], values.shape[2]
    second = length // first
    head = jnp.asarray(host_block_table4(first, sign))
    tail = jnp.asarray(host_block_table4(second, sign))
    twist_cos, twist_sin = (jnp.asarray(t) for t in host_twiddle(first, second, sign))
    split = values.reshape(2, first, second, width)
    mid = jnp.einsum("okrn,rnmc->okmc", head, split, preferred_element_type=jnp.float32)
    mid_real, mid_imag = mid[0], mid[1]
    turn_real = mid_real * twist_cos[:, :, None] - mid_imag * twist_sin[:, :, None]
    turn_imag = mid_real * twist_sin[:, :, None] + mid_imag * twist_cos[:, :, None]
    turned = jnp.stack([turn_real, turn_imag]).astype(jnp.bfloat16)
    out = jnp.einsum("ojrm,rkmc->ojkc", tail, turned, preferred_element_type=jnp.float32)
    return out.reshape(2, length, width)


def per_device(raw_echo, range_replica, interp_weight, band_offset, azimuth_rate, tile_owner):
    echo = raw_echo[:, 0]
    length = echo.shape[2]
    compressed = range_compress(echo, range_replica)
    devices = lax.axis_size("wide")
    width = length // devices
    assert compressed.shape[0] == devices and compressed.shape[3] == width
    turned = lax.all_to_all(compressed, "wide", split_axis=0, concat_axis=2, tiled=True)[0]
    doppler = pulse_transform(turned, PUL_DEV, -1).astype(jnp.bfloat16)
    rim = passed_along(doppler[:, :, :HALO], "wide", -1)
    extended = jnp.concatenate([doppler, rim], axis=2)
    pulses = extended.shape[1]
    columns = jnp.arange(width + HALO, dtype=jnp.int32)
    bins = jnp.arange(width, dtype=jnp.int32) + band_offset
    moved_real = jnp.zeros((pulses, width), jnp.float32)
    moved_imag = jnp.zeros((pulses, width), jnp.float32)
    for tap_index in range(interp_weight.shape[0]):
        select = (columns[:, None] == (bins + tap_index)[None, :]).astype(jnp.bfloat16)
        picked = jnp.einsum("xpc,cr->xpr", extended, select, preferred_element_type=jnp.float32)
        weight = interp_weight[tap_index][:, None]
        moved_real = moved_real + weight * picked[0]
        moved_imag = moved_imag + weight * picked[1]
    half = pulses // 2
    freq = jnp.arange(half + 1, dtype=jnp.int32)
    shifted = ((freq + half) % pulses - half).astype(jnp.float32) / pulses
    phase = math.pi * (shifted * shifted)[:, None] / azimuth_rate[None, :]
    half_cos = jnp.cos(phase)
    half_sin = jnp.sin(phase)
    phase_cos = jnp.concatenate([half_cos, jnp.flip(half_cos[1:half], 0)], axis=0)
    phase_sin = jnp.concatenate([half_sin, jnp.flip(half_sin[1:half], 0)], axis=0)
    focus_real = (moved_real * phase_cos - moved_imag * phase_sin).astype(jnp.bfloat16)
    focus_imag = (moved_real * phase_sin + moved_imag * phase_cos).astype(jnp.bfloat16)
    image = pulse_transform(jnp.stack([focus_real, focus_imag]), PUL_DEV, 1)
    intensity = (image[0] * image[0] + image[1] * image[1]).astype(jnp.bfloat16)
    block_count = tile_owner.shape[1]
    block_rows = pulses // block_count
    blocks = intensity.reshape(block_count, block_rows * width)
    tiles = lax.axis_size("narrow")
    group = lax.axis_index("narrow")
    tile_ids = jnp.arange(tiles, dtype=jnp.int32)
    own_row = lax.dynamic_slice_in_dim(tile_owner, group, 1, 0)[0]
    member = (own_row[None, :] == tile_ids[:, None]).astype(jnp.bfloat16)
    counts = jnp.sum(
        (tile_owner[:, :, None] == tile_ids[None, None, :]).astype(jnp.int32), axis=(0, 1)
    )
    own_count = jnp.sum(jnp.where(tile_ids == group, counts, 0)).astype(jnp.float32)
    partial = jnp.dot(member, blocks, preferred_element_type=jnp.float32)
    partial = partial.reshape(tiles, block_rows, width)
    incoming = lax.all_to_all(partial, "narrow", split_axis=0, concat_axis=0, tiled=True)
    summed = jnp.sum(incoming, axis=0)[None]
    return summed / own_count


def solution(mesh):
    return jax.shard_map(
        per_device,
        mesh=mesh,
        in_specs=(P(None, "narrow", "wide", None), P(), P(), P("wide"), P("wide"), P()),
        out_specs=P("narrow", None, "wide"),
        check_vma=False,
    )
```

```python
import math

import jax
import jax.numpy as jnp
import ml_dtypes
import numpy as np
from jax import lax
from jax.experimental import pallas as pl
from jax.experimental.pallas import tpu as pltpu
from jax.sharding import PartitionSpec as P

RSPLIT = 128
PUL_DEV = 8
CAP = 8
HALO = 31


def passed_along(shard, axis, by):
    devices = lax.axis_size(axis)
    pairs = [(i, i + by) for i in range(devices) if 0 <= i + by < devices]
    return lax.ppermute(shard, axis, pairs)


def host_twiddle(first, second, sign):
    heads = np.arange(first, dtype=np.int64)
    tails = np.arange(second, dtype=np.int64)
    product = (heads[:, None] * tails[None, :] % (first * second)).astype(np.float32)
    angle = np.float32(sign * 2.0 * math.pi / (first * second)) * product
    return np.stack([np.cos(angle), np.sin(angle)]).astype(np.float32)


def host_tables(size, sign):
    index = np.arange(size, dtype=np.int64)
    product = (index[:, None] * index[None, :] % size).astype(np.float32)
    angle = np.float32(sign * 2.0 * math.pi / size) * product
    norm = np.float32(1.0 / math.sqrt(size))
    cos = (np.cos(angle) * norm).astype(ml_dtypes.bfloat16)
    sin = (np.sin(angle) * norm).astype(ml_dtypes.bfloat16)
    table = np.block([[cos, -sin], [sin, cos]])
    return table, np.ascontiguousarray(table.T)


def twist(mid_real, mid_imag, twiddle):
    twist_cos, twist_sin = twiddle[0], twiddle[1]
    turn_real = (mid_real * twist_cos - mid_imag * twist_sin).astype(jnp.bfloat16)
    turn_imag = (mid_real * twist_sin + mid_imag * twist_cos).astype(jnp.bfloat16)
    return turn_real, turn_imag


def forward_transposed(stacked, table, table_t, twiddle):
    half = stacked.shape[0] // 2
    mid = jnp.dot(table, stacked, preferred_element_type=jnp.float32)
    turn_real, turn_imag = twist(mid[:half], mid[half:], twiddle)
    spec = jnp.dot(
        jnp.concatenate([turn_real, turn_imag], axis=1), table_t, preferred_element_type=jnp.float32
    )
    return spec[:, :half], spec[:, half:]


def inverse_from_transposed(real_t, imag_t, table, table_t, twiddle):
    half = real_t.shape[0]
    mid = jnp.dot(
        jnp.concatenate([real_t, imag_t], axis=1), table_t, preferred_element_type=jnp.float32
    )
    turn_real, turn_imag = twist(mid[:, :half], mid[:, half:], twiddle)
    out = jnp.dot(
        table, jnp.concatenate([turn_real, turn_imag], axis=0), preferred_element_type=jnp.float32
    )
    return out[:half], out[half:]


def range_kernel(
    echo_ref, replica_ref, fwd_ref, fwd_t_ref, inv_ref, inv_t_ref, fwd_tw_ref, inv_tw_ref, out_ref, wide_ref
):
    pulses = echo_ref.shape[1] // echo_ref.shape[2]
    side = echo_ref.shape[2]
    fwd, fwd_t = fwd_ref[...], fwd_t_ref[...]
    inv, inv_t = inv_ref[...], inv_t_ref[...]
    fwd_tw, inv_tw = fwd_tw_ref[...], inv_tw_ref[...]
    rep_real, rep_imag = forward_transposed(replica_ref[...], fwd, fwd_t, fwd_tw)
    rep_real = rep_real * 128.0
    rep_imag = rep_imag * 128.0
    for pulse in range(pulses):
        rows = pl.ds(pulse, side, stride=pulses)
        stacked = jnp.concatenate([echo_ref[0, rows, :], echo_ref[1, rows, :]], axis=0)
        spec_real, spec_imag = forward_transposed(stacked, fwd, fwd_t, fwd_tw)
        match_real = (spec_real * rep_real + spec_imag * rep_imag).astype(jnp.bfloat16)
        match_imag = (spec_imag * rep_real - spec_real * rep_imag).astype(jnp.bfloat16)
        comp_real, comp_imag = inverse_from_transposed(match_real, match_imag, inv, inv_t, inv_tw)
        wide_ref[pl.ds(pulse, side, stride=2 * pulses), :] = comp_real
        wide_ref[pl.ds(pulses + pulse, side, stride=2 * pulses), :] = comp_imag
    out_ref[...] = wide_ref[...].astype(jnp.bfloat16)


def range_compress(echo, range_replica):
    pulses, length = echo.shape[1], echo.shape[2]
    side = RSPLIT
    assert length == side * side
    padded = jnp.pad(range_replica, ((0, 0), (0, length - range_replica.shape[1])))
    replica = padded.reshape(2 * side, side)
    rows = echo.reshape(2, pulses, side, side).transpose(0, 2, 1, 3).reshape(2, side * pulses, side)
    fwd, fwd_t = host_tables(side, -1)
    inv, inv_t = host_tables(side, 1)
    fwd_tw = host_twiddle(side, side, -1)
    inv_tw = host_twiddle(side, side, 1)
    whole = pl.BlockSpec(memory_space=pltpu.VMEM)
    out = pl.pallas_call(
        range_kernel,
        in_specs=[whole] * 8,
        out_specs=whole,
        out_shape=jax.ShapeDtypeStruct((side * 2 * pulses, side), jnp.bfloat16),
        scratch_shapes=[pltpu.VMEM((side * 2 * pulses, side), jnp.float32)],
        cost_estimate=pl.CostEstimate(
            flops=(pulses + 1) * 4 * 2 * (2 * side) ** 2 * side,
            bytes_accessed=pulses * 2 * 2 * length * 2,
            transcendentals=0,
        ),
    )(
        rows,
        replica,
        jnp.asarray(fwd),
        jnp.asarray(fwd_t),
        jnp.asarray(inv),
        jnp.asarray(inv_t),
        jnp.asarray(fwd_tw),
        jnp.asarray(inv_tw),
    )
    return out.reshape(side, 2, pulses, side)


def host_block_table4(size, sign):
    index = np.arange(size, dtype=np.int64)
    product = (index[:, None] * index[None, :] % size).astype(np.float32)
    angle = np.float32(sign * 2.0 * math.pi / size) * product
    norm = np.float32(1.0 / math.sqrt(size))
    cos = (np.cos(angle) * norm).astype(ml_dtypes.bfloat16)
    sin = (np.sin(angle) * norm).astype(ml_dtypes.bfloat16)
    return np.stack([np.stack([cos, -sin], axis=1), np.stack([sin, cos], axis=1)])


def pulse_transform(values, first, sign):
    length, width = values.shape[1], values.shape[2]
    second = length // first
    head = jnp.asarray(host_block_table4(first, sign))
    tail = jnp.asarray(host_block_table4(second, sign))
    twist_cos, twist_sin = (jnp.asarray(t) for t in host_twiddle(first, second, sign))
    split = values.reshape(2, first, second, width)
    mid = jnp.einsum("okrn,rnmc->okmc", head, split, preferred_element_type=jnp.float32)
    mid_real, mid_imag = mid[0], mid[1]
    turn_real = mid_real * twist_cos[:, :, None] - mid_imag * twist_sin[:, :, None]
    turn_imag = mid_real * twist_sin[:, :, None] + mid_imag * twist_cos[:, :, None]
    turned = jnp.stack([turn_real, turn_imag]).astype(jnp.bfloat16)
    out = jnp.einsum("ojrm,rkmc->ojkc", tail, turned, preferred_element_type=jnp.float32)
    return out.reshape(2, length, width)


def migrate_kernel(dop_ref, rim_ref, offset_ref, weight_ref, cos_ref, sin_ref, out_ref):
    rows_total, width = dop_ref.shape[1], dop_ref.shape[2]
    taps = weight_ref.shape[1]
    span = 2 * width
    column = lax.broadcasted_iota(jnp.int32, (span, width), 0)
    first = lax.broadcasted_iota(jnp.int32, (span, width), 1) + offset_ref[...]
    block = 256
    for start in range(0, rows_total, block):
        rows = pl.ds(start, block)
        ext = jnp.concatenate(
            [
                jnp.concatenate([dop_ref[0, rows, :], rim_ref[0, rows, :]], axis=1),
                jnp.concatenate([dop_ref[1, rows, :], rim_ref[1, rows, :]], axis=1),
            ],
            axis=0,
        )
        weights = weight_ref[rows, :]
        moved = jnp.zeros((2 * block, width), jnp.float32)
        for tap in range(taps):
            select = (column == first + tap).astype(jnp.bfloat16)
            picked = jnp.dot(ext, select, preferred_element_type=jnp.float32)
            weight = weights[:, tap : tap + 1]
            moved = moved + jnp.concatenate([weight, weight], axis=0) * picked
        moved_real, moved_imag = moved[:block], moved[block:]
        phase_cos, phase_sin = cos_ref[rows, :], sin_ref[rows, :]
        out_ref[0, rows, :] = (moved_real * phase_cos - moved_imag * phase_sin).astype(jnp.bfloat16)
        out_ref[1, rows, :] = (moved_real * phase_sin + moved_imag * phase_cos).astype(jnp.bfloat16)


def migrate_and_focus(doppler, rim, band_offset, interp_weight, phase_cos, phase_sin):
    _, rows, width = doppler.shape
    taps = interp_weight.shape[0]
    rim = jnp.pad(rim, ((0, 0), (0, 0), (0, width - rim.shape[2])))
    whole = pl.BlockSpec(memory_space=pltpu.VMEM)
    return pl.pallas_call(
        migrate_kernel,
        in_specs=[whole] * 6,
        out_specs=whole,
        out_shape=jax.ShapeDtypeStruct((2, rows, width), jnp.bfloat16),
        cost_estimate=pl.CostEstimate(
            flops=taps * 2 * (2 * rows) * (2 * width) * width,
            bytes_accessed=2 * rows * width * (2 + 2 + 2 + 8),
            transcendentals=0,
        ),
    )(
        doppler,
        rim,
        band_offset.reshape(1, width),
        interp_weight.T,
        phase_cos,
        phase_sin,
    )


def per_device(raw_echo, range_replica, interp_weight, band_offset, azimuth_rate, tile_owner):
    echo = raw_echo[:, 0]
    length = echo.shape[2]
    compressed = range_compress(echo, range_replica)
    devices = lax.axis_size("wide")
    width = length // devices
    assert compressed.shape[0] == devices and compressed.shape[3] == width
    turned = lax.all_to_all(compressed, "wide", split_axis=0, concat_axis=2, tiled=True)[0]
    doppler = pulse_transform(turned, PUL_DEV, -1).astype(jnp.bfloat16)
    rim = passed_along(doppler[:, :, :HALO], "wide", -1)
    pulses = doppler.shape[1]
    half = pulses // 2
    freq = jnp.arange(half + 1, dtype=jnp.int32)
    shifted = ((freq + half) % pulses - half).astype(jnp.float32) / pulses
    phase = math.pi * (shifted * shifted)[:, None] / azimuth_rate[None, :]
    half_cos = jnp.cos(phase)
    half_sin = jnp.sin(phase)
    phase_cos = jnp.concatenate([half_cos, jnp.flip(half_cos[1:half], 0)], axis=0)
    phase_sin = jnp.concatenate([half_sin, jnp.flip(half_sin[1:half], 0)], axis=0)
    focused = migrate_and_focus(doppler, rim, band_offset, interp_weight, phase_cos, phase_sin)
    image = pulse_transform(focused, PUL_DEV, 1)
    intensity = (image[0] * image[0] + image[1] * image[1]).astype(jnp.bfloat16)
    block_count = tile_owner.shape[1]
    block_rows = pulses // block_count
    blocks = intensity.reshape(block_count, block_rows * width)
    tiles = lax.axis_size("narrow")
    group = lax.axis_index("narrow")
    tile_ids = jnp.arange(tiles, dtype=jnp.int32)
    own_row = lax.dynamic_slice_in_dim(tile_owner, group, 1, 0)[0]
    member = (own_row[None, :] == tile_ids[:, None]).astype(jnp.bfloat16)
    counts = jnp.sum(
        (tile_owner[:, :, None] == tile_ids[None, None, :]).astype(jnp.int32), axis=(0, 1)
    )
    own_count = jnp.sum(jnp.where(tile_ids == group, counts, 0)).astype(jnp.float32)
    partial = jnp.dot(member, blocks, preferred_element_type=jnp.float32)
    partial = partial.reshape(tiles, block_rows, width)
    incoming = lax.all_to_all(partial, "narrow", split_axis=0, concat_axis=0, tiled=True)
    summed = jnp.sum(incoming, axis=0)[None]
    return summed / own_count


def solution(mesh):
    return jax.shard_map(
        per_device,
        mesh=mesh,
        in_specs=(P(None, "narrow", "wide", None), P(), P(), P("wide"), P("wide"), P()),
        out_specs=P("narrow", None, "wide"),
        check_vma=False,
    )
```

```python
import math

import jax
import jax.numpy as jnp
import ml_dtypes
import numpy as np
from jax import lax
from jax.experimental import pallas as pl
from jax.experimental.pallas import tpu as pltpu
from jax.sharding import PartitionSpec as P

RSPLIT = 128
PUL_DEV = 8
CAP = 8
HALO = 31


def passed_along(shard, axis, by):
    devices = lax.axis_size(axis)
    pairs = [(i, i + by) for i in range(devices) if 0 <= i + by < devices]
    return lax.ppermute(shard, axis, pairs)


def host_twiddle(first, second, sign):
    heads = np.arange(first, dtype=np.int64)
    tails = np.arange(second, dtype=np.int64)
    product = (heads[:, None] * tails[None, :] % (first * second)).astype(np.float32)
    angle = np.float32(sign * 2.0 * math.pi / (first * second)) * product
    return np.stack([np.cos(angle), np.sin(angle)]).astype(np.float32)


def host_tables(size, sign):
    index = np.arange(size, dtype=np.int64)
    product = (index[:, None] * index[None, :] % size).astype(np.float32)
    angle = np.float32(sign * 2.0 * math.pi / size) * product
    norm = np.float32(1.0 / math.sqrt(size))
    cos = (np.cos(angle) * norm).astype(ml_dtypes.bfloat16)
    sin = (np.sin(angle) * norm).astype(ml_dtypes.bfloat16)
    table = np.block([[cos, -sin], [sin, cos]])
    return table, np.ascontiguousarray(table.T)


def twist(mid_real, mid_imag, twiddle):
    twist_cos, twist_sin = twiddle[0], twiddle[1]
    turn_real = (mid_real * twist_cos - mid_imag * twist_sin).astype(jnp.bfloat16)
    turn_imag = (mid_real * twist_sin + mid_imag * twist_cos).astype(jnp.bfloat16)
    return turn_real, turn_imag


def forward_transposed(stacked, table, table_t, twiddle):
    half = stacked.shape[0] // 2
    mid = jnp.dot(table, stacked, preferred_element_type=jnp.float32)
    turn_real, turn_imag = twist(mid[:half], mid[half:], twiddle)
    spec = jnp.dot(
        jnp.concatenate([turn_real, turn_imag], axis=1), table_t, preferred_element_type=jnp.float32
    )
    return spec[:, :half], spec[:, half:]


def inverse_from_transposed(real_t, imag_t, table, table_t, twiddle):
    half = real_t.shape[0]
    mid = jnp.dot(
        jnp.concatenate([real_t, imag_t], axis=1), table_t, preferred_element_type=jnp.float32
    )
    turn_real, turn_imag = twist(mid[:, :half], mid[:, half:], twiddle)
    out = jnp.dot(
        table, jnp.concatenate([turn_real, turn_imag], axis=0), preferred_element_type=jnp.float32
    )
    return out[:half], out[half:]


def range_kernel(
    echo_ref, replica_ref, fwd_ref, fwd_t_ref, inv_ref, inv_t_ref, fwd_tw_ref, inv_tw_ref, out_ref, wide_ref
):
    pulses = echo_ref.shape[1] // echo_ref.shape[2]
    side = echo_ref.shape[2]
    fwd, fwd_t = fwd_ref[...], fwd_t_ref[...]
    inv, inv_t = inv_ref[...], inv_t_ref[...]
    fwd_tw, inv_tw = fwd_tw_ref[...], inv_tw_ref[...]
    taps = replica_ref[...].astype(jnp.float32)
    filled = taps.shape[1] // side
    blank = jnp.zeros((side - filled, side), jnp.float32)
    pieces = []
    for part in range(2):
        pieces += [taps[part : part + 1, n * side : (n + 1) * side] for n in range(filled)]
        pieces.append(blank)
    replica = jnp.concatenate(pieces, axis=0).astype(jnp.bfloat16)
    rep_real, rep_imag = forward_transposed(replica, fwd, fwd_t, fwd_tw)
    rep_real = rep_real * 128.0
    rep_imag = rep_imag * 128.0
    for pulse in range(pulses):
        rows = pl.ds(pulse, side, stride=pulses)
        stacked = jnp.concatenate([echo_ref[0, rows, :], echo_ref[1, rows, :]], axis=0)
        spec_real, spec_imag = forward_transposed(stacked, fwd, fwd_t, fwd_tw)
        match_real = (spec_real * rep_real + spec_imag * rep_imag).astype(jnp.bfloat16)
        match_imag = (spec_imag * rep_real - spec_real * rep_imag).astype(jnp.bfloat16)
        comp_real, comp_imag = inverse_from_transposed(match_real, match_imag, inv, inv_t, inv_tw)
        wide_ref[pl.ds(pulse, side, stride=2 * pulses), :] = comp_real
        wide_ref[pl.ds(pulses + pulse, side, stride=2 * pulses), :] = comp_imag
    out_ref[...] = wide_ref[...].astype(jnp.bfloat16)


def range_compress(echo, range_replica):
    pulses, length = echo.shape[1], echo.shape[2]
    side = RSPLIT
    assert length == side * side
    assert range_replica.shape[1] % side == 0 and range_replica.shape[1] <= length
    rows = echo.reshape(2, pulses, side, side).transpose(0, 2, 1, 3).reshape(2, side * pulses, side)
    fwd, fwd_t = host_tables(side, -1)
    inv, inv_t = host_tables(side, 1)
    fwd_tw = host_twiddle(side, side, -1)
    inv_tw = host_twiddle(side, side, 1)
    whole = pl.BlockSpec(memory_space=pltpu.VMEM)
    out = pl.pallas_call(
        range_kernel,
        in_specs=[whole] * 8,
        out_specs=whole,
        out_shape=jax.ShapeDtypeStruct((side * 2 * pulses, side), jnp.bfloat16),
        scratch_shapes=[pltpu.VMEM((side * 2 * pulses, side), jnp.float32)],
        cost_estimate=pl.CostEstimate(
            flops=(pulses + 1) * 4 * 2 * (2 * side) ** 2 * side,
            bytes_accessed=pulses * 2 * 2 * length * 2,
            transcendentals=0,
        ),
    )(
        rows,
        range_replica,
        jnp.asarray(fwd),
        jnp.asarray(fwd_t),
        jnp.asarray(inv),
        jnp.asarray(inv_t),
        jnp.asarray(fwd_tw),
        jnp.asarray(inv_tw),
    )
    return out.reshape(side, 2, pulses, side)


def host_block_table4(size, sign):
    index = np.arange(size, dtype=np.int64)
    product = (index[:, None] * index[None, :] % size).astype(np.float32)
    angle = np.float32(sign * 2.0 * math.pi / size) * product
    norm = np.float32(1.0 / math.sqrt(size))
    cos = (np.cos(angle) * norm).astype(ml_dtypes.bfloat16)
    sin = (np.sin(angle) * norm).astype(ml_dtypes.bfloat16)
    return np.stack([np.stack([cos, -sin], axis=1), np.stack([sin, cos], axis=1)])


def pulse_transform(values, first, sign):
    length, width = values.shape[1], values.shape[2]
    second = length // first
    head = jnp.asarray(host_block_table4(first, sign))
    tail = jnp.asarray(host_block_table4(second, sign))
    twist_cos, twist_sin = (jnp.asarray(t) for t in host_twiddle(first, second, sign))
    split = values.reshape(2, first, second, width)
    mid = jnp.einsum("okrn,rnmc->okmc", head, split, preferred_element_type=jnp.float32)
    mid_real, mid_imag = mid[0], mid[1]
    turn_real = mid_real * twist_cos[:, :, None] - mid_imag * twist_sin[:, :, None]
    turn_imag = mid_real * twist_sin[:, :, None] + mid_imag * twist_cos[:, :, None]
    turned = jnp.stack([turn_real, turn_imag]).astype(jnp.bfloat16)
    out = jnp.einsum("ojrm,rkmc->ojkc", tail, turned, preferred_element_type=jnp.float32)
    return out.reshape(2, length, width)


def per_device(raw_echo, range_replica, interp_weight, band_offset, azimuth_rate, tile_owner):
    echo = raw_echo[:, 0]
    length = echo.shape[2]
    compressed = range_compress(echo, range_replica)
    devices = lax.axis_size("wide")
    width = length // devices
    assert compressed.shape[0] == devices and compressed.shape[3] == width
    turned = lax.all_to_all(compressed, "wide", split_axis=0, concat_axis=2, tiled=True)[0]
    doppler = pulse_transform(turned, PUL_DEV, -1).astype(jnp.bfloat16)
    rim = passed_along(doppler[:, :, :HALO], "wide", -1)
    extended = jnp.concatenate([doppler, rim], axis=2)
    pulses = extended.shape[1]
    columns = jnp.arange(width + HALO, dtype=jnp.int32)
    bins = jnp.arange(width, dtype=jnp.int32) + band_offset
    moved_real = jnp.zeros((pulses, width), jnp.float32)
    moved_imag = jnp.zeros((pulses, width), jnp.float32)
    for tap_index in range(interp_weight.shape[0]):
        select = (columns[:, None] == (bins + tap_index)[None, :]).astype(jnp.bfloat16)
        picked = jnp.einsum("xpc,cr->xpr", extended, select, preferred_element_type=jnp.float32)
        weight = interp_weight[tap_index][:, None]
        moved_real = moved_real + weight * picked[0]
        moved_imag = moved_imag + weight * picked[1]
    half = pulses // 2
    freq = jnp.arange(half + 1, dtype=jnp.int32)
    shifted = ((freq + half) % pulses - half).astype(jnp.float32) / pulses
    phase = math.pi * (shifted * shifted)[:, None] / azimuth_rate[None, :]
    half_cos = jnp.cos(phase)
    half_sin = jnp.sin(phase)
    phase_cos = jnp.concatenate([half_cos, jnp.flip(half_cos[1:half], 0)], axis=0)
    phase_sin = jnp.concatenate([half_sin, jnp.flip(half_sin[1:half], 0)], axis=0)
    focus_real = (moved_real * phase_cos - moved_imag * phase_sin).astype(jnp.bfloat16)
    focus_imag = (moved_real * phase_sin + moved_imag * phase_cos).astype(jnp.bfloat16)
    image = pulse_transform(jnp.stack([focus_real, focus_imag]), PUL_DEV, 1)
    intensity = (image[0] * image[0] + image[1] * image[1]).astype(jnp.bfloat16)
    block_count = tile_owner.shape[1]
    block_rows = pulses // block_count
    blocks = intensity.reshape(block_count, block_rows * width)
    tiles = lax.axis_size("narrow")
    group = lax.axis_index("narrow")
    tile_ids = jnp.arange(tiles, dtype=jnp.int32)
    own_row = lax.dynamic_slice_in_dim(tile_owner, group, 1, 0)[0]
    member = (own_row[None, :] == tile_ids[:, None]).astype(jnp.bfloat16)
    counts = jnp.sum(
        (tile_owner[:, :, None] == tile_ids[None, None, :]).astype(jnp.int32), axis=(0, 1)
    )
    own_count = jnp.sum(jnp.where(tile_ids == group, counts, 0)).astype(jnp.float32)
    partial = jnp.dot(member, blocks, preferred_element_type=jnp.float32)
    partial = partial.reshape(tiles, block_rows, width)
    incoming = lax.all_to_all(partial, "narrow", split_axis=0, concat_axis=0, tiled=True)
    summed = jnp.sum(incoming, axis=0)[None]
    return summed / own_count


def solution(mesh):
    return jax.shard_map(
        per_device,
        mesh=mesh,
        in_specs=(P(None, "narrow", "wide", None), P(), P(), P("wide"), P("wide"), P()),
        out_specs=P("narrow", None, "wide"),
        check_vma=False,
    )
```

```python
import math

import jax
import jax.numpy as jnp
import ml_dtypes
import numpy as np
from jax import lax
from jax.experimental import pallas as pl
from jax.experimental.pallas import tpu as pltpu
from jax.sharding import PartitionSpec as P

RSPLIT = 128
PUL_DEV = 8
CAP = 8
HALO = 31


def passed_along(shard, axis, by):
    devices = lax.axis_size(axis)
    pairs = [(i, i + by) for i in range(devices) if 0 <= i + by < devices]
    return lax.ppermute(shard, axis, pairs)


def host_twiddle(first, second, sign):
    heads = np.arange(first, dtype=np.int64)
    tails = np.arange(second, dtype=np.int64)
    product = (heads[:, None] * tails[None, :] % (first * second)).astype(np.float32)
    angle = np.float32(sign * 2.0 * math.pi / (first * second)) * product
    return np.stack([np.cos(angle), np.sin(angle)]).astype(np.float32)


def host_tables(size, sign):
    index = np.arange(size, dtype=np.int64)
    product = (index[:, None] * index[None, :] % size).astype(np.float32)
    angle = np.float32(sign * 2.0 * math.pi / size) * product
    norm = np.float32(1.0 / math.sqrt(size))
    cos = (np.cos(angle) * norm).astype(ml_dtypes.bfloat16)
    sin = (np.sin(angle) * norm).astype(ml_dtypes.bfloat16)
    table = np.block([[cos, -sin], [sin, cos]])
    return table, np.ascontiguousarray(table.T)


def twist(mid_real, mid_imag, twiddle):
    twist_cos, twist_sin = twiddle[0], twiddle[1]
    turn_real = (mid_real * twist_cos - mid_imag * twist_sin).astype(jnp.bfloat16)
    turn_imag = (mid_real * twist_sin + mid_imag * twist_cos).astype(jnp.bfloat16)
    return turn_real, turn_imag


def forward_transposed(stacked, table, table_t, twiddle):
    half = stacked.shape[0] // 2
    mid = jnp.dot(table, stacked, preferred_element_type=jnp.float32)
    turn_real, turn_imag = twist(mid[:half], mid[half:], twiddle)
    spec = jnp.dot(
        jnp.concatenate([turn_real, turn_imag], axis=1), table_t, preferred_element_type=jnp.float32
    )
    return spec[:, :half], spec[:, half:]


def inverse_from_transposed(real_t, imag_t, table, table_t, twiddle):
    half = real_t.shape[0]
    mid = jnp.dot(
        jnp.concatenate([real_t, imag_t], axis=1), table_t, preferred_element_type=jnp.float32
    )
    turn_real, turn_imag = twist(mid[:, :half], mid[:, half:], twiddle)
    out = jnp.dot(
        table, jnp.concatenate([turn_real, turn_imag], axis=0), preferred_element_type=jnp.float32
    )
    return out[:half], out[half:]


def range_kernel(
    echo_ref, replica_ref, fwd_ref, fwd_t_ref, inv_ref, inv_t_ref, fwd_tw_ref, inv_tw_ref, out_ref, wide_ref
):
    pulses = echo_ref.shape[1] // echo_ref.shape[2]
    side = echo_ref.shape[2]
    fwd, fwd_t = fwd_ref[...], fwd_t_ref[...]
    inv, inv_t = inv_ref[...], inv_t_ref[...]
    fwd_tw, inv_tw = fwd_tw_ref[...], inv_tw_ref[...]
    taps = replica_ref[...].astype(jnp.float32)
    filled = taps.shape[1] // side
    blank = jnp.zeros((side - filled, side), jnp.float32)
    pieces = []
    for part in range(2):
        pieces += [taps[part : part + 1, n * side : (n + 1) * side] for n in range(filled)]
        pieces.append(blank)
    replica = jnp.concatenate(pieces, axis=0).astype(jnp.bfloat16)
    rep_real, rep_imag = forward_transposed(replica, fwd, fwd_t, fwd_tw)
    rep_real = rep_real * 128.0
    rep_imag = rep_imag * 128.0
    blocks = []
    for pulse in range(pulses):
        rows = pl.ds(pulse, side, stride=pulses)
        blocks.append(jnp.concatenate([echo_ref[0, rows, :], echo_ref[1, rows, :]], axis=0))
    mid = jnp.dot(fwd, jnp.concatenate(blocks, axis=1), preferred_element_type=jnp.float32)
    along = lambda x: jnp.concatenate([x] * pulses, axis=1)
    down = lambda x: jnp.concatenate([x] * pulses, axis=0)
    turn_real, turn_imag = twist(mid[:side], mid[side:], (along(fwd_tw[0]), along(fwd_tw[1])))
    by_pulse = lambda x, p: x[:, p * side : (p + 1) * side]
    stacked = jnp.concatenate(
        [
            jnp.concatenate([by_pulse(turn_real, p), by_pulse(turn_imag, p)], axis=1)
            for p in range(pulses)
        ],
        axis=0,
    )
    spec = jnp.dot(stacked, fwd_t, preferred_element_type=jnp.float32)
    spec_real, spec_imag = spec[:, :side], spec[:, side:]
    rep_real, rep_imag = down(rep_real), down(rep_imag)
    match_real = (spec_real * rep_real + spec_imag * rep_imag).astype(jnp.bfloat16)
    match_imag = (spec_imag * rep_real - spec_real * rep_imag).astype(jnp.bfloat16)
    mid = jnp.dot(
        jnp.concatenate([match_real, match_imag], axis=1), inv_t, preferred_element_type=jnp.float32
    )
    turn_real, turn_imag = twist(mid[:, :side], mid[:, side:], (down(inv_tw[0]), down(inv_tw[1])))
    rows_of = lambda x, p: x[p * side : (p + 1) * side]
    stacked = jnp.concatenate(
        [
            jnp.concatenate([rows_of(turn_real, p), rows_of(turn_imag, p)], axis=0)
            for p in range(pulses)
        ],
        axis=1,
    )
    comp = jnp.dot(inv, stacked, preferred_element_type=jnp.float32)
    for pulse in range(pulses):
        wide_ref[pl.ds(pulse, side, stride=2 * pulses), :] = by_pulse(comp[:side], pulse)
        wide_ref[pl.ds(pulses + pulse, side, stride=2 * pulses), :] = by_pulse(comp[side:], pulse)
    out_ref[...] = wide_ref[...].astype(jnp.bfloat16)


def range_compress(echo, range_replica):
    pulses, length = echo.shape[1], echo.shape[2]
    side = RSPLIT
    assert length == side * side
    assert range_replica.shape[1] % side == 0 and range_replica.shape[1] <= length
    rows = echo.reshape(2, pulses, side, side).transpose(0, 2, 1, 3).reshape(2, side * pulses, side)
    fwd, fwd_t = host_tables(side, -1)
    inv, inv_t = host_tables(side, 1)
    fwd_tw = host_twiddle(side, side, -1)
    inv_tw = host_twiddle(side, side, 1)
    whole = pl.BlockSpec(memory_space=pltpu.VMEM)
    out = pl.pallas_call(
        range_kernel,
        in_specs=[whole] * 8,
        out_specs=whole,
        out_shape=jax.ShapeDtypeStruct((side * 2 * pulses, side), jnp.bfloat16),
        scratch_shapes=[pltpu.VMEM((side * 2 * pulses, side), jnp.float32)],
        cost_estimate=pl.CostEstimate(
            flops=(pulses + 1) * 4 * 2 * (2 * side) ** 2 * side,
            bytes_accessed=pulses * 2 * 2 * length * 2,
            transcendentals=0,
        ),
    )(
        rows,
        range_replica,
        jnp.asarray(fwd),
        jnp.asarray(fwd_t),
        jnp.asarray(inv),
        jnp.asarray(inv_t),
        jnp.asarray(fwd_tw),
        jnp.asarray(inv_tw),
    )
    return out.reshape(side, 2, pulses, side)


def host_block_table4(size, sign):
    index = np.arange(size, dtype=np.int64)
    product = (index[:, None] * index[None, :] % size).astype(np.float32)
    angle = np.float32(sign * 2.0 * math.pi / size) * product
    norm = np.float32(1.0 / math.sqrt(size))
    cos = (np.cos(angle) * norm).astype(ml_dtypes.bfloat16)
    sin = (np.sin(angle) * norm).astype(ml_dtypes.bfloat16)
    return np.stack([np.stack([cos, -sin], axis=1), np.stack([sin, cos], axis=1)])


def pulse_transform(values, first, sign):
    length, width = values.shape[1], values.shape[2]
    second = length // first
    head = jnp.asarray(host_block_table4(first, sign))
    tail = jnp.asarray(host_block_table4(second, sign))
    twist_cos, twist_sin = (jnp.asarray(t) for t in host_twiddle(first, second, sign))
    split = values.reshape(2, first, second, width)
    mid = jnp.einsum("okrn,rnmc->okmc", head, split, preferred_element_type=jnp.float32)
    mid_real, mid_imag = mid[0], mid[1]
    turn_real = mid_real * twist_cos[:, :, None] - mid_imag * twist_sin[:, :, None]
    turn_imag = mid_real * twist_sin[:, :, None] + mid_imag * twist_cos[:, :, None]
    turned = jnp.stack([turn_real, turn_imag]).astype(jnp.bfloat16)
    out = jnp.einsum("ojrm,rkmc->ojkc", tail, turned, preferred_element_type=jnp.float32)
    return out.reshape(2, length, width)


def per_device(raw_echo, range_replica, interp_weight, band_offset, azimuth_rate, tile_owner):
    echo = raw_echo[:, 0]
    length = echo.shape[2]
    compressed = range_compress(echo, range_replica)
    devices = lax.axis_size("wide")
    width = length // devices
    assert compressed.shape[0] == devices and compressed.shape[3] == width
    turned = lax.all_to_all(compressed, "wide", split_axis=0, concat_axis=2, tiled=True)[0]
    doppler = pulse_transform(turned, PUL_DEV, -1).astype(jnp.bfloat16)
    rim = passed_along(doppler[:, :, :HALO], "wide", -1)
    extended = jnp.concatenate([doppler, rim], axis=2)
    pulses = extended.shape[1]
    columns = jnp.arange(width + HALO, dtype=jnp.int32)
    bins = jnp.arange(width, dtype=jnp.int32) + band_offset
    moved_real = jnp.zeros((pulses, width), jnp.float32)
    moved_imag = jnp.zeros((pulses, width), jnp.float32)
    for tap_index in range(interp_weight.shape[0]):
        select = (columns[:, None] == (bins + tap_index)[None, :]).astype(jnp.bfloat16)
        picked = jnp.einsum("xpc,cr->xpr", extended, select, preferred_element_type=jnp.float32)
        weight = interp_weight[tap_index][:, None]
        moved_real = moved_real + weight * picked[0]
        moved_imag = moved_imag + weight * picked[1]
    half = pulses // 2
    freq = jnp.arange(half + 1, dtype=jnp.int32)
    shifted = ((freq + half) % pulses - half).astype(jnp.float32) / pulses
    phase = math.pi * (shifted * shifted)[:, None] / azimuth_rate[None, :]
    half_cos = jnp.cos(phase)
    half_sin = jnp.sin(phase)
    phase_cos = jnp.concatenate([half_cos, jnp.flip(half_cos[1:half], 0)], axis=0)
    phase_sin = jnp.concatenate([half_sin, jnp.flip(half_sin[1:half], 0)], axis=0)
    focus_real = (moved_real * phase_cos - moved_imag * phase_sin).astype(jnp.bfloat16)
    focus_imag = (moved_real * phase_sin + moved_imag * phase_cos).astype(jnp.bfloat16)
    image = pulse_transform(jnp.stack([focus_real, focus_imag]), PUL_DEV, 1)
    intensity = (image[0] * image[0] + image[1] * image[1]).astype(jnp.bfloat16)
    block_count = tile_owner.shape[1]
    block_rows = pulses // block_count
    blocks = intensity.reshape(block_count, block_rows * width)
    tiles = lax.axis_size("narrow")
    group = lax.axis_index("narrow")
    tile_ids = jnp.arange(tiles, dtype=jnp.int32)
    own_row = lax.dynamic_slice_in_dim(tile_owner, group, 1, 0)[0]
    member = (own_row[None, :] == tile_ids[:, None]).astype(jnp.bfloat16)
    counts = jnp.sum(
        (tile_owner[:, :, None] == tile_ids[None, None, :]).astype(jnp.int32), axis=(0, 1)
    )
    own_count = jnp.sum(jnp.where(tile_ids == group, counts, 0)).astype(jnp.float32)
    partial = jnp.dot(member, blocks, preferred_element_type=jnp.float32)
    partial = partial.reshape(tiles, block_rows, width)
    incoming = lax.all_to_all(partial, "narrow", split_axis=0, concat_axis=0, tiled=True)
    summed = jnp.sum(incoming, axis=0)[None]
    return summed / own_count


def solution(mesh):
    return jax.shard_map(
        per_device,
        mesh=mesh,
        in_specs=(P(None, "narrow", "wide", None), P(), P(), P("wide"), P("wide"), P()),
        out_specs=P("narrow", None, "wide"),
        check_vma=False,
    )
```

```python
import math

import jax
import jax.numpy as jnp
import ml_dtypes
import numpy as np
from jax import lax
from jax.experimental import pallas as pl
from jax.experimental.pallas import tpu as pltpu
from jax.sharding import PartitionSpec as P

RSPLIT = 128
PUL_DEV = 8
CAP = 8
HALO = 31


def passed_along(shard, axis, by):
    devices = lax.axis_size(axis)
    pairs = [(i, i + by) for i in range(devices) if 0 <= i + by < devices]
    return lax.ppermute(shard, axis, pairs)


def host_twiddle(first, second, sign):
    heads = np.arange(first, dtype=np.int64)
    tails = np.arange(second, dtype=np.int64)
    product = (heads[:, None] * tails[None, :] % (first * second)).astype(np.float32)
    angle = np.float32(sign * 2.0 * math.pi / (first * second)) * product
    return np.stack([np.cos(angle), np.sin(angle)]).astype(np.float32)


def host_tables(size, sign):
    index = np.arange(size, dtype=np.int64)
    product = (index[:, None] * index[None, :] % size).astype(np.float32)
    angle = np.float32(sign * 2.0 * math.pi / size) * product
    norm = np.float32(1.0 / math.sqrt(size))
    cos = (np.cos(angle) * norm).astype(ml_dtypes.bfloat16)
    sin = (np.sin(angle) * norm).astype(ml_dtypes.bfloat16)
    table = np.block([[cos, -sin], [sin, cos]])
    return table, np.ascontiguousarray(table.T)


def twist(mid_real, mid_imag, twiddle):
    twist_cos, twist_sin = twiddle[0], twiddle[1]
    turn_real = (mid_real * twist_cos - mid_imag * twist_sin).astype(jnp.bfloat16)
    turn_imag = (mid_real * twist_sin + mid_imag * twist_cos).astype(jnp.bfloat16)
    return turn_real, turn_imag


def forward_transposed(stacked, table, table_t, twiddle):
    half = stacked.shape[0] // 2
    mid = jnp.dot(table, stacked, preferred_element_type=jnp.float32)
    turn_real, turn_imag = twist(mid[:half], mid[half:], twiddle)
    spec = jnp.dot(
        jnp.concatenate([turn_real, turn_imag], axis=1), table_t, preferred_element_type=jnp.float32
    )
    return spec[:, :half], spec[:, half:]


def inverse_from_transposed(real_t, imag_t, table, table_t, twiddle):
    half = real_t.shape[0]
    mid = jnp.dot(
        jnp.concatenate([real_t, imag_t], axis=1), table_t, preferred_element_type=jnp.float32
    )
    turn_real, turn_imag = twist(mid[:, :half], mid[:, half:], twiddle)
    out = jnp.dot(
        table, jnp.concatenate([turn_real, turn_imag], axis=0), preferred_element_type=jnp.float32
    )
    return out[:half], out[half:]


def range_kernel(
    echo_ref, replica_ref, fwd_ref, fwd_t_ref, inv_ref, inv_t_ref, fwd_tw_ref, inv_tw_ref, out_ref, wide_ref
):
    pulses = echo_ref.shape[1] // echo_ref.shape[2]
    side = echo_ref.shape[2]
    fwd, fwd_t = fwd_ref[...], fwd_t_ref[...]
    inv, inv_t = inv_ref[...], inv_t_ref[...]
    fwd_tw, inv_tw = fwd_tw_ref[...], inv_tw_ref[...]
    taps = replica_ref[...].astype(jnp.float32)
    filled = taps.shape[1] // side
    blank = jnp.zeros((side - filled, side), jnp.float32)
    pieces = []
    for part in range(2):
        pieces += [taps[part : part + 1, n * side : (n + 1) * side] for n in range(filled)]
        pieces.append(blank)
    replica = jnp.concatenate(pieces, axis=0).astype(jnp.bfloat16)
    rep_real, rep_imag = forward_transposed(replica, fwd, fwd_t, fwd_tw)
    rep_real = rep_real * 128.0
    rep_imag = rep_imag * 128.0
    blocks = []
    for pulse in range(pulses):
        rows = pl.ds(pulse, side, stride=pulses)
        blocks.append(jnp.concatenate([echo_ref[0, rows, :], echo_ref[1, rows, :]], axis=0))
    mid = jnp.dot(fwd, jnp.concatenate(blocks, axis=1), preferred_element_type=jnp.float32)
    along = lambda x: jnp.concatenate([x] * pulses, axis=1)
    down = lambda x: jnp.concatenate([x] * pulses, axis=0)
    turn_real, turn_imag = twist(mid[:side], mid[side:], (along(fwd_tw[0]), along(fwd_tw[1])))
    by_pulse = lambda x, p: x[:, p * side : (p + 1) * side]
    stacked = jnp.concatenate(
        [
            jnp.concatenate([by_pulse(turn_real, p), by_pulse(turn_imag, p)], axis=1)
            for p in range(pulses)
        ],
        axis=0,
    )
    spec = jnp.dot(stacked, fwd_t, preferred_element_type=jnp.float32)
    spec_real, spec_imag = spec[:, :side], spec[:, side:]
    rep_real, rep_imag = down(rep_real), down(rep_imag)
    match_real = (spec_real * rep_real + spec_imag * rep_imag).astype(jnp.bfloat16)
    match_imag = (spec_imag * rep_real - spec_real * rep_imag).astype(jnp.bfloat16)
    mid = jnp.dot(
        jnp.concatenate([match_real, match_imag], axis=1), inv_t, preferred_element_type=jnp.float32
    )
    turn_real, turn_imag = twist(mid[:, :side], mid[:, side:], (down(inv_tw[0]), down(inv_tw[1])))
    rows_of = lambda x, p: x[p * side : (p + 1) * side]
    stacked = jnp.concatenate(
        [
            jnp.concatenate([rows_of(turn_real, p), rows_of(turn_imag, p)], axis=0)
            for p in range(pulses)
        ],
        axis=1,
    )
    comp = jnp.dot(inv, stacked, preferred_element_type=jnp.float32)
    for pulse in range(pulses):
        wide_ref[pl.ds(pulse, side, stride=2 * pulses), :] = by_pulse(comp[:side], pulse)
        wide_ref[pl.ds(pulses + pulse, side, stride=2 * pulses), :] = by_pulse(comp[side:], pulse)
    out_ref[...] = wide_ref[...].astype(jnp.bfloat16)


def range_compress(echo, range_replica):
    pulses, length = echo.shape[1], echo.shape[2]
    side = RSPLIT
    assert length == side * side
    assert range_replica.shape[1] % side == 0 and range_replica.shape[1] <= length
    rows = echo.reshape(2, pulses, side, side).transpose(0, 2, 1, 3).reshape(2, side * pulses, side)
    fwd, fwd_t = host_tables(side, -1)
    inv, inv_t = host_tables(side, 1)
    fwd_tw = host_twiddle(side, side, -1)
    inv_tw = host_twiddle(side, side, 1)
    whole = pl.BlockSpec(memory_space=pltpu.VMEM)
    out = pl.pallas_call(
        range_kernel,
        in_specs=[whole] * 8,
        out_specs=whole,
        out_shape=jax.ShapeDtypeStruct((side * 2 * pulses, side), jnp.bfloat16),
        scratch_shapes=[pltpu.VMEM((side * 2 * pulses, side), jnp.float32)],
        cost_estimate=pl.CostEstimate(
            flops=(pulses + 1) * 4 * 2 * (2 * side) ** 2 * side,
            bytes_accessed=pulses * 2 * 2 * length * 2,
            transcendentals=0,
        ),
    )(
        rows,
        range_replica,
        jnp.asarray(fwd),
        jnp.asarray(fwd_t),
        jnp.asarray(inv),
        jnp.asarray(inv_t),
        jnp.asarray(fwd_tw),
        jnp.asarray(inv_tw),
    )
    return out.reshape(side, 2, pulses, side)


def host_block_table4(size, sign):
    index = np.arange(size, dtype=np.int64)
    product = (index[:, None] * index[None, :] % size).astype(np.float32)
    angle = np.float32(sign * 2.0 * math.pi / size) * product
    norm = np.float32(1.0 / math.sqrt(size))
    cos = (np.cos(angle) * norm).astype(ml_dtypes.bfloat16)
    sin = (np.sin(angle) * norm).astype(ml_dtypes.bfloat16)
    return np.stack([np.stack([cos, -sin], axis=1), np.stack([sin, cos], axis=1)])


def pulse_transform(values, first, sign):
    length, width = values.shape[1], values.shape[2]
    second = length // first
    head = jnp.asarray(host_block_table4(first, sign))
    tail = jnp.asarray(host_block_table4(second, sign))
    twist_cos, twist_sin = (jnp.asarray(t) for t in host_twiddle(first, second, sign))
    split = values.reshape(2, first, second, width)
    mid = jnp.einsum("okrn,rnmc->okmc", head, split, preferred_element_type=jnp.float32)
    mid_real, mid_imag = mid[0], mid[1]
    turn_real = mid_real * twist_cos[:, :, None] - mid_imag * twist_sin[:, :, None]
    turn_imag = mid_real * twist_sin[:, :, None] + mid_imag * twist_cos[:, :, None]
    turned = jnp.stack([turn_real, turn_imag]).astype(jnp.bfloat16)
    out = jnp.einsum("ojrm,rkmc->ojkc", tail, turned, preferred_element_type=jnp.float32)
    return out.reshape(2, length, width)


def per_device(raw_echo, range_replica, interp_weight, band_offset, azimuth_rate, tile_owner):
    echo = raw_echo[:, 0]
    length = echo.shape[2]
    compressed = range_compress(echo, range_replica)
    devices = lax.axis_size("wide")
    width = length // devices
    assert compressed.shape[0] == devices and compressed.shape[3] == width
    turned = lax.all_to_all(compressed, "wide", split_axis=0, concat_axis=2, tiled=True)[0]
    doppler = pulse_transform(turned, PUL_DEV, -1).astype(jnp.bfloat16)
    rim = passed_along(doppler[:, :, :HALO], "wide", -1)
    extended = jnp.concatenate([doppler, rim], axis=2)
    pulses = extended.shape[1]
    columns = jnp.arange(width + HALO, dtype=jnp.int32)
    bins = jnp.arange(width, dtype=jnp.int32) + band_offset
    moved_real = jnp.zeros((pulses, width), jnp.float32)
    moved_imag = jnp.zeros((pulses, width), jnp.float32)
    for tap_index in range(interp_weight.shape[0]):
        select = (columns[:, None] == (bins + tap_index)[None, :]).astype(jnp.bfloat16)
        picked = jnp.einsum("xpc,cr->xpr", extended, select, preferred_element_type=jnp.bfloat16)
        weight = interp_weight[tap_index][:, None]
        moved_real = moved_real + weight * picked[0].astype(jnp.float32)
        moved_imag = moved_imag + weight * picked[1].astype(jnp.float32)
    half = pulses // 2
    freq = jnp.arange(half + 1, dtype=jnp.int32)
    shifted = ((freq + half) % pulses - half).astype(jnp.float32) / pulses
    phase = math.pi * (shifted * shifted)[:, None] / azimuth_rate[None, :]
    half_cos = jnp.cos(phase)
    half_sin = jnp.sin(phase)
    phase_cos = jnp.concatenate([half_cos, jnp.flip(half_cos[1:half], 0)], axis=0)
    phase_sin = jnp.concatenate([half_sin, jnp.flip(half_sin[1:half], 0)], axis=0)
    focus_real = (moved_real * phase_cos - moved_imag * phase_sin).astype(jnp.bfloat16)
    focus_imag = (moved_real * phase_sin + moved_imag * phase_cos).astype(jnp.bfloat16)
    image = pulse_transform(jnp.stack([focus_real, focus_imag]), PUL_DEV, 1)
    intensity = (image[0] * image[0] + image[1] * image[1]).astype(jnp.bfloat16)
    block_count = tile_owner.shape[1]
    block_rows = pulses // block_count
    blocks = intensity.reshape(block_count, block_rows * width)
    tiles = lax.axis_size("narrow")
    group = lax.axis_index("narrow")
    tile_ids = jnp.arange(tiles, dtype=jnp.int32)
    own_row = lax.dynamic_slice_in_dim(tile_owner, group, 1, 0)[0]
    member = (own_row[None, :] == tile_ids[:, None]).astype(jnp.bfloat16)
    counts = jnp.sum(
        (tile_owner[:, :, None] == tile_ids[None, None, :]).astype(jnp.int32), axis=(0, 1)
    )
    own_count = jnp.sum(jnp.where(tile_ids == group, counts, 0)).astype(jnp.float32)
    partial = jnp.dot(member, blocks, preferred_element_type=jnp.float32)
    partial = partial.reshape(tiles, block_rows, width)
    incoming = lax.all_to_all(partial, "narrow", split_axis=0, concat_axis=0, tiled=True)
    summed = jnp.sum(incoming, axis=0)[None]
    return summed / own_count


def solution(mesh):
    return jax.shard_map(
        per_device,
        mesh=mesh,
        in_specs=(P(None, "narrow", "wide", None), P(), P(), P("wide"), P("wide"), P()),
        out_specs=P("narrow", None, "wide"),
        check_vma=False,
    )
```

```python
import math

import jax
import jax.numpy as jnp
import ml_dtypes
import numpy as np
from jax import lax
from jax.experimental import pallas as pl
from jax.experimental.pallas import tpu as pltpu
from jax.sharding import PartitionSpec as P

RSPLIT = 128
PUL_DEV = 8
CAP = 8
HALO = 31


def passed_along(shard, axis, by):
    devices = lax.axis_size(axis)
    pairs = [(i, i + by) for i in range(devices) if 0 <= i + by < devices]
    return lax.ppermute(shard, axis, pairs)


def host_twiddle(first, second, sign):
    heads = np.arange(first, dtype=np.int64)
    tails = np.arange(second, dtype=np.int64)
    product = (heads[:, None] * tails[None, :] % (first * second)).astype(np.float32)
    angle = np.float32(sign * 2.0 * math.pi / (first * second)) * product
    return np.stack([np.cos(angle), np.sin(angle)]).astype(np.float32)


def host_tables(size, sign):
    index = np.arange(size, dtype=np.int64)
    product = (index[:, None] * index[None, :] % size).astype(np.float32)
    angle = np.float32(sign * 2.0 * math.pi / size) * product
    norm = np.float32(1.0 / math.sqrt(size))
    cos = (np.cos(angle) * norm).astype(ml_dtypes.bfloat16)
    sin = (np.sin(angle) * norm).astype(ml_dtypes.bfloat16)
    table = np.block([[cos, -sin], [sin, cos]])
    return table, np.ascontiguousarray(table.T)


def twist(mid_real, mid_imag, twiddle):
    twist_cos, twist_sin = twiddle[0], twiddle[1]
    turn_real = (mid_real * twist_cos - mid_imag * twist_sin).astype(jnp.bfloat16)
    turn_imag = (mid_real * twist_sin + mid_imag * twist_cos).astype(jnp.bfloat16)
    return turn_real, turn_imag


def forward_transposed(stacked, table, table_t, twiddle):
    half = stacked.shape[0] // 2
    mid = jnp.dot(table, stacked, preferred_element_type=jnp.float32)
    turn_real, turn_imag = twist(mid[:half], mid[half:], twiddle)
    spec = jnp.dot(
        jnp.concatenate([turn_real, turn_imag], axis=1), table_t, preferred_element_type=jnp.float32
    )
    return spec[:, :half], spec[:, half:]


def inverse_from_transposed(real_t, imag_t, table, table_t, twiddle):
    half = real_t.shape[0]
    mid = jnp.dot(
        jnp.concatenate([real_t, imag_t], axis=1), table_t, preferred_element_type=jnp.float32
    )
    turn_real, turn_imag = twist(mid[:, :half], mid[:, half:], twiddle)
    out = jnp.dot(
        table, jnp.concatenate([turn_real, turn_imag], axis=0), preferred_element_type=jnp.float32
    )
    return out[:half], out[half:]


def range_kernel(
    echo_ref, replica_ref, fwd_ref, fwd_t_ref, inv_ref, inv_t_ref, fwd_tw_ref, inv_tw_ref, out_ref, wide_ref
):
    pulses = echo_ref.shape[1] // echo_ref.shape[2]
    side = echo_ref.shape[2]
    fwd, fwd_t = fwd_ref[...], fwd_t_ref[...]
    inv, inv_t = inv_ref[...], inv_t_ref[...]
    fwd_tw, inv_tw = fwd_tw_ref[...], inv_tw_ref[...]
    taps = replica_ref[...].astype(jnp.float32)
    filled = taps.shape[1] // side
    blank = jnp.zeros((side - filled, side), jnp.float32)
    pieces = []
    for part in range(2):
        pieces += [taps[part : part + 1, n * side : (n + 1) * side] for n in range(filled)]
        pieces.append(blank)
    replica = jnp.concatenate(pieces, axis=0).astype(jnp.bfloat16)
    rep_real, rep_imag = forward_transposed(replica, fwd, fwd_t, fwd_tw)
    rep_real = rep_real * 128.0
    rep_imag = rep_imag * 128.0
    blocks = []
    for pulse in range(pulses):
        rows = pl.ds(pulse, side, stride=pulses)
        blocks.append(jnp.concatenate([echo_ref[0, rows, :], echo_ref[1, rows, :]], axis=0))
    mid = jnp.dot(fwd, jnp.concatenate(blocks, axis=1), preferred_element_type=jnp.float32)
    along = lambda x: jnp.concatenate([x] * pulses, axis=1)
    down = lambda x: jnp.concatenate([x] * pulses, axis=0)
    turn_real, turn_imag = twist(mid[:side], mid[side:], (along(fwd_tw[0]), along(fwd_tw[1])))
    by_pulse = lambda x, p: x[:, p * side : (p + 1) * side]
    stacked = jnp.concatenate(
        [
            jnp.concatenate([by_pulse(turn_real, p), by_pulse(turn_imag, p)], axis=1)
            for p in range(pulses)
        ],
        axis=0,
    )
    spec = jnp.dot(stacked, fwd_t, preferred_element_type=jnp.float32)
    spec_real, spec_imag = spec[:, :side], spec[:, side:]
    rep_real, rep_imag = down(rep_real), down(rep_imag)
    match_real = (spec_real * rep_real + spec_imag * rep_imag).astype(jnp.bfloat16)
    match_imag = (spec_imag * rep_real - spec_real * rep_imag).astype(jnp.bfloat16)
    mid = jnp.dot(
        jnp.concatenate([match_real, match_imag], axis=1), inv_t, preferred_element_type=jnp.float32
    )
    turn_real, turn_imag = twist(mid[:, :side], mid[:, side:], (down(inv_tw[0]), down(inv_tw[1])))
    rows_of = lambda x, p: x[p * side : (p + 1) * side]
    stacked = jnp.concatenate(
        [
            jnp.concatenate([rows_of(turn_real, p), rows_of(turn_imag, p)], axis=0)
            for p in range(pulses)
        ],
        axis=1,
    )
    comp = jnp.dot(inv, stacked, preferred_element_type=jnp.float32)
    for pulse in range(pulses):
        wide_ref[pl.ds(pulse, side, stride=2 * pulses), :] = by_pulse(comp[:side], pulse)
        wide_ref[pl.ds(pulses + pulse, side, stride=2 * pulses), :] = by_pulse(comp[side:], pulse)
    out_ref[...] = wide_ref[...].astype(jnp.bfloat16)


def range_compress(echo, range_replica):
    pulses, length = echo.shape[1], echo.shape[2]
    side = RSPLIT
    assert length == side * side
    assert range_replica.shape[1] % side == 0 and range_replica.shape[1] <= length
    rows = echo.reshape(2, pulses, side, side).transpose(0, 2, 1, 3).reshape(2, side * pulses, side)
    fwd, fwd_t = host_tables(side, -1)
    inv, inv_t = host_tables(side, 1)
    fwd_tw = host_twiddle(side, side, -1)
    inv_tw = host_twiddle(side, side, 1)
    whole = pl.BlockSpec(memory_space=pltpu.VMEM)
    out = pl.pallas_call(
        range_kernel,
        in_specs=[whole] * 8,
        out_specs=whole,
        out_shape=jax.ShapeDtypeStruct((side * 2 * pulses, side), jnp.bfloat16),
        scratch_shapes=[pltpu.VMEM((side * 2 * pulses, side), jnp.float32)],
        cost_estimate=pl.CostEstimate(
            flops=(pulses + 1) * 4 * 2 * (2 * side) ** 2 * side,
            bytes_accessed=pulses * 2 * 2 * length * 2,
            transcendentals=0,
        ),
    )(
        rows,
        range_replica,
        jnp.asarray(fwd),
        jnp.asarray(fwd_t),
        jnp.asarray(inv),
        jnp.asarray(inv_t),
        jnp.asarray(fwd_tw),
        jnp.asarray(inv_tw),
    )
    return out.reshape(side, 2, pulses, side)


def host_block_table4(size, sign):
    index = np.arange(size, dtype=np.int64)
    product = (index[:, None] * index[None, :] % size).astype(np.float32)
    angle = np.float32(sign * 2.0 * math.pi / size) * product
    norm = np.float32(1.0 / math.sqrt(size))
    cos = (np.cos(angle) * norm).astype(ml_dtypes.bfloat16)
    sin = (np.sin(angle) * norm).astype(ml_dtypes.bfloat16)
    return np.stack([np.stack([cos, -sin], axis=1), np.stack([sin, cos], axis=1)])


def pulse_transform(values, first, sign):
    length, width = values.shape[1], values.shape[2]
    second = length // first
    head = jnp.asarray(host_block_table4(first, sign))
    tail = jnp.asarray(host_block_table4(second, sign))
    twist_cos, twist_sin = (jnp.asarray(t) for t in host_twiddle(first, second, sign))
    split = values.reshape(2, first, second, width)
    mid = jnp.einsum("okrn,rnmc->okmc", head, split, preferred_element_type=jnp.float32)
    mid_real, mid_imag = mid[0], mid[1]
    turn_real = mid_real * twist_cos[:, :, None] - mid_imag * twist_sin[:, :, None]
    turn_imag = mid_real * twist_sin[:, :, None] + mid_imag * twist_cos[:, :, None]
    turned = jnp.stack([turn_real, turn_imag]).astype(jnp.bfloat16)
    out = jnp.einsum("ojrm,rkmc->ojkc", tail, turned, preferred_element_type=jnp.float32)
    return out.reshape(2, length, width)


def per_device(raw_echo, range_replica, interp_weight, band_offset, azimuth_rate, tile_owner):
    echo = raw_echo[:, 0]
    length = echo.shape[2]
    compressed = range_compress(echo, range_replica)
    devices = lax.axis_size("wide")
    width = length // devices
    assert compressed.shape[0] == devices and compressed.shape[3] == width
    turned = lax.all_to_all(compressed, "wide", split_axis=0, concat_axis=2, tiled=True)[0]
    doppler = pulse_transform(turned, PUL_DEV, -1).astype(jnp.bfloat16)
    rim = passed_along(doppler[:, :, :HALO], "wide", -1)
    extended = jnp.concatenate([doppler, rim], axis=2)
    pulses = extended.shape[1]
    columns = jnp.arange(width + HALO, dtype=jnp.int32)
    bins = jnp.arange(width, dtype=jnp.int32) + band_offset
    moved_real = jnp.zeros((pulses, width), jnp.float32)
    moved_imag = jnp.zeros((pulses, width), jnp.float32)
    taps = interp_weight.shape[0]
    targets = (bins[None, :] + jnp.arange(taps, dtype=jnp.int32)[:, None]).reshape(taps * width)
    select = (columns[:, None] == targets[None, :]).astype(jnp.bfloat16)
    picked = jnp.einsum("xpc,cn->xpn", extended, select, preferred_element_type=jnp.bfloat16)
    for tap_index in range(taps):
        weight = interp_weight[tap_index][:, None]
        tap_values = picked[:, :, tap_index * width : (tap_index + 1) * width].astype(jnp.float32)
        moved_real = moved_real + weight * tap_values[0]
        moved_imag = moved_imag + weight * tap_values[1]
    half = pulses // 2
    freq = jnp.arange(half + 1, dtype=jnp.int32)
    shifted = ((freq + half) % pulses - half).astype(jnp.float32) / pulses
    phase = math.pi * (shifted * shifted)[:, None] / azimuth_rate[None, :]
    half_cos = jnp.cos(phase)
    half_sin = jnp.sin(phase)
    phase_cos = jnp.concatenate([half_cos, jnp.flip(half_cos[1:half], 0)], axis=0)
    phase_sin = jnp.concatenate([half_sin, jnp.flip(half_sin[1:half], 0)], axis=0)
    focus_real = (moved_real * phase_cos - moved_imag * phase_sin).astype(jnp.bfloat16)
    focus_imag = (moved_real * phase_sin + moved_imag * phase_cos).astype(jnp.bfloat16)
    image = pulse_transform(jnp.stack([focus_real, focus_imag]), PUL_DEV, 1)
    intensity = (image[0] * image[0] + image[1] * image[1]).astype(jnp.bfloat16)
    block_count = tile_owner.shape[1]
    block_rows = pulses // block_count
    blocks = intensity.reshape(block_count, block_rows * width)
    tiles = lax.axis_size("narrow")
    group = lax.axis_index("narrow")
    tile_ids = jnp.arange(tiles, dtype=jnp.int32)
    own_row = lax.dynamic_slice_in_dim(tile_owner, group, 1, 0)[0]
    member = (own_row[None, :] == tile_ids[:, None]).astype(jnp.bfloat16)
    counts = jnp.sum(
        (tile_owner[:, :, None] == tile_ids[None, None, :]).astype(jnp.int32), axis=(0, 1)
    )
    own_count = jnp.sum(jnp.where(tile_ids == group, counts, 0)).astype(jnp.float32)
    partial = jnp.dot(member, blocks, preferred_element_type=jnp.float32)
    partial = partial.reshape(tiles, block_rows, width)
    incoming = lax.all_to_all(partial, "narrow", split_axis=0, concat_axis=0, tiled=True)
    summed = jnp.sum(incoming, axis=0)[None]
    return summed / own_count


def solution(mesh):
    return jax.shard_map(
        per_device,
        mesh=mesh,
        in_specs=(P(None, "narrow", "wide", None), P(), P(), P("wide"), P("wide"), P()),
        out_specs=P("narrow", None, "wide"),
        check_vma=False,
    )
```

```python
import math

import jax
import jax.numpy as jnp
import ml_dtypes
import numpy as np
from jax import lax
from jax.experimental import pallas as pl
from jax.experimental.pallas import tpu as pltpu
from jax.sharding import PartitionSpec as P

RSPLIT = 128
PUL_DEV = 8
CAP = 8
HALO = 31


def passed_along(shard, axis, by):
    devices = lax.axis_size(axis)
    pairs = [(i, i + by) for i in range(devices) if 0 <= i + by < devices]
    return lax.ppermute(shard, axis, pairs)


def host_twiddle(first, second, sign):
    heads = np.arange(first, dtype=np.int64)
    tails = np.arange(second, dtype=np.int64)
    product = (heads[:, None] * tails[None, :] % (first * second)).astype(np.float32)
    angle = np.float32(sign * 2.0 * math.pi / (first * second)) * product
    return np.stack([np.cos(angle), np.sin(angle)]).astype(np.float32)


def host_tables(size, sign):
    index = np.arange(size, dtype=np.int64)
    product = (index[:, None] * index[None, :] % size).astype(np.float32)
    angle = np.float32(sign * 2.0 * math.pi / size) * product
    norm = np.float32(1.0 / math.sqrt(size))
    cos = (np.cos(angle) * norm).astype(ml_dtypes.bfloat16)
    sin = (np.sin(angle) * norm).astype(ml_dtypes.bfloat16)
    table = np.block([[cos, -sin], [sin, cos]])
    return table, np.ascontiguousarray(table.T)


def twist(mid_real, mid_imag, twiddle):
    twist_cos, twist_sin = twiddle[0], twiddle[1]
    turn_real = (mid_real * twist_cos - mid_imag * twist_sin).astype(jnp.bfloat16)
    turn_imag = (mid_real * twist_sin + mid_imag * twist_cos).astype(jnp.bfloat16)
    return turn_real, turn_imag


def forward_transposed(stacked, table, table_t, twiddle):
    half = stacked.shape[0] // 2
    mid = jnp.dot(table, stacked, preferred_element_type=jnp.float32)
    turn_real, turn_imag = twist(mid[:half], mid[half:], twiddle)
    spec = jnp.dot(
        jnp.concatenate([turn_real, turn_imag], axis=1), table_t, preferred_element_type=jnp.float32
    )
    return spec[:, :half], spec[:, half:]


def inverse_from_transposed(real_t, imag_t, table, table_t, twiddle):
    half = real_t.shape[0]
    mid = jnp.dot(
        jnp.concatenate([real_t, imag_t], axis=1), table_t, preferred_element_type=jnp.float32
    )
    turn_real, turn_imag = twist(mid[:, :half], mid[:, half:], twiddle)
    out = jnp.dot(
        table, jnp.concatenate([turn_real, turn_imag], axis=0), preferred_element_type=jnp.float32
    )
    return out[:half], out[half:]


def range_kernel(
    echo_ref, replica_ref, fwd_ref, fwd_t_ref, inv_ref, inv_t_ref, fwd_tw_ref, inv_tw_ref, out_ref, wide_ref
):
    pulses = echo_ref.shape[1] // echo_ref.shape[2]
    side = echo_ref.shape[2]
    fwd, fwd_t = fwd_ref[...], fwd_t_ref[...]
    inv, inv_t = inv_ref[...], inv_t_ref[...]
    fwd_tw, inv_tw = fwd_tw_ref[...], inv_tw_ref[...]
    taps = replica_ref[...].astype(jnp.float32)
    filled = taps.shape[1] // side
    blank = jnp.zeros((side - filled, side), jnp.float32)
    pieces = []
    for part in range(2):
        pieces += [taps[part : part + 1, n * side : (n + 1) * side] for n in range(filled)]
        pieces.append(blank)
    replica = jnp.concatenate(pieces, axis=0).astype(jnp.bfloat16)
    rep_real, rep_imag = forward_transposed(replica, fwd, fwd_t, fwd_tw)
    rep_real = rep_real * 128.0
    rep_imag = rep_imag * 128.0
    blocks = []
    for pulse in range(pulses):
        rows = pl.ds(pulse, side, stride=pulses)
        blocks.append(jnp.concatenate([echo_ref[0, rows, :], echo_ref[1, rows, :]], axis=0))
    mid = jnp.dot(fwd, jnp.concatenate(blocks, axis=1), preferred_element_type=jnp.float32)
    along = lambda x: jnp.concatenate([x] * pulses, axis=1)
    down = lambda x: jnp.concatenate([x] * pulses, axis=0)
    turn_real, turn_imag = twist(mid[:side], mid[side:], (along(fwd_tw[0]), along(fwd_tw[1])))
    by_pulse = lambda x, p: x[:, p * side : (p + 1) * side]
    stacked = jnp.concatenate(
        [
            jnp.concatenate([by_pulse(turn_real, p), by_pulse(turn_imag, p)], axis=1)
            for p in range(pulses)
        ],
        axis=0,
    )
    spec = jnp.dot(stacked, fwd_t, preferred_element_type=jnp.float32)
    spec_real, spec_imag = spec[:, :side], spec[:, side:]
    rep_real, rep_imag = down(rep_real), down(rep_imag)
    match_real = (spec_real * rep_real + spec_imag * rep_imag).astype(jnp.bfloat16)
    match_imag = (spec_imag * rep_real - spec_real * rep_imag).astype(jnp.bfloat16)
    mid = jnp.dot(
        jnp.concatenate([match_real, match_imag], axis=1), inv_t, preferred_element_type=jnp.float32
    )
    turn_real, turn_imag = twist(mid[:, :side], mid[:, side:], (down(inv_tw[0]), down(inv_tw[1])))
    rows_of = lambda x, p: x[p * side : (p + 1) * side]
    stacked = jnp.concatenate(
        [
            jnp.concatenate([rows_of(turn_real, p), rows_of(turn_imag, p)], axis=0)
            for p in range(pulses)
        ],
        axis=1,
    )
    comp = jnp.dot(inv, stacked, preferred_element_type=jnp.float32)
    for pulse in range(pulses):
        wide_ref[pl.ds(pulse, side, stride=2 * pulses), :] = by_pulse(comp[:side], pulse)
        wide_ref[pl.ds(pulses + pulse, side, stride=2 * pulses), :] = by_pulse(comp[side:], pulse)
    out_ref[...] = wide_ref[...].astype(jnp.bfloat16)


def range_compress(echo, range_replica):
    pulses, length = echo.shape[1], echo.shape[2]
    side = RSPLIT
    assert length == side * side
    assert range_replica.shape[1] % side == 0 and range_replica.shape[1] <= length
    rows = echo.reshape(2, pulses, side, side).transpose(0, 2, 1, 3).reshape(2, side * pulses, side)
    fwd, fwd_t = host_tables(side, -1)
    inv, inv_t = host_tables(side, 1)
    fwd_tw = host_twiddle(side, side, -1)
    inv_tw = host_twiddle(side, side, 1)
    whole = pl.BlockSpec(memory_space=pltpu.VMEM)
    out = pl.pallas_call(
        range_kernel,
        in_specs=[whole] * 8,
        out_specs=whole,
        out_shape=jax.ShapeDtypeStruct((side * 2 * pulses, side), jnp.bfloat16),
        scratch_shapes=[pltpu.VMEM((side * 2 * pulses, side), jnp.float32)],
        cost_estimate=pl.CostEstimate(
            flops=(pulses + 1) * 4 * 2 * (2 * side) ** 2 * side,
            bytes_accessed=pulses * 2 * 2 * length * 2,
            transcendentals=0,
        ),
    )(
        rows,
        range_replica,
        jnp.asarray(fwd),
        jnp.asarray(fwd_t),
        jnp.asarray(inv),
        jnp.asarray(inv_t),
        jnp.asarray(fwd_tw),
        jnp.asarray(inv_tw),
    )
    return out.reshape(side, 2, pulses, side)


def host_block_table4(size, sign):
    index = np.arange(size, dtype=np.int64)
    product = (index[:, None] * index[None, :] % size).astype(np.float32)
    angle = np.float32(sign * 2.0 * math.pi / size) * product
    norm = np.float32(1.0 / math.sqrt(size))
    cos = (np.cos(angle) * norm).astype(ml_dtypes.bfloat16)
    sin = (np.sin(angle) * norm).astype(ml_dtypes.bfloat16)
    return np.stack([np.stack([cos, -sin], axis=1), np.stack([sin, cos], axis=1)])


def pulse_transform(values, first, sign):
    length, width = values.shape[1], values.shape[2]
    second = length // first
    head = jnp.asarray(host_block_table4(first, sign))
    tail = jnp.asarray(host_block_table4(second, sign))
    twist_cos, twist_sin = (jnp.asarray(t) for t in host_twiddle(first, second, sign))
    split = values.reshape(2, first, second, width)
    mid = jnp.einsum("okrn,rnmc->okmc", head, split, preferred_element_type=jnp.float32)
    mid_real, mid_imag = mid[0], mid[1]
    turn_real = mid_real * twist_cos[:, :, None] - mid_imag * twist_sin[:, :, None]
    turn_imag = mid_real * twist_sin[:, :, None] + mid_imag * twist_cos[:, :, None]
    turned = jnp.stack([turn_real, turn_imag]).astype(jnp.bfloat16)
    out = jnp.einsum("ojrm,rkmc->ojkc", tail, turned, preferred_element_type=jnp.float32)
    return out.reshape(2, length, width)


def per_device(raw_echo, range_replica, interp_weight, band_offset, azimuth_rate, tile_owner):
    echo = raw_echo[:, 0]
    length = echo.shape[2]
    compressed = range_compress(echo, range_replica)
    devices = lax.axis_size("wide")
    width = length // devices
    assert compressed.shape[0] == devices and compressed.shape[3] == width
    turned = lax.all_to_all(compressed, "wide", split_axis=0, concat_axis=2, tiled=True)[0]
    doppler = pulse_transform(turned, PUL_DEV, -1).astype(jnp.bfloat16)
    rim = passed_along(doppler[:, :, :HALO], "wide", -1)
    extended = jnp.concatenate([doppler, rim], axis=2)
    pulses = extended.shape[1]
    columns = jnp.arange(width + HALO, dtype=jnp.int32)
    bins = jnp.arange(width, dtype=jnp.int32) + band_offset
    moved_real = jnp.zeros((pulses, width), jnp.float32)
    moved_imag = jnp.zeros((pulses, width), jnp.float32)
    taps = interp_weight.shape[0]
    targets = (bins[None, :] + jnp.arange(taps, dtype=jnp.int32)[:, None]).reshape(taps * width)
    select = (columns[:, None] == targets[None, :]).astype(jnp.bfloat16)
    picked = jnp.einsum("xpc,cn->xpn", extended, select, preferred_element_type=jnp.bfloat16)
    for tap_index in range(taps):
        weight = interp_weight[tap_index][:, None]
        tap_values = picked[:, :, tap_index * width : (tap_index + 1) * width].astype(jnp.float32)
        moved_real = moved_real + weight * tap_values[0]
        moved_imag = moved_imag + weight * tap_values[1]
    half = pulses // 2
    freq = jnp.arange(half + 1, dtype=jnp.int32)
    shifted = ((freq + half) % pulses - half).astype(jnp.float32) / pulses
    phase = math.pi * (shifted * shifted)[:, None] / azimuth_rate[None, :]
    half_cos = jnp.cos(phase)
    half_sin = jnp.sin(phase)
    phase_cos = jnp.concatenate([half_cos, jnp.flip(half_cos[1:half], 0)], axis=0)
    phase_sin = jnp.concatenate([half_sin, jnp.flip(half_sin[1:half], 0)], axis=0)
    focus_real = (moved_real * phase_cos - moved_imag * phase_sin).astype(jnp.bfloat16)
    focus_imag = (moved_real * phase_sin + moved_imag * phase_cos).astype(jnp.bfloat16)
    image = pulse_transform(jnp.stack([focus_real, focus_imag]), PUL_DEV, 1)
    intensity = (image[0] * image[0] + image[1] * image[1]).astype(jnp.bfloat16)
    block_count = tile_owner.shape[1]
    block_rows = pulses // block_count
    second = pulses // PUL_DEV
    per_block = block_rows // PUL_DEV
    blocks = intensity.reshape(second, PUL_DEV, width).transpose(1, 0, 2)
    blocks = blocks.reshape(PUL_DEV, block_count, per_block, width)
    tiles = lax.axis_size("narrow")
    group = lax.axis_index("narrow")
    tile_ids = jnp.arange(tiles, dtype=jnp.int32)
    own_row = lax.dynamic_slice_in_dim(tile_owner, group, 1, 0)[0]
    member = (own_row[None, :] == tile_ids[:, None]).astype(jnp.bfloat16)
    counts = jnp.sum(
        (tile_owner[:, :, None] == tile_ids[None, None, :]).astype(jnp.int32), axis=(0, 1)
    )
    own_count = jnp.sum(jnp.where(tile_ids == group, counts, 0)).astype(jnp.float32)
    partial = jnp.einsum("tb,kbjc->tkjc", member, blocks, preferred_element_type=jnp.float32)
    incoming = lax.all_to_all(partial, "narrow", split_axis=0, concat_axis=0, tiled=True)
    summed = jnp.sum(incoming, axis=0).transpose(1, 0, 2).reshape(1, block_rows, width)
    return summed / own_count


def solution(mesh):
    return jax.shard_map(
        per_device,
        mesh=mesh,
        in_specs=(P(None, "narrow", "wide", None), P(), P(), P("wide"), P("wide"), P()),
        out_specs=P("narrow", None, "wide"),
        check_vma=False,
    )
```

```python
import math

import jax
import jax.numpy as jnp
import ml_dtypes
import numpy as np
from jax import lax
from jax.experimental import pallas as pl
from jax.experimental.pallas import tpu as pltpu
from jax.sharding import PartitionSpec as P

RSPLIT = 128
PUL_DEV = 8
CAP = 8
HALO = 31


def passed_along(shard, axis, by):
    devices = lax.axis_size(axis)
    pairs = [(i, i + by) for i in range(devices) if 0 <= i + by < devices]
    return lax.ppermute(shard, axis, pairs)


def host_twiddle(first, second, sign):
    heads = np.arange(first, dtype=np.int64)
    tails = np.arange(second, dtype=np.int64)
    product = (heads[:, None] * tails[None, :] % (first * second)).astype(np.float32)
    angle = np.float32(sign * 2.0 * math.pi / (first * second)) * product
    return np.stack([np.cos(angle), np.sin(angle)]).astype(np.float32)


def host_tables(size, sign):
    index = np.arange(size, dtype=np.int64)
    product = (index[:, None] * index[None, :] % size).astype(np.float32)
    angle = np.float32(sign * 2.0 * math.pi / size) * product
    norm = np.float32(1.0 / math.sqrt(size))
    cos = (np.cos(angle) * norm).astype(ml_dtypes.bfloat16)
    sin = (np.sin(angle) * norm).astype(ml_dtypes.bfloat16)
    table = np.block([[cos, -sin], [sin, cos]])
    return table, np.ascontiguousarray(table.T)


def twist(mid_real, mid_imag, twiddle):
    twist_cos, twist_sin = twiddle[0], twiddle[1]
    turn_real = (mid_real * twist_cos - mid_imag * twist_sin).astype(jnp.bfloat16)
    turn_imag = (mid_real * twist_sin + mid_imag * twist_cos).astype(jnp.bfloat16)
    return turn_real, turn_imag


def forward_transposed(stacked, table, table_t, twiddle):
    half = stacked.shape[0] // 2
    mid = jnp.dot(table, stacked, preferred_element_type=jnp.float32)
    turn_real, turn_imag = twist(mid[:half], mid[half:], twiddle)
    spec = jnp.dot(
        jnp.concatenate([turn_real, turn_imag], axis=1), table_t, preferred_element_type=jnp.float32
    )
    return spec[:, :half], spec[:, half:]


def inverse_from_transposed(real_t, imag_t, table, table_t, twiddle):
    half = real_t.shape[0]
    mid = jnp.dot(
        jnp.concatenate([real_t, imag_t], axis=1), table_t, preferred_element_type=jnp.float32
    )
    turn_real, turn_imag = twist(mid[:, :half], mid[:, half:], twiddle)
    out = jnp.dot(
        table, jnp.concatenate([turn_real, turn_imag], axis=0), preferred_element_type=jnp.float32
    )
    return out[:half], out[half:]


def range_kernel(
    echo_ref, replica_ref, fwd_ref, fwd_t_ref, inv_ref, inv_t_ref, fwd_tw_ref, inv_tw_ref, out_ref, wide_ref
):
    pulses = echo_ref.shape[1] // echo_ref.shape[2]
    side = echo_ref.shape[2]
    fwd, fwd_t = fwd_ref[...], fwd_t_ref[...]
    inv, inv_t = inv_ref[...], inv_t_ref[...]
    fwd_tw, inv_tw = fwd_tw_ref[...], inv_tw_ref[...]
    taps = replica_ref[...].astype(jnp.float32)
    filled = taps.shape[1] // side
    blank = jnp.zeros((side - filled, side), jnp.float32)
    pieces = []
    for part in range(2):
        pieces += [taps[part : part + 1, n * side : (n + 1) * side] for n in range(filled)]
        pieces.append(blank)
    replica = jnp.concatenate(pieces, axis=0).astype(jnp.bfloat16)
    rep_real, rep_imag = forward_transposed(replica, fwd, fwd_t, fwd_tw)
    rep_real = rep_real * 128.0
    rep_imag = rep_imag * 128.0
    blocks = []
    for pulse in range(pulses):
        rows = pl.ds(pulse, side, stride=pulses)
        blocks.append(jnp.concatenate([echo_ref[0, rows, :], echo_ref[1, rows, :]], axis=0))
    mid = jnp.dot(fwd, jnp.concatenate(blocks, axis=1), preferred_element_type=jnp.float32)
    along = lambda x: jnp.concatenate([x] * pulses, axis=1)
    down = lambda x: jnp.concatenate([x] * pulses, axis=0)
    turn_real, turn_imag = twist(mid[:side], mid[side:], (along(fwd_tw[0]), along(fwd_tw[1])))
    by_pulse = lambda x, p: x[:, p * side : (p + 1) * side]
    stacked = jnp.concatenate(
        [
            jnp.concatenate([by_pulse(turn_real, p), by_pulse(turn_imag, p)], axis=1)
            for p in range(pulses)
        ],
        axis=0,
    )
    spec = jnp.dot(stacked, fwd_t, preferred_element_type=jnp.float32)
    spec_real, spec_imag = spec[:, :side], spec[:, side:]
    rep_real, rep_imag = down(rep_real), down(rep_imag)
    match_real = (spec_real * rep_real + spec_imag * rep_imag).astype(jnp.bfloat16)
    match_imag = (spec_imag * rep_real - spec_real * rep_imag).astype(jnp.bfloat16)
    mid = jnp.dot(
        jnp.concatenate([match_real, match_imag], axis=1), inv_t, preferred_element_type=jnp.float32
    )
    turn_real, turn_imag = twist(mid[:, :side], mid[:, side:], (down(inv_tw[0]), down(inv_tw[1])))
    rows_of = lambda x, p: x[p * side : (p + 1) * side]
    stacked = jnp.concatenate(
        [
            jnp.concatenate([rows_of(turn_real, p), rows_of(turn_imag, p)], axis=0)
            for p in range(pulses)
        ],
        axis=1,
    )
    comp = jnp.dot(inv, stacked, preferred_element_type=jnp.float32)
    for pulse in range(pulses):
        wide_ref[pl.ds(pulse, side, stride=2 * pulses), :] = by_pulse(comp[:side], pulse)
        wide_ref[pl.ds(pulses + pulse, side, stride=2 * pulses), :] = by_pulse(comp[side:], pulse)
    out_ref[...] = wide_ref[...].astype(jnp.bfloat16)


def range_compress(echo, range_replica):
    pulses, length = echo.shape[1], echo.shape[2]
    side = RSPLIT
    assert length == side * side
    assert range_replica.shape[1] % side == 0 and range_replica.shape[1] <= length
    rows = echo.reshape(2, pulses, side, side).transpose(0, 2, 1, 3).reshape(2, side * pulses, side)
    fwd, fwd_t = host_tables(side, -1)
    inv, inv_t = host_tables(side, 1)
    fwd_tw = host_twiddle(side, side, -1)
    inv_tw = host_twiddle(side, side, 1)
    whole = pl.BlockSpec(memory_space=pltpu.VMEM)
    out = pl.pallas_call(
        range_kernel,
        in_specs=[whole] * 8,
        out_specs=whole,
        out_shape=jax.ShapeDtypeStruct((side * 2 * pulses, side), jnp.bfloat16),
        scratch_shapes=[pltpu.VMEM((side * 2 * pulses, side), jnp.float32)],
        cost_estimate=pl.CostEstimate(
            flops=(pulses + 1) * 4 * 2 * (2 * side) ** 2 * side,
            bytes_accessed=pulses * 2 * 2 * length * 2,
            transcendentals=0,
        ),
    )(
        rows,
        range_replica,
        jnp.asarray(fwd),
        jnp.asarray(fwd_t),
        jnp.asarray(inv),
        jnp.asarray(inv_t),
        jnp.asarray(fwd_tw),
        jnp.asarray(inv_tw),
    )
    return out.reshape(side, 2, pulses, side)


def host_block_table4(size, sign):
    index = np.arange(size, dtype=np.int64)
    product = (index[:, None] * index[None, :] % size).astype(np.float32)
    angle = np.float32(sign * 2.0 * math.pi / size) * product
    norm = np.float32(1.0 / math.sqrt(size))
    cos = (np.cos(angle) * norm).astype(ml_dtypes.bfloat16)
    sin = (np.sin(angle) * norm).astype(ml_dtypes.bfloat16)
    return np.stack([np.stack([cos, -sin], axis=1), np.stack([sin, cos], axis=1)])


def pulse_transform(values, first, sign):
    length, width = values.shape[1], values.shape[2]
    second = length // first
    head = jnp.asarray(host_block_table4(first, sign))
    tail = jnp.asarray(host_block_table4(second, sign))
    twist_cos, twist_sin = (jnp.asarray(t) for t in host_twiddle(first, second, sign))
    split = values.reshape(2, first, second, width)
    mid = jnp.einsum("okrn,rnmc->okmc", head, split, preferred_element_type=jnp.float32)
    mid_real, mid_imag = mid[0], mid[1]
    turn_real = mid_real * twist_cos[:, :, None] - mid_imag * twist_sin[:, :, None]
    turn_imag = mid_real * twist_sin[:, :, None] + mid_imag * twist_cos[:, :, None]
    turned = jnp.stack([turn_real, turn_imag]).astype(jnp.bfloat16)
    out = jnp.einsum("ojrm,rkmc->ojkc", tail, turned, preferred_element_type=jnp.float32)
    return out.reshape(2, length, width)


def per_device(raw_echo, range_replica, interp_weight, band_offset, azimuth_rate, tile_owner):
    echo = raw_echo[:, 0]
    length = echo.shape[2]
    compressed = range_compress(echo, range_replica)
    devices = lax.axis_size("wide")
    width = length // devices
    assert compressed.shape[0] == devices and compressed.shape[3] == width
    turned = lax.all_to_all(compressed, "wide", split_axis=0, concat_axis=2, tiled=True)[0]
    doppler = pulse_transform(turned, PUL_DEV, -1).astype(jnp.bfloat16)
    rim = passed_along(doppler[:, :, :HALO], "wide", -1)
    pulses = doppler.shape[1]
    columns = jnp.arange(width + HALO, dtype=jnp.int32)
    bins = jnp.arange(width, dtype=jnp.int32) + band_offset
    moved_real = jnp.zeros((pulses, width), jnp.float32)
    moved_imag = jnp.zeros((pulses, width), jnp.float32)
    taps = interp_weight.shape[0]
    targets = (bins[None, :] + jnp.arange(taps, dtype=jnp.int32)[:, None]).reshape(taps * width)
    select = (columns[:, None] == targets[None, :]).astype(jnp.bfloat16)
    picked = jnp.einsum("xpc,cn->xpn", doppler, select[:width], preferred_element_type=jnp.bfloat16)
    reach = 32
    assert reach > HALO and reach <= width
    rim_select = select[width:].reshape(HALO, taps, width)[:, :, width - reach :]
    rim_picked = jnp.einsum(
        "xpc,ckn->xpkn", rim, rim_select, preferred_element_type=jnp.bfloat16
    )
    for tap_index in range(taps):
        weight = interp_weight[tap_index][:, None]
        own = picked[:, :, tap_index * width : (tap_index + 1) * width]
        beyond = jnp.pad(rim_picked[:, :, tap_index], ((0, 0), (0, 0), (width - reach, 0)))
        tap_values = (own + beyond).astype(jnp.float32)
        moved_real = moved_real + weight * tap_values[0]
        moved_imag = moved_imag + weight * tap_values[1]
    half = pulses // 2
    freq = jnp.arange(half + 1, dtype=jnp.int32)
    shifted = ((freq + half) % pulses - half).astype(jnp.float32) / pulses
    phase = math.pi * (shifted * shifted)[:, None] / azimuth_rate[None, :]
    half_cos = jnp.cos(phase)
    half_sin = jnp.sin(phase)
    phase_cos = jnp.concatenate([half_cos, jnp.flip(half_cos[1:half], 0)], axis=0)
    phase_sin = jnp.concatenate([half_sin, jnp.flip(half_sin[1:half], 0)], axis=0)
    focus_real = (moved_real * phase_cos - moved_imag * phase_sin).astype(jnp.bfloat16)
    focus_imag = (moved_real * phase_sin + moved_imag * phase_cos).astype(jnp.bfloat16)
    image = pulse_transform(jnp.stack([focus_real, focus_imag]), PUL_DEV, 1)
    intensity = (image[0] * image[0] + image[1] * image[1]).astype(jnp.bfloat16)
    block_count = tile_owner.shape[1]
    block_rows = pulses // block_count
    second = pulses // PUL_DEV
    per_block = block_rows // PUL_DEV
    blocks = intensity.reshape(second, PUL_DEV, width).transpose(1, 0, 2)
    blocks = blocks.reshape(PUL_DEV, block_count, per_block, width)
    tiles = lax.axis_size("narrow")
    group = lax.axis_index("narrow")
    tile_ids = jnp.arange(tiles, dtype=jnp.int32)
    own_row = lax.dynamic_slice_in_dim(tile_owner, group, 1, 0)[0]
    member = (own_row[None, :] == tile_ids[:, None]).astype(jnp.bfloat16)
    counts = jnp.sum(
        (tile_owner[:, :, None] == tile_ids[None, None, :]).astype(jnp.int32), axis=(0, 1)
    )
    own_count = jnp.sum(jnp.where(tile_ids == group, counts, 0)).astype(jnp.float32)
    partial = jnp.einsum("tb,kbjc->tkjc", member, blocks, preferred_element_type=jnp.float32)
    incoming = lax.all_to_all(partial, "narrow", split_axis=0, concat_axis=0, tiled=True)
    summed = jnp.sum(incoming, axis=0).transpose(1, 0, 2).reshape(1, block_rows, width)
    return summed / own_count


def solution(mesh):
    return jax.shard_map(
        per_device,
        mesh=mesh,
        in_specs=(P(None, "narrow", "wide", None), P(), P(), P("wide"), P("wide"), P()),
        out_specs=P("narrow", None, "wide"),
        check_vma=False,
    )
```

```python
import math

import jax
import jax.numpy as jnp
import ml_dtypes
import numpy as np
from jax import lax
from jax.experimental import pallas as pl
from jax.experimental.pallas import tpu as pltpu
from jax.sharding import PartitionSpec as P

RSPLIT = 128
PUL_DEV = 8
CAP = 8
HALO = 31


def passed_along(shard, axis, by):
    devices = lax.axis_size(axis)
    pairs = [(i, i + by) for i in range(devices) if 0 <= i + by < devices]
    return lax.ppermute(shard, axis, pairs)


def host_twiddle(first, second, sign):
    heads = np.arange(first, dtype=np.int64)
    tails = np.arange(second, dtype=np.int64)
    product = (heads[:, None] * tails[None, :] % (first * second)).astype(np.float32)
    angle = np.float32(sign * 2.0 * math.pi / (first * second)) * product
    return np.stack([np.cos(angle), np.sin(angle)]).astype(np.float32)


def host_tables(size, sign):
    index = np.arange(size, dtype=np.int64)
    product = (index[:, None] * index[None, :] % size).astype(np.float32)
    angle = np.float32(sign * 2.0 * math.pi / size) * product
    norm = np.float32(1.0 / math.sqrt(size))
    cos = (np.cos(angle) * norm).astype(ml_dtypes.bfloat16)
    sin = (np.sin(angle) * norm).astype(ml_dtypes.bfloat16)
    table = np.block([[cos, -sin], [sin, cos]])
    return table, np.ascontiguousarray(table.T)


def twist(mid_real, mid_imag, twiddle):
    twist_cos, twist_sin = twiddle[0], twiddle[1]
    turn_real = (mid_real * twist_cos - mid_imag * twist_sin).astype(jnp.bfloat16)
    turn_imag = (mid_real * twist_sin + mid_imag * twist_cos).astype(jnp.bfloat16)
    return turn_real, turn_imag


def forward_transposed(stacked, table, table_t, twiddle):
    half = stacked.shape[0] // 2
    mid = jnp.dot(table, stacked, preferred_element_type=jnp.float32)
    turn_real, turn_imag = twist(mid[:half], mid[half:], twiddle)
    spec = jnp.dot(
        jnp.concatenate([turn_real, turn_imag], axis=1), table_t, preferred_element_type=jnp.float32
    )
    return spec[:, :half], spec[:, half:]


def inverse_from_transposed(real_t, imag_t, table, table_t, twiddle):
    half = real_t.shape[0]
    mid = jnp.dot(
        jnp.concatenate([real_t, imag_t], axis=1), table_t, preferred_element_type=jnp.float32
    )
    turn_real, turn_imag = twist(mid[:, :half], mid[:, half:], twiddle)
    out = jnp.dot(
        table, jnp.concatenate([turn_real, turn_imag], axis=0), preferred_element_type=jnp.float32
    )
    return out[:half], out[half:]


def range_kernel(
    echo_ref, replica_ref, fwd_ref, fwd_t_ref, inv_ref, inv_t_ref, fwd_tw_ref, inv_tw_ref, out_ref
):
    pulses = echo_ref.shape[1] // echo_ref.shape[2]
    side = echo_ref.shape[2]
    fwd, fwd_t = fwd_ref[...], fwd_t_ref[...]
    inv, inv_t = inv_ref[...], inv_t_ref[...]
    fwd_tw, inv_tw = fwd_tw_ref[...], inv_tw_ref[...]
    taps = replica_ref[...].astype(jnp.float32)
    filled = taps.shape[1] // side
    blank = jnp.zeros((side - filled, side), jnp.float32)
    pieces = []
    for part in range(2):
        pieces += [taps[part : part + 1, n * side : (n + 1) * side] for n in range(filled)]
        pieces.append(blank)
    replica = jnp.concatenate(pieces, axis=0).astype(jnp.bfloat16)
    rep_real, rep_imag = forward_transposed(replica, fwd, fwd_t, fwd_tw)
    rep_real = rep_real * 128.0
    rep_imag = rep_imag * 128.0
    blocks = []
    for pulse in range(pulses):
        rows = pl.ds(pulse, side, stride=pulses)
        blocks.append(jnp.concatenate([echo_ref[0, rows, :], echo_ref[1, rows, :]], axis=0))
    mid = jnp.dot(fwd, jnp.concatenate(blocks, axis=1), preferred_element_type=jnp.float32)
    along = lambda x: jnp.concatenate([x] * pulses, axis=1)
    down = lambda x: jnp.concatenate([x] * pulses, axis=0)
    turn_real, turn_imag = twist(mid[:side], mid[side:], (along(fwd_tw[0]), along(fwd_tw[1])))
    by_pulse = lambda x, p: x[:, p * side : (p + 1) * side]
    stacked = jnp.concatenate(
        [
            jnp.concatenate([by_pulse(turn_real, p), by_pulse(turn_imag, p)], axis=1)
            for p in range(pulses)
        ],
        axis=0,
    )
    spec = jnp.dot(stacked, fwd_t, preferred_element_type=jnp.float32)
    spec_real, spec_imag = spec[:, :side], spec[:, side:]
    rep_real, rep_imag = down(rep_real), down(rep_imag)
    match_real = (spec_real * rep_real + spec_imag * rep_imag).astype(jnp.bfloat16)
    match_imag = (spec_imag * rep_real - spec_real * rep_imag).astype(jnp.bfloat16)
    mid = jnp.dot(
        jnp.concatenate([match_real, match_imag], axis=1), inv_t, preferred_element_type=jnp.float32
    )
    turn_real, turn_imag = twist(mid[:, :side], mid[:, side:], (down(inv_tw[0]), down(inv_tw[1])))
    rows_of = lambda x, p: x[p * side : (p + 1) * side]
    stacked = jnp.concatenate(
        [
            jnp.concatenate([rows_of(turn_real, p), rows_of(turn_imag, p)], axis=0)
            for p in range(pulses)
        ],
        axis=1,
    )
    comp = jnp.dot(inv, stacked, preferred_element_type=jnp.float32)
    out_ref[...] = pltpu.einshape("(rd)(pb)->(drp)b", comp, r=2, p=pulses).astype(jnp.bfloat16)


def range_compress(echo, range_replica):
    pulses, length = echo.shape[1], echo.shape[2]
    side = RSPLIT
    assert length == side * side
    assert range_replica.shape[1] % side == 0 and range_replica.shape[1] <= length
    rows = echo.reshape(2, pulses, side, side).transpose(0, 2, 1, 3).reshape(2, side * pulses, side)
    fwd, fwd_t = host_tables(side, -1)
    inv, inv_t = host_tables(side, 1)
    fwd_tw = host_twiddle(side, side, -1)
    inv_tw = host_twiddle(side, side, 1)
    whole = pl.BlockSpec(memory_space=pltpu.VMEM)
    out = pl.pallas_call(
        range_kernel,
        in_specs=[whole] * 8,
        out_specs=whole,
        out_shape=jax.ShapeDtypeStruct((side * 2 * pulses, side), jnp.bfloat16),
        cost_estimate=pl.CostEstimate(
            flops=(pulses + 1) * 4 * 2 * (2 * side) ** 2 * side,
            bytes_accessed=pulses * 2 * 2 * length * 2,
            transcendentals=0,
        ),
    )(
        rows,
        range_replica,
        jnp.asarray(fwd),
        jnp.asarray(fwd_t),
        jnp.asarray(inv),
        jnp.asarray(inv_t),
        jnp.asarray(fwd_tw),
        jnp.asarray(inv_tw),
    )
    return out.reshape(side, 2, pulses, side)


def host_block_table4(size, sign):
    index = np.arange(size, dtype=np.int64)
    product = (index[:, None] * index[None, :] % size).astype(np.float32)
    angle = np.float32(sign * 2.0 * math.pi / size) * product
    norm = np.float32(1.0 / math.sqrt(size))
    cos = (np.cos(angle) * norm).astype(ml_dtypes.bfloat16)
    sin = (np.sin(angle) * norm).astype(ml_dtypes.bfloat16)
    return np.stack([np.stack([cos, -sin], axis=1), np.stack([sin, cos], axis=1)])


def pulse_transform(values, first, sign):
    length, width = values.shape[1], values.shape[2]
    second = length // first
    head = jnp.asarray(host_block_table4(first, sign))
    tail = jnp.asarray(host_block_table4(second, sign))
    twist_cos, twist_sin = (jnp.asarray(t) for t in host_twiddle(first, second, sign))
    split = values.reshape(2, first, second, width)
    mid = jnp.einsum("okrn,rnmc->okmc", head, split, preferred_element_type=jnp.float32)
    mid_real, mid_imag = mid[0], mid[1]
    turn_real = mid_real * twist_cos[:, :, None] - mid_imag * twist_sin[:, :, None]
    turn_imag = mid_real * twist_sin[:, :, None] + mid_imag * twist_cos[:, :, None]
    turned = jnp.stack([turn_real, turn_imag]).astype(jnp.bfloat16)
    out = jnp.einsum("ojrm,rkmc->ojkc", tail, turned, preferred_element_type=jnp.float32)
    return out.reshape(2, length, width)


def per_device(raw_echo, range_replica, interp_weight, band_offset, azimuth_rate, tile_owner):
    echo = raw_echo[:, 0]
    length = echo.shape[2]
    compressed = range_compress(echo, range_replica)
    devices = lax.axis_size("wide")
    width = length // devices
    assert compressed.shape[0] == devices and compressed.shape[3] == width
    turned = lax.all_to_all(compressed, "wide", split_axis=0, concat_axis=2, tiled=True)[0]
    doppler = pulse_transform(turned, PUL_DEV, -1).astype(jnp.bfloat16)
    rim = passed_along(doppler[:, :, :HALO], "wide", -1)
    extended = jnp.concatenate([doppler, rim], axis=2)
    pulses = extended.shape[1]
    columns = jnp.arange(width + HALO, dtype=jnp.int32)
    bins = jnp.arange(width, dtype=jnp.int32) + band_offset
    moved_real = jnp.zeros((pulses, width), jnp.float32)
    moved_imag = jnp.zeros((pulses, width), jnp.float32)
    taps = interp_weight.shape[0]
    targets = (bins[None, :] + jnp.arange(taps, dtype=jnp.int32)[:, None]).reshape(taps * width)
    select = (columns[:, None] == targets[None, :]).astype(jnp.bfloat16)
    picked = jnp.einsum("xpc,cn->xpn", extended, select, preferred_element_type=jnp.bfloat16)
    for tap_index in range(taps):
        weight = interp_weight[tap_index][:, None]
        tap_values = picked[:, :, tap_index * width : (tap_index + 1) * width].astype(jnp.float32)
        moved_real = moved_real + weight * tap_values[0]
        moved_imag = moved_imag + weight * tap_values[1]
    half = pulses // 2
    freq = jnp.arange(half + 1, dtype=jnp.int32)
    shifted = ((freq + half) % pulses - half).astype(jnp.float32) / pulses
    phase = math.pi * (shifted * shifted)[:, None] / azimuth_rate[None, :]
    half_cos = jnp.cos(phase)
    half_sin = jnp.sin(phase)
    phase_cos = jnp.concatenate([half_cos, jnp.flip(half_cos[1:half], 0)], axis=0)
    phase_sin = jnp.concatenate([half_sin, jnp.flip(half_sin[1:half], 0)], axis=0)
    focus_real = (moved_real * phase_cos - moved_imag * phase_sin).astype(jnp.bfloat16)
    focus_imag = (moved_real * phase_sin + moved_imag * phase_cos).astype(jnp.bfloat16)
    image = pulse_transform(jnp.stack([focus_real, focus_imag]), PUL_DEV, 1)
    intensity = (image[0] * image[0] + image[1] * image[1]).astype(jnp.bfloat16)
    block_count = tile_owner.shape[1]
    block_rows = pulses // block_count
    second = pulses // PUL_DEV
    per_block = block_rows // PUL_DEV
    blocks = intensity.reshape(second, PUL_DEV, width).transpose(1, 0, 2)
    blocks = blocks.reshape(PUL_DEV, block_count, per_block, width)
    tiles = lax.axis_size("narrow")
    group = lax.axis_index("narrow")
    tile_ids = jnp.arange(tiles, dtype=jnp.int32)
    own_row = lax.dynamic_slice_in_dim(tile_owner, group, 1, 0)[0]
    member = (own_row[None, :] == tile_ids[:, None]).astype(jnp.bfloat16)
    counts = jnp.sum(
        (tile_owner[:, :, None] == tile_ids[None, None, :]).astype(jnp.int32), axis=(0, 1)
    )
    own_count = jnp.sum(jnp.where(tile_ids == group, counts, 0)).astype(jnp.float32)
    partial = jnp.einsum("tb,kbjc->tkjc", member, blocks, preferred_element_type=jnp.float32)
    incoming = lax.all_to_all(partial, "narrow", split_axis=0, concat_axis=0, tiled=True)
    summed = jnp.sum(incoming, axis=0).transpose(1, 0, 2).reshape(1, block_rows, width)
    return summed / own_count


def solution(mesh):
    return jax.shard_map(
        per_device,
        mesh=mesh,
        in_specs=(P(None, "narrow", "wide", None), P(), P(), P("wide"), P("wide"), P()),
        out_specs=P("narrow", None, "wide"),
        check_vma=False,
    )
```

```python
import math

import jax
import jax.numpy as jnp
import ml_dtypes
import numpy as np
from jax import lax
from jax.experimental import pallas as pl
from jax.experimental.pallas import tpu as pltpu
from jax.sharding import PartitionSpec as P

RSPLIT = 128
PUL_DEV = 8
CAP = 8
HALO = 31


def passed_along(shard, axis, by):
    devices = lax.axis_size(axis)
    pairs = [(i, i + by) for i in range(devices) if 0 <= i + by < devices]
    return lax.ppermute(shard, axis, pairs)


def host_twiddle(first, second, sign):
    heads = np.arange(first, dtype=np.int64)
    tails = np.arange(second, dtype=np.int64)
    product = (heads[:, None] * tails[None, :] % (first * second)).astype(np.float32)
    angle = np.float32(sign * 2.0 * math.pi / (first * second)) * product
    return np.stack([np.cos(angle), np.sin(angle)]).astype(np.float32)


def host_tables(size, sign):
    index = np.arange(size, dtype=np.int64)
    product = (index[:, None] * index[None, :] % size).astype(np.float32)
    angle = np.float32(sign * 2.0 * math.pi / size) * product
    norm = np.float32(1.0 / math.sqrt(size))
    cos = (np.cos(angle) * norm).astype(ml_dtypes.bfloat16)
    sin = (np.sin(angle) * norm).astype(ml_dtypes.bfloat16)
    table = np.block([[cos, -sin], [sin, cos]])
    return table, np.ascontiguousarray(table.T)


def twist(mid_real, mid_imag, twiddle):
    twist_cos, twist_sin = twiddle[0], twiddle[1]
    turn_real = (mid_real * twist_cos - mid_imag * twist_sin).astype(jnp.bfloat16)
    turn_imag = (mid_real * twist_sin + mid_imag * twist_cos).astype(jnp.bfloat16)
    return turn_real, turn_imag


def forward_transposed(stacked, table, table_t, twiddle):
    half = stacked.shape[0] // 2
    mid = jnp.dot(table, stacked, preferred_element_type=jnp.float32)
    turn_real, turn_imag = twist(mid[:half], mid[half:], twiddle)
    spec = jnp.dot(
        jnp.concatenate([turn_real, turn_imag], axis=1), table_t, preferred_element_type=jnp.float32
    )
    return spec[:, :half], spec[:, half:]


def inverse_from_transposed(real_t, imag_t, table, table_t, twiddle):
    half = real_t.shape[0]
    mid = jnp.dot(
        jnp.concatenate([real_t, imag_t], axis=1), table_t, preferred_element_type=jnp.float32
    )
    turn_real, turn_imag = twist(mid[:, :half], mid[:, half:], twiddle)
    out = jnp.dot(
        table, jnp.concatenate([turn_real, turn_imag], axis=0), preferred_element_type=jnp.float32
    )
    return out[:half], out[half:]


def range_kernel(
    echo_ref, replica_ref, fwd_ref, fwd_t_ref, inv_ref, inv_t_ref, fwd_tw_ref, inv_tw_ref, out_ref
):
    pulses = echo_ref.shape[1] // echo_ref.shape[2]
    side = echo_ref.shape[2]
    fwd, fwd_t = fwd_ref[...], fwd_t_ref[...]
    inv, inv_t = inv_ref[...], inv_t_ref[...]
    fwd_tw, inv_tw = fwd_tw_ref[...], inv_tw_ref[...]
    taps = replica_ref[...].astype(jnp.float32)
    filled = taps.shape[1] // side
    blank = jnp.zeros((side - filled, side), jnp.float32)
    pieces = []
    for part in range(2):
        pieces += [taps[part : part + 1, n * side : (n + 1) * side] for n in range(filled)]
        pieces.append(blank)
    replica = jnp.concatenate(pieces, axis=0).astype(jnp.bfloat16)
    rep_real, rep_imag = forward_transposed(replica, fwd, fwd_t, fwd_tw)
    rep_real = rep_real * 128.0
    rep_imag = rep_imag * 128.0
    split = [
        pltpu.einshape("(np)b->n(pb)", echo_ref[part].astype(jnp.float32), p=pulses)
        for part in range(2)
    ]
    stacked = jnp.concatenate(split, axis=0).astype(jnp.bfloat16)
    mid = jnp.dot(fwd, stacked, preferred_element_type=jnp.float32)
    along = lambda x: jnp.concatenate([x] * pulses, axis=1)
    down = lambda x: jnp.concatenate([x] * pulses, axis=0)
    turn_real, turn_imag = twist(mid[:side], mid[side:], (along(fwd_tw[0]), along(fwd_tw[1])))
    by_pulse = lambda x, p: x[:, p * side : (p + 1) * side]
    stacked = jnp.concatenate(
        [
            jnp.concatenate([by_pulse(turn_real, p), by_pulse(turn_imag, p)], axis=1)
            for p in range(pulses)
        ],
        axis=0,
    )
    spec = jnp.dot(stacked, fwd_t, preferred_element_type=jnp.float32)
    spec_real, spec_imag = spec[:, :side], spec[:, side:]
    rep_real, rep_imag = down(rep_real), down(rep_imag)
    match_real = (spec_real * rep_real + spec_imag * rep_imag).astype(jnp.bfloat16)
    match_imag = (spec_imag * rep_real - spec_real * rep_imag).astype(jnp.bfloat16)
    mid = jnp.dot(
        jnp.concatenate([match_real, match_imag], axis=1), inv_t, preferred_element_type=jnp.float32
    )
    turn_real, turn_imag = twist(mid[:, :side], mid[:, side:], (down(inv_tw[0]), down(inv_tw[1])))
    rows_of = lambda x, p: x[p * side : (p + 1) * side]
    stacked = jnp.concatenate(
        [
            jnp.concatenate([rows_of(turn_real, p), rows_of(turn_imag, p)], axis=0)
            for p in range(pulses)
        ],
        axis=1,
    )
    comp = jnp.dot(inv, stacked, preferred_element_type=jnp.float32)
    out_ref[...] = pltpu.einshape("(rd)(pb)->(drp)b", comp, r=2, p=pulses).astype(jnp.bfloat16)


def range_compress(echo, range_replica):
    pulses, length = echo.shape[1], echo.shape[2]
    side = RSPLIT
    assert length == side * side
    assert range_replica.shape[1] % side == 0 and range_replica.shape[1] <= length
    rows = echo.reshape(2, pulses, side, side).transpose(0, 2, 1, 3).reshape(2, side * pulses, side)
    fwd, fwd_t = host_tables(side, -1)
    inv, inv_t = host_tables(side, 1)
    fwd_tw = host_twiddle(side, side, -1)
    inv_tw = host_twiddle(side, side, 1)
    whole = pl.BlockSpec(memory_space=pltpu.VMEM)
    out = pl.pallas_call(
        range_kernel,
        in_specs=[whole] * 8,
        out_specs=whole,
        out_shape=jax.ShapeDtypeStruct((side * 2 * pulses, side), jnp.bfloat16),
        cost_estimate=pl.CostEstimate(
            flops=(pulses + 1) * 4 * 2 * (2 * side) ** 2 * side,
            bytes_accessed=pulses * 2 * 2 * length * 2,
            transcendentals=0,
        ),
    )(
        rows,
        range_replica,
        jnp.asarray(fwd),
        jnp.asarray(fwd_t),
        jnp.asarray(inv),
        jnp.asarray(inv_t),
        jnp.asarray(fwd_tw),
        jnp.asarray(inv_tw),
    )
    return out.reshape(side, 2, pulses, side)


def host_block_table4(size, sign):
    index = np.arange(size, dtype=np.int64)
    product = (index[:, None] * index[None, :] % size).astype(np.float32)
    angle = np.float32(sign * 2.0 * math.pi / size) * product
    norm = np.float32(1.0 / math.sqrt(size))
    cos = (np.cos(angle) * norm).astype(ml_dtypes.bfloat16)
    sin = (np.sin(angle) * norm).astype(ml_dtypes.bfloat16)
    return np.stack([np.stack([cos, -sin], axis=1), np.stack([sin, cos], axis=1)])


def pulse_transform(values, first, sign):
    length, width = values.shape[1], values.shape[2]
    second = length // first
    head = jnp.asarray(host_block_table4(first, sign))
    tail = jnp.asarray(host_block_table4(second, sign))
    twist_cos, twist_sin = (jnp.asarray(t) for t in host_twiddle(first, second, sign))
    split = values.reshape(2, first, second, width)
    mid = jnp.einsum("okrn,rnmc->okmc", head, split, preferred_element_type=jnp.float32)
    mid_real, mid_imag = mid[0], mid[1]
    turn_real = mid_real * twist_cos[:, :, None] - mid_imag * twist_sin[:, :, None]
    turn_imag = mid_real * twist_sin[:, :, None] + mid_imag * twist_cos[:, :, None]
    turned = jnp.stack([turn_real, turn_imag]).astype(jnp.bfloat16)
    out = jnp.einsum("ojrm,rkmc->ojkc", tail, turned, preferred_element_type=jnp.float32)
    return out.reshape(2, length, width)


def per_device(raw_echo, range_replica, interp_weight, band_offset, azimuth_rate, tile_owner):
    echo = raw_echo[:, 0]
    length = echo.shape[2]
    compressed = range_compress(echo, range_replica)
    devices = lax.axis_size("wide")
    width = length // devices
    assert compressed.shape[0] == devices and compressed.shape[3] == width
    turned = lax.all_to_all(compressed, "wide", split_axis=0, concat_axis=2, tiled=True)[0]
    doppler = pulse_transform(turned, PUL_DEV, -1).astype(jnp.bfloat16)
    rim = passed_along(doppler[:, :, :HALO], "wide", -1)
    extended = jnp.concatenate([doppler, rim], axis=2)
    pulses = extended.shape[1]
    columns = jnp.arange(width + HALO, dtype=jnp.int32)
    bins = jnp.arange(width, dtype=jnp.int32) + band_offset
    moved_real = jnp.zeros((pulses, width), jnp.float32)
    moved_imag = jnp.zeros((pulses, width), jnp.float32)
    taps = interp_weight.shape[0]
    targets = (bins[None, :] + jnp.arange(taps, dtype=jnp.int32)[:, None]).reshape(taps * width)
    select = (columns[:, None] == targets[None, :]).astype(jnp.bfloat16)
    picked = jnp.einsum("xpc,cn->xpn", extended, select, preferred_element_type=jnp.bfloat16)
    for tap_index in range(taps):
        weight = interp_weight[tap_index][:, None]
        tap_values = picked[:, :, tap_index * width : (tap_index + 1) * width].astype(jnp.float32)
        moved_real = moved_real + weight * tap_values[0]
        moved_imag = moved_imag + weight * tap_values[1]
    half = pulses // 2
    freq = jnp.arange(half + 1, dtype=jnp.int32)
    shifted = ((freq + half) % pulses - half).astype(jnp.float32) / pulses
    phase = math.pi * (shifted * shifted)[:, None] / azimuth_rate[None, :]
    half_cos = jnp.cos(phase)
    half_sin = jnp.sin(phase)
    phase_cos = jnp.concatenate([half_cos, jnp.flip(half_cos[1:half], 0)], axis=0)
    phase_sin = jnp.concatenate([half_sin, jnp.flip(half_sin[1:half], 0)], axis=0)
    focus_real = (moved_real * phase_cos - moved_imag * phase_sin).astype(jnp.bfloat16)
    focus_imag = (moved_real * phase_sin + moved_imag * phase_cos).astype(jnp.bfloat16)
    image = pulse_transform(jnp.stack([focus_real, focus_imag]), PUL_DEV, 1)
    intensity = (image[0] * image[0] + image[1] * image[1]).astype(jnp.bfloat16)
    block_count = tile_owner.shape[1]
    block_rows = pulses // block_count
    second = pulses // PUL_DEV
    per_block = block_rows // PUL_DEV
    blocks = intensity.reshape(second, PUL_DEV, width).transpose(1, 0, 2)
    blocks = blocks.reshape(PUL_DEV, block_count, per_block, width)
    tiles = lax.axis_size("narrow")
    group = lax.axis_index("narrow")
    tile_ids = jnp.arange(tiles, dtype=jnp.int32)
    own_row = lax.dynamic_slice_in_dim(tile_owner, group, 1, 0)[0]
    member = (own_row[None, :] == tile_ids[:, None]).astype(jnp.bfloat16)
    counts = jnp.sum(
        (tile_owner[:, :, None] == tile_ids[None, None, :]).astype(jnp.int32), axis=(0, 1)
    )
    own_count = jnp.sum(jnp.where(tile_ids == group, counts, 0)).astype(jnp.float32)
    partial = jnp.einsum("tb,kbjc->tkjc", member, blocks, preferred_element_type=jnp.float32)
    incoming = lax.all_to_all(partial, "narrow", split_axis=0, concat_axis=0, tiled=True)
    summed = jnp.sum(incoming, axis=0).transpose(1, 0, 2).reshape(1, block_rows, width)
    return summed / own_count


def solution(mesh):
    return jax.shard_map(
        per_device,
        mesh=mesh,
        in_specs=(P(None, "narrow", "wide", None), P(), P(), P("wide"), P("wide"), P()),
        out_specs=P("narrow", None, "wide"),
        check_vma=False,
    )
```

```python
import math

import jax
import jax.numpy as jnp
import ml_dtypes
import numpy as np
from jax import lax
from jax.experimental import pallas as pl
from jax.experimental.pallas import tpu as pltpu
from jax.sharding import PartitionSpec as P

RSPLIT = 128
PUL_DEV = 8
CAP = 8
HALO = 31


def passed_along(shard, axis, by):
    devices = lax.axis_size(axis)
    pairs = [(i, i + by) for i in range(devices) if 0 <= i + by < devices]
    return lax.ppermute(shard, axis, pairs)


def host_twiddle(first, second, sign):
    heads = np.arange(first, dtype=np.int64)
    tails = np.arange(second, dtype=np.int64)
    product = (heads[:, None] * tails[None, :] % (first * second)).astype(np.float32)
    angle = np.float32(sign * 2.0 * math.pi / (first * second)) * product
    return np.stack([np.cos(angle), np.sin(angle)]).astype(np.float32)


def host_tables(size, sign):
    index = np.arange(size, dtype=np.int64)
    product = (index[:, None] * index[None, :] % size).astype(np.float32)
    angle = np.float32(sign * 2.0 * math.pi / size) * product
    norm = np.float32(1.0 / math.sqrt(size))
    cos = (np.cos(angle) * norm).astype(ml_dtypes.bfloat16)
    sin = (np.sin(angle) * norm).astype(ml_dtypes.bfloat16)
    table = np.block([[cos, -sin], [sin, cos]])
    return table, np.ascontiguousarray(table.T)


def twist(mid_real, mid_imag, twiddle):
    twist_cos, twist_sin = twiddle[0], twiddle[1]
    turn_real = (mid_real * twist_cos - mid_imag * twist_sin).astype(jnp.bfloat16)
    turn_imag = (mid_real * twist_sin + mid_imag * twist_cos).astype(jnp.bfloat16)
    return turn_real, turn_imag


def forward_transposed(stacked, table, table_t, twiddle):
    half = stacked.shape[0] // 2
    mid = jnp.dot(table, stacked, preferred_element_type=jnp.float32)
    turn_real, turn_imag = twist(mid[:half], mid[half:], twiddle)
    spec = jnp.dot(
        jnp.concatenate([turn_real, turn_imag], axis=1), table_t, preferred_element_type=jnp.float32
    )
    return spec[:, :half], spec[:, half:]


def inverse_from_transposed(real_t, imag_t, table, table_t, twiddle):
    half = real_t.shape[0]
    mid = jnp.dot(
        jnp.concatenate([real_t, imag_t], axis=1), table_t, preferred_element_type=jnp.float32
    )
    turn_real, turn_imag = twist(mid[:, :half], mid[:, half:], twiddle)
    out = jnp.dot(
        table, jnp.concatenate([turn_real, turn_imag], axis=0), preferred_element_type=jnp.float32
    )
    return out[:half], out[half:]


def range_kernel(
    echo_ref, replica_ref, fwd_ref, fwd_t_ref, inv_ref, inv_t_ref, fwd_tw_ref, inv_tw_ref, out_ref
):
    pulses = echo_ref.shape[1] // echo_ref.shape[2]
    side = echo_ref.shape[2]
    fwd, fwd_t = fwd_ref[...], fwd_t_ref[...]
    inv, inv_t = inv_ref[...], inv_t_ref[...]
    fwd_tw, inv_tw = fwd_tw_ref[...], inv_tw_ref[...]
    taps = replica_ref[...].astype(jnp.float32)
    filled = taps.shape[1] // side
    blank = jnp.zeros((side - filled, side), jnp.float32)
    pieces = []
    for part in range(2):
        pieces += [taps[part : part + 1, n * side : (n + 1) * side] for n in range(filled)]
        pieces.append(blank)
    replica = jnp.concatenate(pieces, axis=0).astype(jnp.bfloat16)
    rep_real, rep_imag = forward_transposed(replica, fwd, fwd_t, fwd_tw)
    rep_real = rep_real * 128.0
    rep_imag = rep_imag * 128.0
    blocks = []
    for pulse in range(pulses):
        rows = pl.ds(pulse, side, stride=pulses)
        blocks.append(jnp.concatenate([echo_ref[0, rows, :], echo_ref[1, rows, :]], axis=0))
    mid = jnp.dot(fwd, jnp.concatenate(blocks, axis=1), preferred_element_type=jnp.float32)
    along = lambda x: jnp.concatenate([x] * pulses, axis=1)
    down = lambda x: jnp.concatenate([x] * pulses, axis=0)
    turn_real, turn_imag = twist(mid[:side], mid[side:], (along(fwd_tw[0]), along(fwd_tw[1])))
    by_pulse = lambda x, p: x[:, p * side : (p + 1) * side]
    stacked = jnp.concatenate(
        [
            jnp.concatenate([by_pulse(turn_real, p), by_pulse(turn_imag, p)], axis=1)
            for p in range(pulses)
        ],
        axis=0,
    )
    spec = jnp.dot(stacked, fwd_t, preferred_element_type=jnp.float32)
    spec_real, spec_imag = spec[:, :side], spec[:, side:]
    rep_real, rep_imag = down(rep_real), down(rep_imag)
    match_real = (spec_real * rep_real + spec_imag * rep_imag).astype(jnp.bfloat16)
    match_imag = (spec_imag * rep_real - spec_real * rep_imag).astype(jnp.bfloat16)
    mid = jnp.dot(
        jnp.concatenate([match_real, match_imag], axis=1), inv_t, preferred_element_type=jnp.float32
    )
    turn_real, turn_imag = twist(mid[:, :side], mid[:, side:], (down(inv_tw[0]), down(inv_tw[1])))
    rows_of = lambda x, p: x[p * side : (p + 1) * side]
    stacked = jnp.concatenate(
        [
            jnp.concatenate([rows_of(turn_real, p), rows_of(turn_imag, p)], axis=0)
            for p in range(pulses)
        ],
        axis=1,
    )
    comp = jnp.dot(inv, stacked, preferred_element_type=jnp.float32)
    out_ref[...] = pltpu.einshape("(rd)(pb)->(drp)b", comp, r=2, p=pulses).astype(jnp.bfloat16)


def range_compress(echo, range_replica):
    pulses, length = echo.shape[1], echo.shape[2]
    side = RSPLIT
    assert length == side * side
    assert range_replica.shape[1] % side == 0 and range_replica.shape[1] <= length
    rows = echo.reshape(2, pulses, side, side).transpose(0, 2, 1, 3).reshape(2, side * pulses, side)
    fwd, fwd_t = host_tables(side, -1)
    inv, inv_t = host_tables(side, 1)
    fwd_tw = host_twiddle(side, side, -1)
    inv_tw = host_twiddle(side, side, 1)
    whole = pl.BlockSpec(memory_space=pltpu.VMEM)
    out = pl.pallas_call(
        range_kernel,
        in_specs=[whole] * 8,
        out_specs=whole,
        out_shape=jax.ShapeDtypeStruct((side * 2 * pulses, side), jnp.bfloat16),
        cost_estimate=pl.CostEstimate(
            flops=(pulses + 1) * 4 * 2 * (2 * side) ** 2 * side,
            bytes_accessed=pulses * 2 * 2 * length * 2,
            transcendentals=0,
        ),
    )(
        rows,
        range_replica,
        jnp.asarray(fwd),
        jnp.asarray(fwd_t),
        jnp.asarray(inv),
        jnp.asarray(inv_t),
        jnp.asarray(fwd_tw),
        jnp.asarray(inv_tw),
    )
    return out.reshape(side, 2, pulses, side)


def host_block_table4(size, sign):
    index = np.arange(size, dtype=np.int64)
    product = (index[:, None] * index[None, :] % size).astype(np.float32)
    angle = np.float32(sign * 2.0 * math.pi / size) * product
    norm = np.float32(1.0 / math.sqrt(size))
    cos = (np.cos(angle) * norm).astype(ml_dtypes.bfloat16)
    sin = (np.sin(angle) * norm).astype(ml_dtypes.bfloat16)
    return np.stack([np.stack([cos, -sin], axis=1), np.stack([sin, cos], axis=1)])


def pulse_transform(values, first, sign):
    length, width = values.shape[1], values.shape[2]
    second = length // first
    head = jnp.asarray(host_block_table4(first, sign))
    tail = jnp.asarray(host_block_table4(second, sign))
    twist_cos, twist_sin = (jnp.asarray(t) for t in host_twiddle(first, second, sign))
    split = values.reshape(2, first, second, width)
    mid = jnp.einsum("okrn,rnmc->okmc", head, split, preferred_element_type=jnp.float32)
    mid_real, mid_imag = mid[0], mid[1]
    turn_real = mid_real * twist_cos[:, :, None] - mid_imag * twist_sin[:, :, None]
    turn_imag = mid_real * twist_sin[:, :, None] + mid_imag * twist_cos[:, :, None]
    turned = jnp.stack([turn_real, turn_imag]).astype(jnp.bfloat16)
    out = jnp.einsum("ojrm,rkmc->ojkc", tail, turned, preferred_element_type=jnp.float32)
    return out.reshape(2, length, width)


def per_device(raw_echo, range_replica, interp_weight, band_offset, azimuth_rate, tile_owner):
    echo = raw_echo[:, 0]
    length = echo.shape[2]
    compressed = range_compress(echo, range_replica)
    devices = lax.axis_size("wide")
    width = length // devices
    assert compressed.shape[0] == devices and compressed.shape[3] == width
    turned = lax.all_to_all(compressed, "wide", split_axis=0, concat_axis=2, tiled=True)[0]
    doppler = pulse_transform(turned, PUL_DEV, -1).astype(jnp.bfloat16)
    rim = passed_along(doppler[:, :, :HALO], "wide", -1)
    extended = jnp.concatenate([doppler, rim], axis=2)
    pulses = extended.shape[1]
    columns = jnp.arange(width + HALO, dtype=jnp.int32)
    bins = jnp.arange(width, dtype=jnp.int32) + band_offset
    moved_real = jnp.zeros((pulses, width), jnp.float32)
    moved_imag = jnp.zeros((pulses, width), jnp.float32)
    taps = interp_weight.shape[0]
    targets = (bins[None, :] + jnp.arange(taps, dtype=jnp.int32)[:, None]).reshape(taps * width)
    select = (columns[:, None] == targets[None, :]).astype(jnp.bfloat16)
    picked = jnp.einsum("xpc,cn->xpn", extended, select, preferred_element_type=jnp.bfloat16)
    for tap_index in range(taps):
        weight = interp_weight[tap_index][:, None]
        tap_values = picked[:, :, tap_index * width : (tap_index + 1) * width].astype(jnp.float32)
        moved_real = moved_real + weight * tap_values[0]
        moved_imag = moved_imag + weight * tap_values[1]
    half = pulses // 2
    freq = jnp.arange(half + 1, dtype=jnp.int32)
    shifted = ((freq + half) % pulses - half).astype(jnp.float32) / pulses
    phase = math.pi * (shifted * shifted)[:, None] / azimuth_rate[None, :]
    half_cos = jnp.cos(phase)
    half_sin = jnp.sin(phase)
    phase_cos = jnp.concatenate([half_cos, jnp.flip(half_cos[1:half], 0)], axis=0)
    phase_sin = jnp.concatenate([half_sin, jnp.flip(half_sin[1:half], 0)], axis=0)
    focus_real = (moved_real * phase_cos - moved_imag * phase_sin).astype(jnp.bfloat16)
    focus_imag = (moved_real * phase_sin + moved_imag * phase_cos).astype(jnp.bfloat16)
    image = pulse_transform(jnp.stack([focus_real, focus_imag]), PUL_DEV, 1)
    intensity = (image[0] * image[0] + image[1] * image[1]).astype(jnp.bfloat16)
    block_count = tile_owner.shape[1]
    block_rows = pulses // block_count
    blocks = intensity.reshape(block_count, block_rows * width)
    tiles = lax.axis_size("narrow")
    group = lax.axis_index("narrow")
    tile_ids = jnp.arange(tiles, dtype=jnp.int32)
    own_row = lax.dynamic_slice_in_dim(tile_owner, group, 1, 0)[0]
    member = (own_row[None, :] == tile_ids[:, None]).astype(jnp.bfloat16)
    counts = jnp.sum(
        (tile_owner[:, :, None] == tile_ids[None, None, :]).astype(jnp.int32), axis=(0, 1)
    )
    own_count = jnp.sum(jnp.where(tile_ids == group, counts, 0)).astype(jnp.float32)
    partial = jnp.dot(member, blocks, preferred_element_type=jnp.float32)
    partial = partial.reshape(tiles, block_rows, width)
    incoming = lax.all_to_all(partial, "narrow", split_axis=0, concat_axis=0, tiled=True)
    summed = jnp.sum(incoming, axis=0)[None]
    return summed / own_count


def solution(mesh):
    return jax.shard_map(
        per_device,
        mesh=mesh,
        in_specs=(P(None, "narrow", "wide", None), P(), P(), P("wide"), P("wide"), P()),
        out_specs=P("narrow", None, "wide"),
        check_vma=False,
    )
```

```python
import math

import jax
import jax.numpy as jnp
import ml_dtypes
import numpy as np
from jax import lax
from jax.experimental import pallas as pl
from jax.experimental.pallas import tpu as pltpu
from jax.sharding import PartitionSpec as P

RSPLIT = 128
PUL_DEV = 8
CAP = 8
HALO = 31


def passed_along(shard, axis, by):
    devices = lax.axis_size(axis)
    pairs = [(i, i + by) for i in range(devices) if 0 <= i + by < devices]
    return lax.ppermute(shard, axis, pairs)


def host_twiddle(first, second, sign):
    heads = np.arange(first, dtype=np.int64)
    tails = np.arange(second, dtype=np.int64)
    product = (heads[:, None] * tails[None, :] % (first * second)).astype(np.float32)
    angle = np.float32(sign * 2.0 * math.pi / (first * second)) * product
    return np.stack([np.cos(angle), np.sin(angle)]).astype(np.float32)


def host_tables(size, sign):
    index = np.arange(size, dtype=np.int64)
    product = (index[:, None] * index[None, :] % size).astype(np.float32)
    angle = np.float32(sign * 2.0 * math.pi / size) * product
    norm = np.float32(1.0 / math.sqrt(size))
    cos = (np.cos(angle) * norm).astype(ml_dtypes.bfloat16)
    sin = (np.sin(angle) * norm).astype(ml_dtypes.bfloat16)
    table = np.block([[cos, -sin], [sin, cos]])
    return table, np.ascontiguousarray(table.T)


def twist(mid_real, mid_imag, twiddle):
    twist_cos, twist_sin = twiddle[0], twiddle[1]
    turn_real = (mid_real * twist_cos - mid_imag * twist_sin).astype(jnp.bfloat16)
    turn_imag = (mid_real * twist_sin + mid_imag * twist_cos).astype(jnp.bfloat16)
    return turn_real, turn_imag


def forward_transposed(stacked, table, table_t, twiddle):
    half = stacked.shape[0] // 2
    mid = jnp.dot(table, stacked, preferred_element_type=jnp.float32)
    turn_real, turn_imag = twist(mid[:half], mid[half:], twiddle)
    spec = jnp.dot(
        jnp.concatenate([turn_real, turn_imag], axis=1), table_t, preferred_element_type=jnp.float32
    )
    return spec[:, :half], spec[:, half:]


def inverse_from_transposed(real_t, imag_t, table, table_t, twiddle):
    half = real_t.shape[0]
    mid = jnp.dot(
        jnp.concatenate([real_t, imag_t], axis=1), table_t, preferred_element_type=jnp.float32
    )
    turn_real, turn_imag = twist(mid[:, :half], mid[:, half:], twiddle)
    out = jnp.dot(
        table, jnp.concatenate([turn_real, turn_imag], axis=0), preferred_element_type=jnp.float32
    )
    return out[:half], out[half:]


def range_kernel(
    echo_ref, replica_ref, fwd_ref, fwd_t_ref, inv_ref, inv_t_ref, fwd_tw_ref, inv_tw_ref, out_ref
):
    pulses = echo_ref.shape[1] // echo_ref.shape[2]
    side = echo_ref.shape[2]
    fwd, fwd_t = fwd_ref[...], fwd_t_ref[...]
    inv, inv_t = inv_ref[...], inv_t_ref[...]
    fwd_tw, inv_tw = fwd_tw_ref[...], inv_tw_ref[...]
    taps = replica_ref[...].astype(jnp.float32)
    filled = taps.shape[1] // side
    rows = pltpu.einshape("r(nb)->(rn)b", taps, b=side)
    blank = jnp.zeros((side - filled, side), jnp.float32)
    replica = jnp.concatenate([rows[:filled], blank, rows[filled:], blank], axis=0)
    replica = replica.astype(jnp.bfloat16)
    rep_real, rep_imag = forward_transposed(replica, fwd, fwd_t, fwd_tw)
    rep_real = rep_real * 128.0
    rep_imag = rep_imag * 128.0
    blocks = []
    for pulse in range(pulses):
        rows = pl.ds(pulse, side, stride=pulses)
        blocks.append(jnp.concatenate([echo_ref[0, rows, :], echo_ref[1, rows, :]], axis=0))
    mid = jnp.dot(fwd, jnp.concatenate(blocks, axis=1), preferred_element_type=jnp.float32)
    along = lambda x: jnp.concatenate([x] * pulses, axis=1)
    down = lambda x: jnp.concatenate([x] * pulses, axis=0)
    turn_real, turn_imag = twist(mid[:side], mid[side:], (along(fwd_tw[0]), along(fwd_tw[1])))
    by_pulse = lambda x, p: x[:, p * side : (p + 1) * side]
    stacked = jnp.concatenate(
        [
            jnp.concatenate([by_pulse(turn_real, p), by_pulse(turn_imag, p)], axis=1)
            for p in range(pulses)
        ],
        axis=0,
    )
    spec = jnp.dot(stacked, fwd_t, preferred_element_type=jnp.float32)
    spec_real, spec_imag = spec[:, :side], spec[:, side:]
    rep_real, rep_imag = down(rep_real), down(rep_imag)
    match_real = (spec_real * rep_real + spec_imag * rep_imag).astype(jnp.bfloat16)
    match_imag = (spec_imag * rep_real - spec_real * rep_imag).astype(jnp.bfloat16)
    mid = jnp.dot(
        jnp.concatenate([match_real, match_imag], axis=1), inv_t, preferred_element_type=jnp.float32
    )
    turn_real, turn_imag = twist(mid[:, :side], mid[:, side:], (down(inv_tw[0]), down(inv_tw[1])))
    rows_of = lambda x, p: x[p * side : (p + 1) * side]
    stacked = jnp.concatenate(
        [
            jnp.concatenate([rows_of(turn_real, p), rows_of(turn_imag, p)], axis=0)
            for p in range(pulses)
        ],
        axis=1,
    )
    comp = jnp.dot(inv, stacked, preferred_element_type=jnp.float32)
    out_ref[...] = pltpu.einshape("(rd)(pb)->(drp)b", comp, r=2, p=pulses).astype(jnp.bfloat16)


def range_compress(echo, range_replica):
    pulses, length = echo.shape[1], echo.shape[2]
    side = RSPLIT
    assert length == side * side
    assert range_replica.shape[1] % side == 0 and range_replica.shape[1] <= length
    rows = echo.reshape(2, pulses, side, side).transpose(0, 2, 1, 3).reshape(2, side * pulses, side)
    fwd, fwd_t = host_tables(side, -1)
    inv, inv_t = host_tables(side, 1)
    fwd_tw = host_twiddle(side, side, -1)
    inv_tw = host_twiddle(side, side, 1)
    whole = pl.BlockSpec(memory_space=pltpu.VMEM)
    out = pl.pallas_call(
        range_kernel,
        in_specs=[whole] * 8,
        out_specs=whole,
        out_shape=jax.ShapeDtypeStruct((side * 2 * pulses, side), jnp.bfloat16),
        cost_estimate=pl.CostEstimate(
            flops=(pulses + 1) * 4 * 2 * (2 * side) ** 2 * side,
            bytes_accessed=pulses * 2 * 2 * length * 2,
            transcendentals=0,
        ),
    )(
        rows,
        range_replica,
        jnp.asarray(fwd),
        jnp.asarray(fwd_t),
        jnp.asarray(inv),
        jnp.asarray(inv_t),
        jnp.asarray(fwd_tw),
        jnp.asarray(inv_tw),
    )
    return out.reshape(side, 2, pulses, side)


def host_block_table4(size, sign):
    index = np.arange(size, dtype=np.int64)
    product = (index[:, None] * index[None, :] % size).astype(np.float32)
    angle = np.float32(sign * 2.0 * math.pi / size) * product
    norm = np.float32(1.0 / math.sqrt(size))
    cos = (np.cos(angle) * norm).astype(ml_dtypes.bfloat16)
    sin = (np.sin(angle) * norm).astype(ml_dtypes.bfloat16)
    return np.stack([np.stack([cos, -sin], axis=1), np.stack([sin, cos], axis=1)])


def pulse_transform(values, first, sign):
    length, width = values.shape[1], values.shape[2]
    second = length // first
    head = jnp.asarray(host_block_table4(first, sign))
    tail = jnp.asarray(host_block_table4(second, sign))
    twist_cos, twist_sin = (jnp.asarray(t) for t in host_twiddle(first, second, sign))
    split = values.reshape(2, first, second, width)
    mid = jnp.einsum("okrn,rnmc->okmc", head, split, preferred_element_type=jnp.float32)
    mid_real, mid_imag = mid[0], mid[1]
    turn_real = mid_real * twist_cos[:, :, None] - mid_imag * twist_sin[:, :, None]
    turn_imag = mid_real * twist_sin[:, :, None] + mid_imag * twist_cos[:, :, None]
    turned = jnp.stack([turn_real, turn_imag]).astype(jnp.bfloat16)
    out = jnp.einsum("ojrm,rkmc->ojkc", tail, turned, preferred_element_type=jnp.float32)
    return out.reshape(2, length, width)


def per_device(raw_echo, range_replica, interp_weight, band_offset, azimuth_rate, tile_owner):
    echo = raw_echo[:, 0]
    length = echo.shape[2]
    compressed = range_compress(echo, range_replica)
    devices = lax.axis_size("wide")
    width = length // devices
    assert compressed.shape[0] == devices and compressed.shape[3] == width
    turned = lax.all_to_all(compressed, "wide", split_axis=0, concat_axis=2, tiled=True)[0]
    doppler = pulse_transform(turned, PUL_DEV, -1).astype(jnp.bfloat16)
    rim = passed_along(doppler[:, :, :HALO], "wide", -1)
    extended = jnp.concatenate([doppler, rim], axis=2)
    pulses = extended.shape[1]
    columns = jnp.arange(width + HALO, dtype=jnp.int32)
    bins = jnp.arange(width, dtype=jnp.int32) + band_offset
    moved_real = jnp.zeros((pulses, width), jnp.float32)
    moved_imag = jnp.zeros((pulses, width), jnp.float32)
    taps = interp_weight.shape[0]
    targets = (bins[None, :] + jnp.arange(taps, dtype=jnp.int32)[:, None]).reshape(taps * width)
    select = (columns[:, None] == targets[None, :]).astype(jnp.bfloat16)
    picked = jnp.einsum("xpc,cn->xpn", extended, select, preferred_element_type=jnp.bfloat16)
    for tap_index in range(taps):
        weight = interp_weight[tap_index][:, None]
        tap_values = picked[:, :, tap_index * width : (tap_index + 1) * width].astype(jnp.float32)
        moved_real = moved_real + weight * tap_values[0]
        moved_imag = moved_imag + weight * tap_values[1]
    half = pulses // 2
    freq = jnp.arange(half + 1, dtype=jnp.int32)
    shifted = ((freq + half) % pulses - half).astype(jnp.float32) / pulses
    phase = math.pi * (shifted * shifted)[:, None] / azimuth_rate[None, :]
    half_cos = jnp.cos(phase)
    half_sin = jnp.sin(phase)
    phase_cos = jnp.concatenate([half_cos, jnp.flip(half_cos[1:half], 0)], axis=0)
    phase_sin = jnp.concatenate([half_sin, jnp.flip(half_sin[1:half], 0)], axis=0)
    focus_real = (moved_real * phase_cos - moved_imag * phase_sin).astype(jnp.bfloat16)
    focus_imag = (moved_real * phase_sin + moved_imag * phase_cos).astype(jnp.bfloat16)
    image = pulse_transform(jnp.stack([focus_real, focus_imag]), PUL_DEV, 1)
    intensity = (image[0] * image[0] + image[1] * image[1]).astype(jnp.bfloat16)
    block_count = tile_owner.shape[1]
    block_rows = pulses // block_count
    second = pulses // PUL_DEV
    per_block = block_rows // PUL_DEV
    blocks = intensity.reshape(second, PUL_DEV, width).transpose(1, 0, 2)
    blocks = blocks.reshape(PUL_DEV, block_count, per_block, width)
    tiles = lax.axis_size("narrow")
    group = lax.axis_index("narrow")
    tile_ids = jnp.arange(tiles, dtype=jnp.int32)
    own_row = lax.dynamic_slice_in_dim(tile_owner, group, 1, 0)[0]
    member = (own_row[None, :] == tile_ids[:, None]).astype(jnp.bfloat16)
    counts = jnp.sum(
        (tile_owner[:, :, None] == tile_ids[None, None, :]).astype(jnp.int32), axis=(0, 1)
    )
    own_count = jnp.sum(jnp.where(tile_ids == group, counts, 0)).astype(jnp.float32)
    partial = jnp.einsum("tb,kbjc->tkjc", member, blocks, preferred_element_type=jnp.float32)
    incoming = lax.all_to_all(partial, "narrow", split_axis=0, concat_axis=0, tiled=True)
    summed = jnp.sum(incoming, axis=0).transpose(1, 0, 2).reshape(1, block_rows, width)
    return summed / own_count


def solution(mesh):
    return jax.shard_map(
        per_device,
        mesh=mesh,
        in_specs=(P(None, "narrow", "wide", None), P(), P(), P("wide"), P("wide"), P()),
        out_specs=P("narrow", None, "wide"),
        check_vma=False,
    )
```

```python
import math

import jax
import jax.numpy as jnp
import ml_dtypes
import numpy as np
from jax import lax
from jax.experimental import pallas as pl
from jax.experimental.pallas import tpu as pltpu
from jax.sharding import PartitionSpec as P

RSPLIT = 128
PUL_DEV = 8
CAP = 8
HALO = 31


def passed_along(shard, axis, by):
    devices = lax.axis_size(axis)
    pairs = [(i, i + by) for i in range(devices) if 0 <= i + by < devices]
    return lax.ppermute(shard, axis, pairs)


def host_twiddle(first, second, sign):
    heads = np.arange(first, dtype=np.int64)
    tails = np.arange(second, dtype=np.int64)
    product = (heads[:, None] * tails[None, :] % (first * second)).astype(np.float32)
    angle = np.float32(sign * 2.0 * math.pi / (first * second)) * product
    return np.stack([np.cos(angle), np.sin(angle)]).astype(np.float32)


def host_tables(size, sign):
    index = np.arange(size, dtype=np.int64)
    product = (index[:, None] * index[None, :] % size).astype(np.float32)
    angle = np.float32(sign * 2.0 * math.pi / size) * product
    norm = np.float32(1.0 / math.sqrt(size))
    cos = (np.cos(angle) * norm).astype(ml_dtypes.bfloat16)
    sin = (np.sin(angle) * norm).astype(ml_dtypes.bfloat16)
    table = np.block([[cos, -sin], [sin, cos]])
    return table, np.ascontiguousarray(table.T)


def twist(mid_real, mid_imag, twiddle):
    twist_cos, twist_sin = twiddle[0], twiddle[1]
    turn_real = (mid_real * twist_cos - mid_imag * twist_sin).astype(jnp.bfloat16)
    turn_imag = (mid_real * twist_sin + mid_imag * twist_cos).astype(jnp.bfloat16)
    return turn_real, turn_imag


def forward_transposed(stacked, table, table_t, twiddle):
    half = stacked.shape[0] // 2
    mid = jnp.dot(table, stacked, preferred_element_type=jnp.float32)
    turn_real, turn_imag = twist(mid[:half], mid[half:], twiddle)
    spec = jnp.dot(
        jnp.concatenate([turn_real, turn_imag], axis=1), table_t, preferred_element_type=jnp.float32
    )
    return spec[:, :half], spec[:, half:]


def inverse_from_transposed(real_t, imag_t, table, table_t, twiddle):
    half = real_t.shape[0]
    mid = jnp.dot(
        jnp.concatenate([real_t, imag_t], axis=1), table_t, preferred_element_type=jnp.float32
    )
    turn_real, turn_imag = twist(mid[:, :half], mid[:, half:], twiddle)
    out = jnp.dot(
        table, jnp.concatenate([turn_real, turn_imag], axis=0), preferred_element_type=jnp.float32
    )
    return out[:half], out[half:]


def range_kernel(
    echo_ref, replica_ref, fwd_ref, fwd_t_ref, inv_ref, inv_t_ref, fwd_tw_ref, inv_tw_ref, out_ref
):
    pulses = echo_ref.shape[1] // echo_ref.shape[2]
    side = echo_ref.shape[2]
    fwd, fwd_t = fwd_ref[...], fwd_t_ref[...]
    inv, inv_t = inv_ref[...], inv_t_ref[...]
    fwd_tw, inv_tw = fwd_tw_ref[...], inv_tw_ref[...]
    taps = replica_ref[...].astype(jnp.float32)
    filled = taps.shape[1] // side
    blank = jnp.zeros((side - filled, side), jnp.float32)
    pieces = []
    for part in range(2):
        pieces += [taps[part : part + 1, n * side : (n + 1) * side] for n in range(filled)]
        pieces.append(blank)
    replica = jnp.concatenate(pieces, axis=0).astype(jnp.bfloat16)
    rep_real, rep_imag = forward_transposed(replica, fwd, fwd_t, fwd_tw)
    rep_real = rep_real * 128.0
    rep_imag = rep_imag * 128.0
    blocks = []
    for pulse in range(pulses):
        rows = pl.ds(pulse, side, stride=pulses)
        blocks.append(jnp.concatenate([echo_ref[0, rows, :], echo_ref[1, rows, :]], axis=0))
    mid = jnp.dot(fwd, jnp.concatenate(blocks, axis=1), preferred_element_type=jnp.float32)
    along = lambda x: jnp.concatenate([x] * pulses, axis=1)
    down = lambda x: jnp.concatenate([x] * pulses, axis=0)
    turn_real, turn_imag = twist(mid[:side], mid[side:], (along(fwd_tw[0]), along(fwd_tw[1])))
    by_pulse = lambda x, p: x[:, p * side : (p + 1) * side]
    stacked = jnp.concatenate(
        [
            jnp.concatenate([by_pulse(turn_real, p), by_pulse(turn_imag, p)], axis=1)
            for p in range(pulses)
        ],
        axis=0,
    )
    spec = jnp.dot(stacked, fwd_t, preferred_element_type=jnp.float32)
    spec_real, spec_imag = spec[:, :side], spec[:, side:]
    rep_real, rep_imag = down(rep_real), down(rep_imag)
    match_real = (spec_real * rep_real + spec_imag * rep_imag).astype(jnp.bfloat16)
    match_imag = (spec_imag * rep_real - spec_real * rep_imag).astype(jnp.bfloat16)
    mid = jnp.dot(
        jnp.concatenate([match_real, match_imag], axis=1), inv_t, preferred_element_type=jnp.float32
    )
    turn_real, turn_imag = twist(mid[:, :side], mid[:, side:], (down(inv_tw[0]), down(inv_tw[1])))
    rows_of = lambda x, p: x[p * side : (p + 1) * side]
    stacked = jnp.concatenate(
        [
            jnp.concatenate([rows_of(turn_real, p), rows_of(turn_imag, p)], axis=0)
            for p in range(pulses)
        ],
        axis=1,
    )
    comp = jnp.dot(inv, stacked, preferred_element_type=jnp.float32)
    out_ref[...] = pltpu.einshape("(rd)(pb)->(drp)b", comp, r=2, p=pulses).astype(jnp.bfloat16)


def range_compress(echo, range_replica):
    pulses, length = echo.shape[1], echo.shape[2]
    side = RSPLIT
    assert length == side * side
    assert range_replica.shape[1] % side == 0 and range_replica.shape[1] <= length
    rows = echo.reshape(2, pulses, side, side).transpose(0, 2, 1, 3).reshape(2, side * pulses, side)
    fwd, fwd_t = host_tables(side, -1)
    inv, inv_t = host_tables(side, 1)
    fwd_tw = host_twiddle(side, side, -1)
    inv_tw = host_twiddle(side, side, 1)
    whole = pl.BlockSpec(memory_space=pltpu.VMEM)
    out = pl.pallas_call(
        range_kernel,
        in_specs=[whole] * 8,
        out_specs=whole,
        out_shape=jax.ShapeDtypeStruct((side * 2 * pulses, side), jnp.bfloat16),
        cost_estimate=pl.CostEstimate(
            flops=(pulses + 1) * 4 * 2 * (2 * side) ** 2 * side,
            bytes_accessed=pulses * 2 * 2 * length * 2,
            transcendentals=0,
        ),
    )(
        rows,
        range_replica,
        jnp.asarray(fwd),
        jnp.asarray(fwd_t),
        jnp.asarray(inv),
        jnp.asarray(inv_t),
        jnp.asarray(fwd_tw),
        jnp.asarray(inv_tw),
    )
    return out.reshape(side, 2, pulses, side)


def host_block_table4(size, sign):
    index = np.arange(size, dtype=np.int64)
    product = (index[:, None] * index[None, :] % size).astype(np.float32)
    angle = np.float32(sign * 2.0 * math.pi / size) * product
    norm = np.float32(1.0 / math.sqrt(size))
    cos = (np.cos(angle) * norm).astype(ml_dtypes.bfloat16)
    sin = (np.sin(angle) * norm).astype(ml_dtypes.bfloat16)
    return np.stack([np.stack([cos, -sin], axis=1), np.stack([sin, cos], axis=1)])


def pulse_transform(values, first, sign):
    length, width = values.shape[1], values.shape[2]
    second = length // first
    head = jnp.asarray(host_block_table4(first, sign))
    tail = jnp.asarray(host_block_table4(second, sign))
    twist_cos, twist_sin = (jnp.asarray(t) for t in host_twiddle(first, second, sign))
    split = values.reshape(2, first, second, width)
    mid = jnp.einsum("okrn,rnmc->okmc", head, split, preferred_element_type=jnp.float32)
    mid_real, mid_imag = mid[0], mid[1]
    turn_real = mid_real * twist_cos[:, :, None] - mid_imag * twist_sin[:, :, None]
    turn_imag = mid_real * twist_sin[:, :, None] + mid_imag * twist_cos[:, :, None]
    turned = jnp.stack([turn_real, turn_imag]).astype(jnp.bfloat16)
    out = jnp.einsum("ojrm,rkmc->ojkc", tail, turned, preferred_element_type=jnp.float32)
    return out.reshape(2, length, width)


def per_device(raw_echo, range_replica, interp_weight, band_offset, azimuth_rate, tile_owner):
    echo = raw_echo[:, 0]
    length = echo.shape[2]
    compressed = range_compress(echo, range_replica)
    devices = lax.axis_size("wide")
    width = length // devices
    assert compressed.shape[0] == devices and compressed.shape[3] == width
    turned = lax.all_to_all(compressed, "wide", split_axis=0, concat_axis=2, tiled=True)[0]
    doppler = pulse_transform(turned, PUL_DEV, -1).astype(jnp.bfloat16)
    rim = passed_along(doppler[:, :, :HALO], "wide", -1)
    extended = jnp.concatenate([doppler, rim], axis=2)
    pulses = extended.shape[1]
    columns = jnp.arange(width + HALO, dtype=jnp.int32)
    bins = jnp.arange(width, dtype=jnp.int32) + band_offset
    moved_real = jnp.zeros((pulses, width), jnp.float32)
    moved_imag = jnp.zeros((pulses, width), jnp.float32)
    taps = interp_weight.shape[0]
    targets = (bins[None, :] + jnp.arange(taps, dtype=jnp.int32)[:, None]).reshape(taps * width)
    select = (columns[:, None] == targets[None, :]).astype(jnp.bfloat16)
    picked = jnp.einsum("xpc,cn->xpn", extended, select, preferred_element_type=jnp.bfloat16)
    for tap_index in range(taps):
        weight = interp_weight[tap_index][:, None]
        tap_values = picked[:, :, tap_index * width : (tap_index + 1) * width].astype(jnp.float32)
        moved_real = moved_real + weight * tap_values[0]
        moved_imag = moved_imag + weight * tap_values[1]
    half = pulses // 2
    freq = jnp.arange(half + 1, dtype=jnp.int32)
    shifted = ((freq + half) % pulses - half).astype(jnp.float32) / pulses
    phase = math.pi * (shifted * shifted)[:, None] / azimuth_rate[None, :]
    half_cos = jnp.cos(phase)
    half_sin = jnp.sin(phase)
    phase_cos = jnp.concatenate([half_cos, jnp.flip(half_cos[1:half], 0)], axis=0)
    phase_sin = jnp.concatenate([half_sin, jnp.flip(half_sin[1:half], 0)], axis=0)
    focus_real = (moved_real * phase_cos - moved_imag * phase_sin).astype(jnp.bfloat16)
    focus_imag = (moved_real * phase_sin + moved_imag * phase_cos).astype(jnp.bfloat16)
    image = pulse_transform(jnp.stack([focus_real, focus_imag]), PUL_DEV, 1)
    intensity = (image[0] * image[0] + image[1] * image[1]).astype(jnp.bfloat16)
    block_count = tile_owner.shape[1]
    block_rows = pulses // block_count
    blocks = intensity.reshape(block_count, block_rows * width)
    tiles = lax.axis_size("narrow")
    group = lax.axis_index("narrow")
    tile_ids = jnp.arange(tiles, dtype=jnp.int32)
    own_row = lax.dynamic_slice_in_dim(tile_owner, group, 1, 0)[0]
    member = (own_row[None, :] == tile_ids[:, None]).astype(jnp.bfloat16)
    counts = jnp.sum(
        (tile_owner[:, :, None] == tile_ids[None, None, :]).astype(jnp.int32), axis=(0, 1)
    )
    own_count = jnp.sum(jnp.where(tile_ids == group, counts, 0)).astype(jnp.float32)
    spaced = jnp.stack([member, jnp.zeros_like(member)], axis=1).reshape(2 * tiles, block_count)
    partial = jnp.dot(spaced, blocks, preferred_element_type=jnp.float32)
    incoming = lax.all_to_all(partial, "narrow", split_axis=0, concat_axis=0, tiled=True)
    summed = jnp.sum(incoming, axis=0).reshape(1, block_rows, width)
    return summed / own_count


def solution(mesh):
    return jax.shard_map(
        per_device,
        mesh=mesh,
        in_specs=(P(None, "narrow", "wide", None), P(), P(), P("wide"), P("wide"), P()),
        out_specs=P("narrow", None, "wide"),
        check_vma=False,
    )
```

```python
import math

import jax
import jax.numpy as jnp
import ml_dtypes
import numpy as np
from jax import lax
from jax.experimental import pallas as pl
from jax.experimental.pallas import tpu as pltpu
from jax.sharding import PartitionSpec as P

RSPLIT = 128
PUL_DEV = 8
CAP = 8
HALO = 31
WIDE = ("y", "z", "c")


def passed_along(shard, axis, by):
    devices = lax.axis_size(axis)
    pairs = [(i, i + by) for i in range(devices) if 0 <= i + by < devices]
    return lax.ppermute(shard, axis, pairs)


def host_twiddle(first, second, sign):
    heads = np.arange(first, dtype=np.int64)
    tails = np.arange(second, dtype=np.int64)
    product = (heads[:, None] * tails[None, :] % (first * second)).astype(np.float32)
    angle = np.float32(sign * 2.0 * math.pi / (first * second)) * product
    return np.stack([np.cos(angle), np.sin(angle)]).astype(np.float32)


def host_tables(size, sign):
    index = np.arange(size, dtype=np.int64)
    product = (index[:, None] * index[None, :] % size).astype(np.float32)
    angle = np.float32(sign * 2.0 * math.pi / size) * product
    norm = np.float32(1.0 / math.sqrt(size))
    cos = (np.cos(angle) * norm).astype(ml_dtypes.bfloat16)
    sin = (np.sin(angle) * norm).astype(ml_dtypes.bfloat16)
    table = np.block([[cos, -sin], [sin, cos]])
    return table, np.ascontiguousarray(table.T)


def twist(mid_real, mid_imag, twiddle):
    twist_cos, twist_sin = twiddle[0], twiddle[1]
    turn_real = (mid_real * twist_cos - mid_imag * twist_sin).astype(jnp.bfloat16)
    turn_imag = (mid_real * twist_sin + mid_imag * twist_cos).astype(jnp.bfloat16)
    return turn_real, turn_imag


def forward_transposed(stacked, table, table_t, twiddle):
    half = stacked.shape[0] // 2
    mid = jnp.dot(table, stacked, preferred_element_type=jnp.float32)
    turn_real, turn_imag = twist(mid[:half], mid[half:], twiddle)
    spec = jnp.dot(
        jnp.concatenate([turn_real, turn_imag], axis=1), table_t, preferred_element_type=jnp.float32
    )
    return spec[:, :half], spec[:, half:]


def inverse_from_transposed(real_t, imag_t, table, table_t, twiddle):
    half = real_t.shape[0]
    mid = jnp.dot(
        jnp.concatenate([real_t, imag_t], axis=1), table_t, preferred_element_type=jnp.float32
    )
    turn_real, turn_imag = twist(mid[:, :half], mid[:, half:], twiddle)
    out = jnp.dot(
        table, jnp.concatenate([turn_real, turn_imag], axis=0), preferred_element_type=jnp.float32
    )
    return out[:half], out[half:]


def range_kernel(
    echo_ref, replica_ref, fwd_ref, fwd_t_ref, inv_ref, inv_t_ref, fwd_tw_ref, inv_tw_ref, out_ref
):
    pulses = echo_ref.shape[1] // echo_ref.shape[2]
    side = echo_ref.shape[2]
    fwd, fwd_t = fwd_ref[...], fwd_t_ref[...]
    inv, inv_t = inv_ref[...], inv_t_ref[...]
    fwd_tw, inv_tw = fwd_tw_ref[...], inv_tw_ref[...]
    taps = replica_ref[...].astype(jnp.float32)
    filled = taps.shape[1] // side
    blank = jnp.zeros((side - filled, side), jnp.float32)
    pieces = []
    for part in range(2):
        pieces += [taps[part : part + 1, n * side : (n + 1) * side] for n in range(filled)]
        pieces.append(blank)
    replica = jnp.concatenate(pieces, axis=0).astype(jnp.bfloat16)
    rep_real, rep_imag = forward_transposed(replica, fwd, fwd_t, fwd_tw)
    rep_real = rep_real * 128.0
    rep_imag = rep_imag * 128.0
    blocks = []
    for pulse in range(pulses):
        rows = pl.ds(pulse, side, stride=pulses)
        blocks.append(jnp.concatenate([echo_ref[0, rows, :], echo_ref[1, rows, :]], axis=0))
    mid = jnp.dot(fwd, jnp.concatenate(blocks, axis=1), preferred_element_type=jnp.float32)
    along = lambda x: jnp.concatenate([x] * pulses, axis=1)
    down = lambda x: jnp.concatenate([x] * pulses, axis=0)
    turn_real, turn_imag = twist(mid[:side], mid[side:], (along(fwd_tw[0]), along(fwd_tw[1])))
    by_pulse = lambda x, p: x[:, p * side : (p + 1) * side]
    stacked = jnp.concatenate(
        [
            jnp.concatenate([by_pulse(turn_real, p), by_pulse(turn_imag, p)], axis=1)
            for p in range(pulses)
        ],
        axis=0,
    )
    spec = jnp.dot(stacked, fwd_t, preferred_element_type=jnp.float32)
    spec_real, spec_imag = spec[:, :side], spec[:, side:]
    rep_real, rep_imag = down(rep_real), down(rep_imag)
    match_real = (spec_real * rep_real + spec_imag * rep_imag).astype(jnp.bfloat16)
    match_imag = (spec_imag * rep_real - spec_real * rep_imag).astype(jnp.bfloat16)
    mid = jnp.dot(
        jnp.concatenate([match_real, match_imag], axis=1), inv_t, preferred_element_type=jnp.float32
    )
    turn_real, turn_imag = twist(mid[:, :side], mid[:, side:], (down(inv_tw[0]), down(inv_tw[1])))
    rows_of = lambda x, p: x[p * side : (p + 1) * side]
    stacked = jnp.concatenate(
        [
            jnp.concatenate([rows_of(turn_real, p), rows_of(turn_imag, p)], axis=0)
            for p in range(pulses)
        ],
        axis=1,
    )
    comp = jnp.dot(inv, stacked, preferred_element_type=jnp.float32)
    out_ref[...] = pltpu.einshape("(rd)(pb)->(drp)b", comp, r=2, p=pulses).astype(jnp.bfloat16)


def range_compress(echo, range_replica):
    pulses, length = echo.shape[1], echo.shape[2]
    side = RSPLIT
    assert length == side * side
    assert range_replica.shape[1] % side == 0 and range_replica.shape[1] <= length
    rows = echo.reshape(2, pulses, side, side).transpose(0, 2, 1, 3).reshape(2, side * pulses, side)
    fwd, fwd_t = host_tables(side, -1)
    inv, inv_t = host_tables(side, 1)
    fwd_tw = host_twiddle(side, side, -1)
    inv_tw = host_twiddle(side, side, 1)
    whole = pl.BlockSpec(memory_space=pltpu.VMEM)
    out = pl.pallas_call(
        range_kernel,
        in_specs=[whole] * 8,
        out_specs=whole,
        out_shape=jax.ShapeDtypeStruct((side * 2 * pulses, side), jnp.bfloat16),
        cost_estimate=pl.CostEstimate(
            flops=(pulses + 1) * 4 * 2 * (2 * side) ** 2 * side,
            bytes_accessed=pulses * 2 * 2 * length * 2,
            transcendentals=0,
        ),
    )(
        rows,
        range_replica,
        jnp.asarray(fwd),
        jnp.asarray(fwd_t),
        jnp.asarray(inv),
        jnp.asarray(inv_t),
        jnp.asarray(fwd_tw),
        jnp.asarray(inv_tw),
    )
    return out.reshape(side, 2, pulses, side)


def host_block_table4(size, sign):
    index = np.arange(size, dtype=np.int64)
    product = (index[:, None] * index[None, :] % size).astype(np.float32)
    angle = np.float32(sign * 2.0 * math.pi / size) * product
    norm = np.float32(1.0 / math.sqrt(size))
    cos = (np.cos(angle) * norm).astype(ml_dtypes.bfloat16)
    sin = (np.sin(angle) * norm).astype(ml_dtypes.bfloat16)
    return np.stack([np.stack([cos, -sin], axis=1), np.stack([sin, cos], axis=1)])


def pulse_transform(values, first, sign):
    length, width = values.shape[1], values.shape[2]
    second = length // first
    head = jnp.asarray(host_block_table4(first, sign))
    tail = jnp.asarray(host_block_table4(second, sign))
    twist_cos, twist_sin = (jnp.asarray(t) for t in host_twiddle(first, second, sign))
    split = values.reshape(2, first, second, width)
    mid = jnp.einsum("okrn,rnmc->okmc", head, split, preferred_element_type=jnp.float32)
    mid_real, mid_imag = mid[0], mid[1]
    turn_real = mid_real * twist_cos[:, :, None] - mid_imag * twist_sin[:, :, None]
    turn_imag = mid_real * twist_sin[:, :, None] + mid_imag * twist_cos[:, :, None]
    turned = jnp.stack([turn_real, turn_imag]).astype(jnp.bfloat16)
    out = jnp.einsum("ojrm,rkmc->ojkc", tail, turned, preferred_element_type=jnp.float32)
    return out.reshape(2, length, width)


def per_device(raw_echo, range_replica, interp_weight, band_offset, azimuth_rate, tile_owner):
    echo = raw_echo[:, 0]
    length = echo.shape[2]
    compressed = range_compress(echo, range_replica)
    devices = lax.axis_size(WIDE)
    width = length // devices
    assert compressed.shape[0] == devices and compressed.shape[3] == width
    ys, zs, cores = lax.axis_size("y"), lax.axis_size("z"), lax.axis_size("c")
    chunked = compressed.reshape(ys, zs, cores, 2, compressed.shape[2], width).transpose(2, 0, 1, 3, 4, 5)
    turned = lax.all_to_all(
        chunked.reshape(compressed.shape), ("c", "y", "z"), split_axis=0, concat_axis=2, tiled=True
    )[0]
    turned = turned.reshape(2, cores, ys, zs, -1, width).transpose(0, 2, 3, 1, 4, 5)
    turned = turned.reshape(2, -1, width)
    doppler = pulse_transform(turned, PUL_DEV, -1).astype(jnp.bfloat16)
    rim = passed_along(doppler[:, :, :HALO], WIDE, -1)
    extended = jnp.concatenate([doppler, rim], axis=2)
    pulses = extended.shape[1]
    columns = jnp.arange(width + HALO, dtype=jnp.int32)
    bins = jnp.arange(width, dtype=jnp.int32) + band_offset
    moved_real = jnp.zeros((pulses, width), jnp.float32)
    moved_imag = jnp.zeros((pulses, width), jnp.float32)
    taps = interp_weight.shape[0]
    targets = (bins[None, :] + jnp.arange(taps, dtype=jnp.int32)[:, None]).reshape(taps * width)
    select = (columns[:, None] == targets[None, :]).astype(jnp.bfloat16)
    picked = jnp.einsum("xpc,cn->xpn", extended, select, preferred_element_type=jnp.bfloat16)
    for tap_index in range(taps):
        weight = interp_weight[tap_index][:, None]
        tap_values = picked[:, :, tap_index * width : (tap_index + 1) * width].astype(jnp.float32)
        moved_real = moved_real + weight * tap_values[0]
        moved_imag = moved_imag + weight * tap_values[1]
    half = pulses // 2
    freq = jnp.arange(half + 1, dtype=jnp.int32)
    shifted = ((freq + half) % pulses - half).astype(jnp.float32) / pulses
    phase = math.pi * (shifted * shifted)[:, None] / azimuth_rate[None, :]
    half_cos = jnp.cos(phase)
    half_sin = jnp.sin(phase)
    phase_cos = jnp.concatenate([half_cos, jnp.flip(half_cos[1:half], 0)], axis=0)
    phase_sin = jnp.concatenate([half_sin, jnp.flip(half_sin[1:half], 0)], axis=0)
    focus_real = (moved_real * phase_cos - moved_imag * phase_sin).astype(jnp.bfloat16)
    focus_imag = (moved_real * phase_sin + moved_imag * phase_cos).astype(jnp.bfloat16)
    image = pulse_transform(jnp.stack([focus_real, focus_imag]), PUL_DEV, 1)
    intensity = (image[0] * image[0] + image[1] * image[1]).astype(jnp.bfloat16)
    block_count = tile_owner.shape[1]
    block_rows = pulses // block_count
    second = pulses // PUL_DEV
    per_block = block_rows // PUL_DEV
    blocks = intensity.reshape(second, PUL_DEV, width).transpose(1, 0, 2)
    blocks = blocks.reshape(PUL_DEV, block_count, per_block, width)
    tiles = lax.axis_size("narrow")
    group = lax.axis_index("narrow")
    tile_ids = jnp.arange(tiles, dtype=jnp.int32)
    own_row = lax.dynamic_slice_in_dim(tile_owner, group, 1, 0)[0]
    member = (own_row[None, :] == tile_ids[:, None]).astype(jnp.bfloat16)
    counts = jnp.sum(
        (tile_owner[:, :, None] == tile_ids[None, None, :]).astype(jnp.int32), axis=(0, 1)
    )
    own_count = jnp.sum(jnp.where(tile_ids == group, counts, 0)).astype(jnp.float32)
    partial = jnp.einsum("tb,kbjc->tkjc", member, blocks, preferred_element_type=jnp.float32)
    incoming = lax.all_to_all(partial, "narrow", split_axis=0, concat_axis=0, tiled=True)
    summed = jnp.sum(incoming, axis=0).transpose(1, 0, 2).reshape(1, block_rows, width)
    return summed / own_count


def solution(mesh):
    wide, narrow = mesh.devices.shape
    parts = mesh.devices.reshape(4, wide // 8, 2, narrow)
    split = jax.sharding.Mesh(parts, ("y", "z", "c", "narrow"))
    return jax.shard_map(
        per_device,
        mesh=split,
        in_specs=(P(None, "narrow", WIDE, None), P(), P(), P(WIDE), P(WIDE), P()),
        out_specs=P("narrow", None, WIDE),
        check_vma=False,
    )
```

```python
import math

import jax
import jax.numpy as jnp
import ml_dtypes
import numpy as np
from jax import lax
from jax.experimental import pallas as pl
from jax.experimental.pallas import tpu as pltpu
from jax.sharding import PartitionSpec as P

RSPLIT = 128
PUL_DEV = 8
CAP = 8
HALO = 31


def passed_along(shard, axis, by):
    devices = lax.axis_size(axis)
    pairs = [(i, i + by) for i in range(devices) if 0 <= i + by < devices]
    return lax.ppermute(shard, axis, pairs)


def host_twiddle(first, second, sign):
    heads = np.arange(first, dtype=np.int64)
    tails = np.arange(second, dtype=np.int64)
    product = (heads[:, None] * tails[None, :] % (first * second)).astype(np.float32)
    angle = np.float32(sign * 2.0 * math.pi / (first * second)) * product
    return np.stack([np.cos(angle), np.sin(angle)]).astype(np.float32)


def host_tables(size, sign):
    index = np.arange(size, dtype=np.int64)
    product = (index[:, None] * index[None, :] % size).astype(np.float32)
    angle = np.float32(sign * 2.0 * math.pi / size) * product
    norm = np.float32(1.0 / math.sqrt(size))
    cos = (np.cos(angle) * norm).astype(ml_dtypes.bfloat16)
    sin = (np.sin(angle) * norm).astype(ml_dtypes.bfloat16)
    table = np.block([[cos, -sin], [sin, cos]])
    return table, np.ascontiguousarray(table.T)


def twist(mid_real, mid_imag, twiddle):
    twist_cos, twist_sin = twiddle[0], twiddle[1]
    turn_real = (mid_real * twist_cos - mid_imag * twist_sin).astype(jnp.bfloat16)
    turn_imag = (mid_real * twist_sin + mid_imag * twist_cos).astype(jnp.bfloat16)
    return turn_real, turn_imag


def forward_transposed(stacked, table, table_t, twiddle):
    half = stacked.shape[0] // 2
    mid = jnp.dot(table, stacked, preferred_element_type=jnp.float32)
    turn_real, turn_imag = twist(mid[:half], mid[half:], twiddle)
    spec = jnp.dot(
        jnp.concatenate([turn_real, turn_imag], axis=1), table_t, preferred_element_type=jnp.float32
    )
    return spec[:, :half], spec[:, half:]


def inverse_from_transposed(real_t, imag_t, table, table_t, twiddle):
    half = real_t.shape[0]
    mid = jnp.dot(
        jnp.concatenate([real_t, imag_t], axis=1), table_t, preferred_element_type=jnp.float32
    )
    turn_real, turn_imag = twist(mid[:, :half], mid[:, half:], twiddle)
    out = jnp.dot(
        table, jnp.concatenate([turn_real, turn_imag], axis=0), preferred_element_type=jnp.float32
    )
    return out[:half], out[half:]


def range_kernel(
    echo_ref, replica_ref, fwd_ref, fwd_t_ref, inv_ref, inv_t_ref, fwd_tw_ref, inv_tw_ref, out_ref
):
    pulses = echo_ref.shape[1] // echo_ref.shape[2]
    side = echo_ref.shape[2]
    fwd, fwd_t = fwd_ref[...], fwd_t_ref[...]
    inv, inv_t = inv_ref[...], inv_t_ref[...]
    fwd_tw, inv_tw = fwd_tw_ref[...], inv_tw_ref[...]
    taps = replica_ref[...].astype(jnp.float32)
    filled = taps.shape[1] // side
    rows = pltpu.einshape("r(nb)->(rn)b", taps, b=side)
    blank = jnp.zeros((side - filled, side), jnp.float32)
    replica = jnp.concatenate([rows[:filled], blank, rows[filled:], blank], axis=0)
    replica = replica.astype(jnp.bfloat16)
    rep_real, rep_imag = forward_transposed(replica, fwd, fwd_t, fwd_tw)
    rep_real = rep_real * 128.0
    rep_imag = rep_imag * 128.0
    blocks = []
    for pulse in range(pulses):
        rows = pl.ds(pulse, side, stride=pulses)
        blocks.append(jnp.concatenate([echo_ref[0, rows, :], echo_ref[1, rows, :]], axis=0))
    mid = jnp.dot(fwd, jnp.concatenate(blocks, axis=1), preferred_element_type=jnp.float32)
    along = lambda x: jnp.concatenate([x] * pulses, axis=1)
    down = lambda x: jnp.concatenate([x] * pulses, axis=0)
    turn_real, turn_imag = twist(mid[:side], mid[side:], (along(fwd_tw[0]), along(fwd_tw[1])))
    by_pulse = lambda x, p: x[:, p * side : (p + 1) * side]
    stacked = jnp.concatenate(
        [
            jnp.concatenate([by_pulse(turn_real, p), by_pulse(turn_imag, p)], axis=1)
            for p in range(pulses)
        ],
        axis=0,
    )
    spec = jnp.dot(stacked, fwd_t, preferred_element_type=jnp.float32)
    spec_real, spec_imag = spec[:, :side], spec[:, side:]
    rep_real, rep_imag = down(rep_real), down(rep_imag)
    match_real = (spec_real * rep_real + spec_imag * rep_imag).astype(jnp.bfloat16)
    match_imag = (spec_imag * rep_real - spec_real * rep_imag).astype(jnp.bfloat16)
    mid = jnp.dot(
        jnp.concatenate([match_real, match_imag], axis=1), inv_t, preferred_element_type=jnp.float32
    )
    turn_real, turn_imag = twist(mid[:, :side], mid[:, side:], (down(inv_tw[0]), down(inv_tw[1])))
    rows_of = lambda x, p: x[p * side : (p + 1) * side]
    stacked = jnp.concatenate(
        [
            jnp.concatenate([rows_of(turn_real, p), rows_of(turn_imag, p)], axis=0)
            for p in range(pulses)
        ],
        axis=1,
    )
    comp = jnp.dot(inv, stacked, preferred_element_type=jnp.float32)
    out_ref[...] = pltpu.einshape("(rd)(pb)->(drp)b", comp, r=2, p=pulses).astype(jnp.bfloat16)


def range_compress(echo, range_replica):
    pulses, length = echo.shape[1], echo.shape[2]
    side = RSPLIT
    assert length == side * side
    assert range_replica.shape[1] % side == 0 and range_replica.shape[1] <= length
    rows = echo.reshape(2, pulses, side, side).transpose(0, 2, 1, 3).reshape(2, side * pulses, side)
    fwd, fwd_t = host_tables(side, -1)
    inv, inv_t = host_tables(side, 1)
    fwd_tw = host_twiddle(side, side, -1)
    inv_tw = host_twiddle(side, side, 1)
    whole = pl.BlockSpec(memory_space=pltpu.VMEM)
    out = pl.pallas_call(
        range_kernel,
        in_specs=[whole] * 8,
        out_specs=whole,
        out_shape=jax.ShapeDtypeStruct((side * 2 * pulses, side), jnp.bfloat16),
        cost_estimate=pl.CostEstimate(
            flops=(pulses + 1) * 4 * 2 * (2 * side) ** 2 * side,
            bytes_accessed=pulses * 2 * 2 * length * 2,
            transcendentals=0,
        ),
    )(
        rows,
        range_replica,
        jnp.asarray(fwd),
        jnp.asarray(fwd_t),
        jnp.asarray(inv),
        jnp.asarray(inv_t),
        jnp.asarray(fwd_tw),
        jnp.asarray(inv_tw),
    )
    return out.reshape(side, 2, pulses, side)


def host_block_table4(size, sign):
    index = np.arange(size, dtype=np.int64)
    product = (index[:, None] * index[None, :] % size).astype(np.float32)
    angle = np.float32(sign * 2.0 * math.pi / size) * product
    norm = np.float32(1.0 / math.sqrt(size))
    cos = (np.cos(angle) * norm).astype(ml_dtypes.bfloat16)
    sin = (np.sin(angle) * norm).astype(ml_dtypes.bfloat16)
    return np.stack([np.stack([cos, -sin], axis=1), np.stack([sin, cos], axis=1)])


def pulse_transform(values, first, sign):
    length, width = values.shape[1], values.shape[2]
    second = length // first
    head = jnp.asarray(host_block_table4(first, sign))
    tail = jnp.asarray(host_block_table4(second, sign))
    twist_cos, twist_sin = (jnp.asarray(t) for t in host_twiddle(first, second, sign))
    split = values.reshape(2, first, second, width)
    mid = jnp.einsum("okrn,rnmc->okmc", head, split, preferred_element_type=jnp.float32)
    mid_real, mid_imag = mid[0], mid[1]
    turn_real = mid_real * twist_cos[:, :, None] - mid_imag * twist_sin[:, :, None]
    turn_imag = mid_real * twist_sin[:, :, None] + mid_imag * twist_cos[:, :, None]
    turned = jnp.stack([turn_real, turn_imag]).astype(jnp.bfloat16)
    out = jnp.einsum("ojrm,rkmc->ojkc", tail, turned, preferred_element_type=jnp.float32)
    return out.reshape(2, length, width)


def per_device(raw_echo, range_replica, interp_weight, band_offset, azimuth_rate, tile_owner):
    echo = raw_echo[:, 0]
    length = echo.shape[2]
    compressed = range_compress(echo, range_replica)
    devices = lax.axis_size("wide")
    width = length // devices
    assert compressed.shape[0] == devices and compressed.shape[3] == width
    turned = lax.all_to_all(compressed, "wide", split_axis=0, concat_axis=2, tiled=True)[0]
    doppler = pulse_transform(turned, PUL_DEV, -1).astype(jnp.bfloat16)
    rim = passed_along(doppler[:, :, :HALO], "wide", -1)
    extended = jnp.concatenate([doppler, rim], axis=2)
    pulses = extended.shape[1]
    columns = jnp.arange(width + HALO, dtype=jnp.int32)
    bins = jnp.arange(width, dtype=jnp.int32) + band_offset
    moved_real = jnp.zeros((pulses, width), jnp.float32)
    moved_imag = jnp.zeros((pulses, width), jnp.float32)
    taps = interp_weight.shape[0]
    targets = (bins[None, :] + jnp.arange(taps, dtype=jnp.int32)[:, None]).reshape(taps * width)
    select = (columns[:, None] == targets[None, :]).astype(jnp.bfloat16)
    picked = jnp.einsum("xpc,cn->xpn", extended, select, preferred_element_type=jnp.bfloat16)
    for tap_index in range(taps):
        weight = interp_weight[tap_index][:, None]
        tap_values = picked[:, :, tap_index * width : (tap_index + 1) * width].astype(jnp.float32)
        moved_real = moved_real + weight * tap_values[0]
        moved_imag = moved_imag + weight * tap_values[1]
    half = pulses // 2
    freq = jnp.arange(half + 1, dtype=jnp.int32)
    shifted = ((freq + half) % pulses - half).astype(jnp.float32) / pulses
    phase = math.pi * (shifted * shifted)[:, None] / azimuth_rate[None, :]
    half_cos = jnp.cos(phase)
    half_sin = jnp.sin(phase)
    phase_cos = jnp.concatenate([half_cos, jnp.flip(half_cos[1:half], 0)], axis=0)
    phase_sin = jnp.concatenate([half_sin, jnp.flip(half_sin[1:half], 0)], axis=0)
    focus_real = (moved_real * phase_cos - moved_imag * phase_sin).astype(jnp.bfloat16)
    focus_imag = (moved_real * phase_sin + moved_imag * phase_cos).astype(jnp.bfloat16)
    image = pulse_transform(jnp.stack([focus_real, focus_imag]), PUL_DEV, 1)
    intensity = (image[0] * image[0] + image[1] * image[1]).astype(jnp.bfloat16)
    block_count = tile_owner.shape[1]
    block_rows = pulses // block_count
    blocks = intensity.reshape(block_count, block_rows * width)
    tiles = lax.axis_size("narrow")
    group = lax.axis_index("narrow")
    tile_ids = jnp.arange(tiles, dtype=jnp.int32)
    own_row = lax.dynamic_slice_in_dim(tile_owner, group, 1, 0)[0]
    member = (own_row[None, :] == tile_ids[:, None]).astype(jnp.bfloat16)
    counts = jnp.sum(
        (tile_owner[:, :, None] == tile_ids[None, None, :]).astype(jnp.int32), axis=(0, 1)
    )
    own_count = jnp.sum(jnp.where(tile_ids == group, counts, 0)).astype(jnp.float32)
    partial = jnp.dot(member, blocks, preferred_element_type=jnp.float32)
    partial = partial.reshape(tiles, block_rows, width)
    incoming = lax.all_to_all(partial, "narrow", split_axis=0, concat_axis=0, tiled=True)
    summed = jnp.sum(incoming, axis=0)[None]
    return summed / own_count


def solution(mesh):
    return jax.shard_map(
        per_device,
        mesh=mesh,
        in_specs=(P(None, "narrow", "wide", None), P(), P(), P("wide"), P("wide"), P()),
        out_specs=P("narrow", None, "wide"),
        check_vma=False,
    )
```

```python
import math

import jax
import jax.numpy as jnp
import ml_dtypes
import numpy as np
from jax import lax
from jax.experimental import pallas as pl
from jax.experimental.pallas import tpu as pltpu
from jax.sharding import PartitionSpec as P

RSPLIT = 128
PUL_DEV = 8
CAP = 8
HALO = 31


def passed_along(shard, axis, by):
    devices = lax.axis_size(axis)
    pairs = [(i, i + by) for i in range(devices) if 0 <= i + by < devices]
    return lax.ppermute(shard, axis, pairs)


def host_twiddle(first, second, sign):
    heads = np.arange(first, dtype=np.int64)
    tails = np.arange(second, dtype=np.int64)
    product = (heads[:, None] * tails[None, :] % (first * second)).astype(np.float32)
    angle = np.float32(sign * 2.0 * math.pi / (first * second)) * product
    return np.stack([np.cos(angle), np.sin(angle)]).astype(np.float32)


def host_tables(size, sign):
    index = np.arange(size, dtype=np.int64)
    product = (index[:, None] * index[None, :] % size).astype(np.float32)
    angle = np.float32(sign * 2.0 * math.pi / size) * product
    norm = np.float32(1.0 / math.sqrt(size))
    cos = (np.cos(angle) * norm).astype(ml_dtypes.bfloat16)
    sin = (np.sin(angle) * norm).astype(ml_dtypes.bfloat16)
    table = np.block([[cos, -sin], [sin, cos]])
    return table, np.ascontiguousarray(table.T)


def twist(mid_real, mid_imag, twiddle):
    twist_cos, twist_sin = twiddle[0], twiddle[1]
    turn_real = (mid_real * twist_cos - mid_imag * twist_sin).astype(jnp.bfloat16)
    turn_imag = (mid_real * twist_sin + mid_imag * twist_cos).astype(jnp.bfloat16)
    return turn_real, turn_imag


def forward_transposed(stacked, table, table_t, twiddle):
    half = stacked.shape[0] // 2
    mid = jnp.dot(table, stacked, preferred_element_type=jnp.float32)
    turn_real, turn_imag = twist(mid[:half], mid[half:], twiddle)
    spec = jnp.dot(
        jnp.concatenate([turn_real, turn_imag], axis=1), table_t, preferred_element_type=jnp.float32
    )
    return spec[:, :half], spec[:, half:]


def inverse_from_transposed(real_t, imag_t, table, table_t, twiddle):
    half = real_t.shape[0]
    mid = jnp.dot(
        jnp.concatenate([real_t, imag_t], axis=1), table_t, preferred_element_type=jnp.float32
    )
    turn_real, turn_imag = twist(mid[:, :half], mid[:, half:], twiddle)
    out = jnp.dot(
        table, jnp.concatenate([turn_real, turn_imag], axis=0), preferred_element_type=jnp.float32
    )
    return out[:half], out[half:]


def range_kernel(
    echo_ref, replica_ref, fwd_ref, fwd_t_ref, inv_ref, inv_t_ref, fwd_tw_ref, inv_tw_ref, out_ref
):
    pulses = echo_ref.shape[1] // echo_ref.shape[2]
    side = echo_ref.shape[2]
    fwd, fwd_t = fwd_ref[...], fwd_t_ref[...]
    inv, inv_t = inv_ref[...], inv_t_ref[...]
    fwd_tw, inv_tw = fwd_tw_ref[...], inv_tw_ref[...]
    taps = replica_ref[...].astype(jnp.float32)
    filled = taps.shape[1] // side
    blank = jnp.zeros((side - filled, side), jnp.float32)
    pieces = []
    for part in range(2):
        pieces += [taps[part : part + 1, n * side : (n + 1) * side] for n in range(filled)]
        pieces.append(blank)
    replica = jnp.concatenate(pieces, axis=0).astype(jnp.bfloat16)
    rep_real, rep_imag = forward_transposed(replica, fwd, fwd_t, fwd_tw)
    rep_real = rep_real * 128.0
    rep_imag = rep_imag * 128.0
    blocks = []
    for pulse in range(pulses):
        rows = pl.ds(pulse, side, stride=pulses)
        blocks.append(jnp.concatenate([echo_ref[0, rows, :], echo_ref[1, rows, :]], axis=0))
    mid = jnp.dot(fwd, jnp.concatenate(blocks, axis=1), preferred_element_type=jnp.float32)
    along = lambda x: jnp.concatenate([x] * pulses, axis=1)
    down = lambda x: jnp.concatenate([x] * pulses, axis=0)
    turn_real, turn_imag = twist(mid[:side], mid[side:], (along(fwd_tw[0]), along(fwd_tw[1])))
    by_pulse = lambda x, p: x[:, p * side : (p + 1) * side]
    stacked = jnp.concatenate(
        [
            jnp.concatenate([by_pulse(turn_real, p), by_pulse(turn_imag, p)], axis=1)
            for p in range(pulses)
        ],
        axis=0,
    )
    spec = jnp.dot(stacked, fwd_t, preferred_element_type=jnp.float32)
    spec_real, spec_imag = spec[:, :side], spec[:, side:]
    rep_real, rep_imag = down(rep_real), down(rep_imag)
    match_real = (spec_real * rep_real + spec_imag * rep_imag).astype(jnp.bfloat16)
    match_imag = (spec_imag * rep_real - spec_real * rep_imag).astype(jnp.bfloat16)
    mid = jnp.dot(
        jnp.concatenate([match_real, match_imag], axis=1), inv_t, preferred_element_type=jnp.float32
    )
    turn_real, turn_imag = twist(mid[:, :side], mid[:, side:], (down(inv_tw[0]), down(inv_tw[1])))
    rows_of = lambda x, p: x[p * side : (p + 1) * side]
    stacked = jnp.concatenate(
        [
            jnp.concatenate([rows_of(turn_real, p), rows_of(turn_imag, p)], axis=0)
            for p in range(pulses)
        ],
        axis=1,
    )
    comp = jnp.dot(inv, stacked, preferred_element_type=jnp.float32)
    out_ref[...] = pltpu.einshape("(rd)(pb)->(drp)b", comp, r=2, p=pulses).astype(jnp.bfloat16)


def range_compress(echo, range_replica):
    pulses, length = echo.shape[1], echo.shape[2]
    side = RSPLIT
    assert length == side * side
    assert range_replica.shape[1] % side == 0 and range_replica.shape[1] <= length
    rows = echo.reshape(2, pulses, side, side).transpose(0, 2, 1, 3).reshape(2, side * pulses, side)
    fwd, fwd_t = host_tables(side, -1)
    inv, inv_t = host_tables(side, 1)
    fwd_tw = host_twiddle(side, side, -1)
    inv_tw = host_twiddle(side, side, 1)
    whole = pl.BlockSpec(memory_space=pltpu.VMEM)
    out = pl.pallas_call(
        range_kernel,
        in_specs=[whole] * 8,
        out_specs=whole,
        out_shape=jax.ShapeDtypeStruct((side * 2 * pulses, side), jnp.bfloat16),
        cost_estimate=pl.CostEstimate(
            flops=(pulses + 1) * 4 * 2 * (2 * side) ** 2 * side,
            bytes_accessed=pulses * 2 * 2 * length * 2,
            transcendentals=0,
        ),
    )(
        rows,
        range_replica,
        jnp.asarray(fwd),
        jnp.asarray(fwd_t),
        jnp.asarray(inv),
        jnp.asarray(inv_t),
        jnp.asarray(fwd_tw),
        jnp.asarray(inv_tw),
    )
    return out.reshape(side, 2, pulses, side)


def host_block_table4(size, sign):
    index = np.arange(size, dtype=np.int64)
    product = (index[:, None] * index[None, :] % size).astype(np.float32)
    angle = np.float32(sign * 2.0 * math.pi / size) * product
    norm = np.float32(1.0 / math.sqrt(size))
    cos = (np.cos(angle) * norm).astype(ml_dtypes.bfloat16)
    sin = (np.sin(angle) * norm).astype(ml_dtypes.bfloat16)
    return np.stack([np.stack([cos, -sin], axis=1), np.stack([sin, cos], axis=1)])


def pulse_transform(values, first, sign):
    length, width = values.shape[1], values.shape[2]
    second = length // first
    head = jnp.asarray(host_block_table4(first, sign))
    tail = jnp.asarray(host_block_table4(second, sign))
    twist_cos, twist_sin = (jnp.asarray(t) for t in host_twiddle(first, second, sign))
    split = values.reshape(2, first, second, width)
    mid = jnp.einsum("okrn,rnmc->okmc", head, split, preferred_element_type=jnp.float32)
    mid_real, mid_imag = mid[0], mid[1]
    turn_real = mid_real * twist_cos[:, :, None] - mid_imag * twist_sin[:, :, None]
    turn_imag = mid_real * twist_sin[:, :, None] + mid_imag * twist_cos[:, :, None]
    turned = jnp.stack([turn_real, turn_imag]).astype(jnp.bfloat16)
    out = jnp.einsum("ojrm,rkmc->ojkc", tail, turned, preferred_element_type=jnp.float32)
    return out.reshape(2, length, width)


def per_device(raw_echo, range_replica, interp_weight, band_offset, azimuth_rate, tile_owner):
    echo = raw_echo[:, 0]
    length = echo.shape[2]
    compressed = range_compress(echo, range_replica)
    devices = lax.axis_size("wide")
    width = length // devices
    assert compressed.shape[0] == devices and compressed.shape[3] == width
    turned = lax.all_to_all(compressed, "wide", split_axis=0, concat_axis=2, tiled=True)[0]
    spectra = pulse_transform(turned, PUL_DEV, -1)
    doppler = spectra.astype(jnp.bfloat16)
    rim = passed_along(spectra[:, :, :HALO].astype(jnp.bfloat16), "wide", -1)
    extended = jnp.concatenate([doppler, rim], axis=2)
    pulses = extended.shape[1]
    columns = jnp.arange(width + HALO, dtype=jnp.int32)
    bins = jnp.arange(width, dtype=jnp.int32) + band_offset
    moved_real = jnp.zeros((pulses, width), jnp.float32)
    moved_imag = jnp.zeros((pulses, width), jnp.float32)
    taps = interp_weight.shape[0]
    targets = (bins[None, :] + jnp.arange(taps, dtype=jnp.int32)[:, None]).reshape(taps * width)
    select = (columns[:, None] == targets[None, :]).astype(jnp.bfloat16)
    picked = jnp.einsum("xpc,cn->xpn", extended, select, preferred_element_type=jnp.bfloat16)
    for tap_index in range(taps):
        weight = interp_weight[tap_index][:, None]
        tap_values = picked[:, :, tap_index * width : (tap_index + 1) * width].astype(jnp.float32)
        moved_real = moved_real + weight * tap_values[0]
        moved_imag = moved_imag + weight * tap_values[1]
    half = pulses // 2
    freq = jnp.arange(half + 1, dtype=jnp.int32)
    shifted = ((freq + half) % pulses - half).astype(jnp.float32) / pulses
    phase = math.pi * (shifted * shifted)[:, None] / azimuth_rate[None, :]
    half_cos = jnp.cos(phase)
    half_sin = jnp.sin(phase)
    phase_cos = jnp.concatenate([half_cos, jnp.flip(half_cos[1:half], 0)], axis=0)
    phase_sin = jnp.concatenate([half_sin, jnp.flip(half_sin[1:half], 0)], axis=0)
    focus_real = (moved_real * phase_cos - moved_imag * phase_sin).astype(jnp.bfloat16)
    focus_imag = (moved_real * phase_sin + moved_imag * phase_cos).astype(jnp.bfloat16)
    image = pulse_transform(jnp.stack([focus_real, focus_imag]), PUL_DEV, 1)
    intensity = (image[0] * image[0] + image[1] * image[1]).astype(jnp.bfloat16)
    block_count = tile_owner.shape[1]
    block_rows = pulses // block_count
    second = pulses // PUL_DEV
    per_block = block_rows // PUL_DEV
    blocks = intensity.reshape(second, PUL_DEV, width).transpose(1, 0, 2)
    blocks = blocks.reshape(PUL_DEV, block_count, per_block, width)
    tiles = lax.axis_size("narrow")
    group = lax.axis_index("narrow")
    tile_ids = jnp.arange(tiles, dtype=jnp.int32)
    own_row = lax.dynamic_slice_in_dim(tile_owner, group, 1, 0)[0]
    member = (own_row[None, :] == tile_ids[:, None]).astype(jnp.bfloat16)
    counts = jnp.sum(
        (tile_owner[:, :, None] == tile_ids[None, None, :]).astype(jnp.int32), axis=(0, 1)
    )
    own_count = jnp.sum(jnp.where(tile_ids == group, counts, 0)).astype(jnp.float32)
    partial = jnp.einsum("tb,kbjc->tkjc", member, blocks, preferred_element_type=jnp.float32)
    incoming = lax.all_to_all(partial, "narrow", split_axis=0, concat_axis=0, tiled=True)
    summed = jnp.sum(incoming, axis=0).transpose(1, 0, 2).reshape(1, block_rows, width)
    return summed / own_count


def solution(mesh):
    return jax.shard_map(
        per_device,
        mesh=mesh,
        in_specs=(P(None, "narrow", "wide", None), P(), P(), P("wide"), P("wide"), P()),
        out_specs=P("narrow", None, "wide"),
        check_vma=False,
    )
```

```python
import math

import jax
import jax.numpy as jnp
import ml_dtypes
import numpy as np
from jax import lax
from jax.experimental import pallas as pl
from jax.experimental.pallas import tpu as pltpu
from jax.sharding import PartitionSpec as P

RSPLIT = 128
PUL_DEV = 8
CAP = 8
HALO = 31


def passed_along(shard, axis, by):
    devices = lax.axis_size(axis)
    pairs = [(i, i + by) for i in range(devices) if 0 <= i + by < devices]
    return lax.ppermute(shard, axis, pairs)


def host_twiddle(first, second, sign):
    heads = np.arange(first, dtype=np.int64)
    tails = np.arange(second, dtype=np.int64)
    product = (heads[:, None] * tails[None, :] % (first * second)).astype(np.float32)
    angle = np.float32(sign * 2.0 * math.pi / (first * second)) * product
    return np.stack([np.cos(angle), np.sin(angle)]).astype(np.float32)


def host_tables(size, sign):
    index = np.arange(size, dtype=np.int64)
    product = (index[:, None] * index[None, :] % size).astype(np.float32)
    angle = np.float32(sign * 2.0 * math.pi / size) * product
    norm = np.float32(1.0 / math.sqrt(size))
    cos = (np.cos(angle) * norm).astype(ml_dtypes.bfloat16)
    sin = (np.sin(angle) * norm).astype(ml_dtypes.bfloat16)
    table = np.block([[cos, -sin], [sin, cos]])
    return table, np.ascontiguousarray(table.T)


def twist(mid_real, mid_imag, twiddle):
    twist_cos, twist_sin = twiddle[0], twiddle[1]
    turn_real = (mid_real * twist_cos - mid_imag * twist_sin).astype(jnp.bfloat16)
    turn_imag = (mid_real * twist_sin + mid_imag * twist_cos).astype(jnp.bfloat16)
    return turn_real, turn_imag


def forward_transposed(stacked, table, table_t, twiddle):
    half = stacked.shape[0] // 2
    mid = jnp.dot(table, stacked, preferred_element_type=jnp.float32)
    turn_real, turn_imag = twist(mid[:half], mid[half:], twiddle)
    spec = jnp.dot(
        jnp.concatenate([turn_real, turn_imag], axis=1), table_t, preferred_element_type=jnp.float32
    )
    return spec[:, :half], spec[:, half:]


def inverse_from_transposed(real_t, imag_t, table, table_t, twiddle):
    half = real_t.shape[0]
    mid = jnp.dot(
        jnp.concatenate([real_t, imag_t], axis=1), table_t, preferred_element_type=jnp.float32
    )
    turn_real, turn_imag = twist(mid[:, :half], mid[:, half:], twiddle)
    out = jnp.dot(
        table, jnp.concatenate([turn_real, turn_imag], axis=0), preferred_element_type=jnp.float32
    )
    return out[:half], out[half:]


def range_kernel(
    echo_ref, replica_ref, fwd_ref, fwd_t_ref, inv_ref, inv_t_ref, fwd_tw_ref, inv_tw_ref, out_ref
):
    pulses = echo_ref.shape[1] // echo_ref.shape[2]
    side = echo_ref.shape[2]
    fwd, fwd_t = fwd_ref[...], fwd_t_ref[...]
    inv, inv_t = inv_ref[...], inv_t_ref[...]
    fwd_tw, inv_tw = fwd_tw_ref[...], inv_tw_ref[...]
    taps = replica_ref[...].astype(jnp.float32)
    filled = taps.shape[1] // side
    rows = pltpu.einshape("r(nb)->(rn)b", taps, b=side)
    blank = jnp.zeros((side - filled, side), jnp.float32)
    replica = jnp.concatenate([rows[:filled], blank, rows[filled:], blank], axis=0)
    replica = replica.astype(jnp.bfloat16)
    rep_real, rep_imag = forward_transposed(replica, fwd, fwd_t, fwd_tw)
    rep_real = rep_real * 128.0
    rep_imag = rep_imag * 128.0
    blocks = []
    for pulse in range(pulses):
        rows = pl.ds(pulse, side, stride=pulses)
        blocks.append(jnp.concatenate([echo_ref[0, rows, :], echo_ref[1, rows, :]], axis=0))
    mid = jnp.dot(fwd, jnp.concatenate(blocks, axis=1), preferred_element_type=jnp.float32)
    along = lambda x: jnp.concatenate([x] * pulses, axis=1)
    down = lambda x: jnp.concatenate([x] * pulses, axis=0)
    turn_real, turn_imag = twist(mid[:side], mid[side:], (along(fwd_tw[0]), along(fwd_tw[1])))
    by_pulse = lambda x, p: x[:, p * side : (p + 1) * side]
    stacked = jnp.concatenate(
        [
            jnp.concatenate([by_pulse(turn_real, p), by_pulse(turn_imag, p)], axis=1)
            for p in range(pulses)
        ],
        axis=0,
    )
    spec = jnp.dot(stacked, fwd_t, preferred_element_type=jnp.float32)
    spec_real, spec_imag = spec[:, :side], spec[:, side:]
    rep_real, rep_imag = down(rep_real), down(rep_imag)
    match_real = (spec_real * rep_real + spec_imag * rep_imag).astype(jnp.bfloat16)
    match_imag = (spec_imag * rep_real - spec_real * rep_imag).astype(jnp.bfloat16)
    mid = jnp.dot(
        jnp.concatenate([match_real, match_imag], axis=1), inv_t, preferred_element_type=jnp.float32
    )
    turn_real, turn_imag = twist(mid[:, :side], mid[:, side:], (down(inv_tw[0]), down(inv_tw[1])))
    rows_of = lambda x, p: x[p * side : (p + 1) * side]
    stacked = jnp.concatenate(
        [
            jnp.concatenate([rows_of(turn_real, p), rows_of(turn_imag, p)], axis=0)
            for p in range(pulses)
        ],
        axis=1,
    )
    comp = jnp.dot(inv, stacked, preferred_element_type=jnp.float32)
    out_ref[...] = pltpu.einshape("(rd)(pb)->(drp)b", comp, r=2, p=pulses).astype(jnp.bfloat16)


def range_compress(echo, range_replica):
    pulses, length = echo.shape[1], echo.shape[2]
    side = RSPLIT
    assert length == side * side
    assert range_replica.shape[1] % side == 0 and range_replica.shape[1] <= length
    rows = echo.reshape(2, pulses, side, side).transpose(0, 2, 1, 3).reshape(2, side * pulses, side)
    fwd, fwd_t = host_tables(side, -1)
    inv, inv_t = host_tables(side, 1)
    fwd_tw = host_twiddle(side, side, -1)
    inv_tw = host_twiddle(side, side, 1)
    whole = pl.BlockSpec(memory_space=pltpu.VMEM)
    out = pl.pallas_call(
        range_kernel,
        in_specs=[whole] * 8,
        out_specs=whole,
        out_shape=jax.ShapeDtypeStruct((side * 2 * pulses, side), jnp.bfloat16),
        cost_estimate=pl.CostEstimate(
            flops=(pulses + 1) * 4 * 2 * (2 * side) ** 2 * side,
            bytes_accessed=pulses * 2 * 2 * length * 2,
            transcendentals=0,
        ),
    )(
        rows,
        range_replica,
        jnp.asarray(fwd),
        jnp.asarray(fwd_t),
        jnp.asarray(inv),
        jnp.asarray(inv_t),
        jnp.asarray(fwd_tw),
        jnp.asarray(inv_tw),
    )
    return out.reshape(side, 2, pulses, side)


def host_block_table4(size, sign):
    index = np.arange(size, dtype=np.int64)
    product = (index[:, None] * index[None, :] % size).astype(np.float32)
    angle = np.float32(sign * 2.0 * math.pi / size) * product
    norm = np.float32(1.0 / math.sqrt(size))
    cos = (np.cos(angle) * norm).astype(ml_dtypes.bfloat16)
    sin = (np.sin(angle) * norm).astype(ml_dtypes.bfloat16)
    return np.stack([np.stack([cos, -sin], axis=1), np.stack([sin, cos], axis=1)])


def pulse_transform(values, first, sign):
    length, width = values.shape[1], values.shape[2]
    second = length // first
    head = jnp.asarray(host_block_table4(first, sign))
    tail = jnp.asarray(host_block_table4(second, sign))
    twist_cos, twist_sin = (jnp.asarray(t) for t in host_twiddle(first, second, sign))
    split = values.reshape(2, first, second, width)
    mid = jnp.einsum("okrn,rnmc->okmc", head, split, preferred_element_type=jnp.float32)
    mid_real, mid_imag = mid[0], mid[1]
    turn_real = mid_real * twist_cos[:, :, None] - mid_imag * twist_sin[:, :, None]
    turn_imag = mid_real * twist_sin[:, :, None] + mid_imag * twist_cos[:, :, None]
    turned = jnp.stack([turn_real, turn_imag]).astype(jnp.bfloat16)
    out = jnp.einsum("ojrm,rkmc->ojkc", tail, turned, preferred_element_type=jnp.float32)
    return out.reshape(2, length, width)


def per_device(raw_echo, range_replica, interp_weight, band_offset, azimuth_rate, tile_owner):
    echo = raw_echo[:, 0]
    length = echo.shape[2]
    compressed = range_compress(echo, range_replica)
    devices = lax.axis_size("wide")
    width = length // devices
    assert compressed.shape[0] == devices and compressed.shape[3] == width
    turned = lax.all_to_all(compressed, "wide", split_axis=0, concat_axis=2, tiled=True)[0]
    spectra = pulse_transform(turned, PUL_DEV, -1)
    doppler = spectra.astype(jnp.bfloat16)
    rim = passed_along(spectra[:, :, :HALO].astype(jnp.bfloat16), "wide", -1)
    extended = jnp.concatenate([doppler, rim], axis=2)
    pulses = extended.shape[1]
    columns = jnp.arange(width + HALO, dtype=jnp.int32)
    bins = jnp.arange(width, dtype=jnp.int32) + band_offset
    moved_real = jnp.zeros((pulses, width), jnp.float32)
    moved_imag = jnp.zeros((pulses, width), jnp.float32)
    taps = interp_weight.shape[0]
    targets = (bins[None, :] + jnp.arange(taps, dtype=jnp.int32)[:, None]).reshape(taps * width)
    select = (columns[:, None] == targets[None, :]).astype(jnp.bfloat16)
    picked = jnp.einsum("xpc,cn->xpn", extended, select, preferred_element_type=jnp.bfloat16)
    for tap_index in range(taps):
        weight = interp_weight[tap_index][:, None]
        tap_values = picked[:, :, tap_index * width : (tap_index + 1) * width].astype(jnp.float32)
        moved_real = moved_real + weight * tap_values[0]
        moved_imag = moved_imag + weight * tap_values[1]
    half = pulses // 2
    freq = jnp.arange(half + 1, dtype=jnp.int32)
    shifted = ((freq + half) % pulses - half).astype(jnp.float32) / pulses
    phase = math.pi * (shifted * shifted)[:, None] / azimuth_rate[None, :]
    half_cos = jnp.cos(phase)
    half_sin = jnp.sin(phase)
    phase_cos = jnp.concatenate([half_cos, jnp.flip(half_cos[1:half], 0)], axis=0)
    phase_sin = jnp.concatenate([half_sin, jnp.flip(half_sin[1:half], 0)], axis=0)
    focus_real = (moved_real * phase_cos - moved_imag * phase_sin).astype(jnp.bfloat16)
    focus_imag = (moved_real * phase_sin + moved_imag * phase_cos).astype(jnp.bfloat16)
    image = pulse_transform(jnp.stack([focus_real, focus_imag]), PUL_DEV, 1)
    intensity = (image[0] * image[0] + image[1] * image[1]).astype(jnp.bfloat16)
    block_count = tile_owner.shape[1]
    block_rows = pulses // block_count
    second = pulses // PUL_DEV
    per_block = block_rows // PUL_DEV
    blocks = intensity.reshape(second, PUL_DEV, width).transpose(1, 0, 2)
    blocks = blocks.reshape(PUL_DEV, block_count, per_block, width)
    tiles = lax.axis_size("narrow")
    group = lax.axis_index("narrow")
    tile_ids = jnp.arange(tiles, dtype=jnp.int32)
    own_row = lax.dynamic_slice_in_dim(tile_owner, group, 1, 0)[0]
    member = (own_row[None, :] == tile_ids[:, None]).astype(jnp.bfloat16)
    counts = jnp.sum(
        (tile_owner[:, :, None] == tile_ids[None, None, :]).astype(jnp.int32), axis=(0, 1)
    )
    own_count = jnp.sum(jnp.where(tile_ids == group, counts, 0)).astype(jnp.float32)
    partial = jnp.einsum("tb,kbjc->tkjc", member, blocks, preferred_element_type=jnp.float32)
    incoming = lax.all_to_all(partial, "narrow", split_axis=0, concat_axis=0, tiled=True)
    summed = jnp.sum(incoming, axis=0).transpose(1, 0, 2).reshape(1, block_rows, width)
    return summed / own_count


def solution(mesh):
    return jax.shard_map(
        per_device,
        mesh=mesh,
        in_specs=(P(None, "narrow", "wide", None), P(), P(), P("wide"), P("wide"), P()),
        out_specs=P("narrow", None, "wide"),
        check_vma=False,
    )
```

```python
import math

import jax
import jax.numpy as jnp
import ml_dtypes
import numpy as np
from jax import lax
from jax.experimental import pallas as pl
from jax.experimental.pallas import tpu as pltpu
from jax.sharding import PartitionSpec as P

RSPLIT = 128
PUL_DEV = 8
CAP = 8
HALO = 31


def passed_along(shard, axis, by):
    devices = lax.axis_size(axis)
    pairs = [(i, i + by) for i in range(devices) if 0 <= i + by < devices]
    return lax.ppermute(shard, axis, pairs)


def host_twiddle(first, second, sign):
    heads = np.arange(first, dtype=np.int64)
    tails = np.arange(second, dtype=np.int64)
    product = (heads[:, None] * tails[None, :] % (first * second)).astype(np.float32)
    angle = np.float32(sign * 2.0 * math.pi / (first * second)) * product
    return np.stack([np.cos(angle), np.sin(angle)]).astype(np.float32)


def host_tables(size, sign):
    index = np.arange(size, dtype=np.int64)
    product = (index[:, None] * index[None, :] % size).astype(np.float32)
    angle = np.float32(sign * 2.0 * math.pi / size) * product
    norm = np.float32(1.0 / math.sqrt(size))
    cos = (np.cos(angle) * norm).astype(ml_dtypes.bfloat16)
    sin = (np.sin(angle) * norm).astype(ml_dtypes.bfloat16)
    table = np.block([[cos, -sin], [sin, cos]])
    return table, np.ascontiguousarray(table.T)


def twist(mid_real, mid_imag, twiddle):
    twist_cos, twist_sin = twiddle[0], twiddle[1]
    turn_real = (mid_real * twist_cos - mid_imag * twist_sin).astype(jnp.bfloat16)
    turn_imag = (mid_real * twist_sin + mid_imag * twist_cos).astype(jnp.bfloat16)
    return turn_real, turn_imag


def forward_transposed(stacked, table, table_t, twiddle):
    half = stacked.shape[0] // 2
    mid = jnp.dot(table, stacked, preferred_element_type=jnp.float32)
    turn_real, turn_imag = twist(mid[:half], mid[half:], twiddle)
    spec = jnp.dot(
        jnp.concatenate([turn_real, turn_imag], axis=1), table_t, preferred_element_type=jnp.float32
    )
    return spec[:, :half], spec[:, half:]


def inverse_from_transposed(real_t, imag_t, table, table_t, twiddle):
    half = real_t.shape[0]
    mid = jnp.dot(
        jnp.concatenate([real_t, imag_t], axis=1), table_t, preferred_element_type=jnp.float32
    )
    turn_real, turn_imag = twist(mid[:, :half], mid[:, half:], twiddle)
    out = jnp.dot(
        table, jnp.concatenate([turn_real, turn_imag], axis=0), preferred_element_type=jnp.float32
    )
    return out[:half], out[half:]


def range_kernel(
    echo_ref, replica_ref, fwd_ref, fwd_t_ref, inv_ref, inv_t_ref, fwd_tw_ref, inv_tw_ref, out_ref
):
    pulses = echo_ref.shape[1] // echo_ref.shape[2]
    side = echo_ref.shape[2]
    fwd, fwd_t = fwd_ref[...], fwd_t_ref[...]
    inv, inv_t = inv_ref[...], inv_t_ref[...]
    fwd_tw, inv_tw = fwd_tw_ref[...], inv_tw_ref[...]
    taps = replica_ref[...].astype(jnp.float32)
    filled = taps.shape[1] // side
    rows = pltpu.einshape("r(nb)->(rn)b", taps, b=side)
    blank = jnp.zeros((side - filled, side), jnp.float32)
    replica = jnp.concatenate([rows[:filled], blank, rows[filled:], blank], axis=0)
    replica = replica.astype(jnp.bfloat16)
    rep_real, rep_imag = forward_transposed(replica, fwd, fwd_t, fwd_tw)
    rep_real = rep_real * 128.0
    rep_imag = rep_imag * 128.0
    blocks = []
    for pulse in range(pulses):
        rows = pl.ds(pulse, side, stride=pulses)
        blocks.append(jnp.concatenate([echo_ref[0, rows, :], echo_ref[1, rows, :]], axis=0))
    mid = jnp.dot(fwd, jnp.concatenate(blocks, axis=1), preferred_element_type=jnp.float32)
    along = lambda x: jnp.concatenate([x] * pulses, axis=1)
    down = lambda x: jnp.concatenate([x] * pulses, axis=0)
    turn_real, turn_imag = twist(mid[:side], mid[side:], (along(fwd_tw[0]), along(fwd_tw[1])))
    by_pulse = lambda x, p: x[:, p * side : (p + 1) * side]
    stacked = jnp.concatenate(
        [
            jnp.concatenate([by_pulse(turn_real, p), by_pulse(turn_imag, p)], axis=1)
            for p in range(pulses)
        ],
        axis=0,
    )
    spec = jnp.dot(stacked, fwd_t, preferred_element_type=jnp.float32)
    spec_real, spec_imag = spec[:, :side], spec[:, side:]
    rep_real, rep_imag = down(rep_real), down(rep_imag)
    match_real = (spec_real * rep_real + spec_imag * rep_imag).astype(jnp.bfloat16)
    match_imag = (spec_imag * rep_real - spec_real * rep_imag).astype(jnp.bfloat16)
    mid = jnp.dot(
        jnp.concatenate([match_real, match_imag], axis=1), inv_t, preferred_element_type=jnp.float32
    )
    turn_real, turn_imag = twist(mid[:, :side], mid[:, side:], (down(inv_tw[0]), down(inv_tw[1])))
    rows_of = lambda x, p: x[p * side : (p + 1) * side]
    stacked = jnp.concatenate(
        [
            jnp.concatenate([rows_of(turn_real, p), rows_of(turn_imag, p)], axis=0)
            for p in range(pulses)
        ],
        axis=1,
    )
    comp = jnp.dot(inv, stacked, preferred_element_type=jnp.float32)
    out_ref[...] = pltpu.einshape("(rd)(pb)->(drp)b", comp, r=2, p=pulses).astype(jnp.bfloat16)


def range_compress(echo, range_replica):
    pulses, length = echo.shape[1], echo.shape[2]
    side = RSPLIT
    assert length == side * side
    assert range_replica.shape[1] % side == 0 and range_replica.shape[1] <= length
    rows = echo.reshape(2, pulses, side, side).transpose(0, 2, 1, 3).reshape(2, side * pulses, side)
    fwd, fwd_t = host_tables(side, -1)
    inv, inv_t = host_tables(side, 1)
    fwd_tw = host_twiddle(side, side, -1)
    inv_tw = host_twiddle(side, side, 1)
    whole = pl.BlockSpec(memory_space=pltpu.VMEM)
    out = pl.pallas_call(
        range_kernel,
        in_specs=[whole] * 8,
        out_specs=whole,
        out_shape=jax.ShapeDtypeStruct((side * 2 * pulses, side), jnp.bfloat16),
        cost_estimate=pl.CostEstimate(
            flops=(pulses + 1) * 4 * 2 * (2 * side) ** 2 * side,
            bytes_accessed=pulses * 2 * 2 * length * 2,
            transcendentals=0,
        ),
    )(
        rows,
        range_replica,
        jnp.asarray(fwd),
        jnp.asarray(fwd_t),
        jnp.asarray(inv),
        jnp.asarray(inv_t),
        jnp.asarray(fwd_tw),
        jnp.asarray(inv_tw),
    )
    return out.reshape(side, 2, pulses, side)


def host_block_table4(size, sign):
    index = np.arange(size, dtype=np.int64)
    product = (index[:, None] * index[None, :] % size).astype(np.float32)
    angle = np.float32(sign * 2.0 * math.pi / size) * product
    norm = np.float32(1.0 / math.sqrt(size))
    cos = (np.cos(angle) * norm).astype(ml_dtypes.bfloat16)
    sin = (np.sin(angle) * norm).astype(ml_dtypes.bfloat16)
    return np.stack([np.stack([cos, -sin], axis=1), np.stack([sin, cos], axis=1)])


def pulse_transform(values, first, sign):
    length, width = values.shape[1], values.shape[2]
    second = length // first
    head = jnp.asarray(host_block_table4(first, sign))
    tail = jnp.asarray(host_block_table4(second, sign))
    twist_cos, twist_sin = (jnp.asarray(t) for t in host_twiddle(first, second, sign))
    split = values.reshape(2, first, second, width)
    mid = jnp.einsum("okrn,rnmc->okmc", head, split, preferred_element_type=jnp.float32)
    mid_real, mid_imag = mid[0], mid[1]
    turn_real = mid_real * twist_cos[:, :, None] - mid_imag * twist_sin[:, :, None]
    turn_imag = mid_real * twist_sin[:, :, None] + mid_imag * twist_cos[:, :, None]
    turned = jnp.stack([turn_real, turn_imag]).astype(jnp.bfloat16)
    out = jnp.einsum("ojrm,rkmc->ojkc", tail, turned, preferred_element_type=jnp.float32)
    return out.reshape(2, length, width)


def per_device(raw_echo, range_replica, interp_weight, band_offset, azimuth_rate, tile_owner):
    echo = raw_echo[:, 0]
    length = echo.shape[2]
    compressed = range_compress(echo, range_replica)
    devices = lax.axis_size("wide")
    width = length // devices
    assert compressed.shape[0] == devices and compressed.shape[3] == width
    turned = lax.all_to_all(compressed, "wide", split_axis=0, concat_axis=2, tiled=True)[0]
    spectra = pulse_transform(turned, PUL_DEV, -1)
    doppler = spectra.astype(jnp.bfloat16)
    rim = passed_along(spectra[:, :, :HALO].astype(jnp.bfloat16), "wide", -1)
    extended = jnp.concatenate([doppler, rim], axis=2)
    pulses = extended.shape[1]
    columns = jnp.arange(width + HALO, dtype=jnp.int32)
    bins = jnp.arange(width, dtype=jnp.int32) + band_offset
    moved_real = jnp.zeros((pulses, width), jnp.float32)
    moved_imag = jnp.zeros((pulses, width), jnp.float32)
    taps = interp_weight.shape[0]
    targets = (bins[None, :] + jnp.arange(taps, dtype=jnp.int32)[:, None]).reshape(taps * width)
    select = (columns[:, None] == targets[None, :]).astype(jnp.bfloat16)
    picked = jnp.einsum("xpc,cn->xpn", extended, select, preferred_element_type=jnp.bfloat16)
    for tap_index in range(taps):
        weight = interp_weight[tap_index][:, None]
        tap_values = picked[:, :, tap_index * width : (tap_index + 1) * width].astype(jnp.float32)
        moved_real = moved_real + weight * tap_values[0]
        moved_imag = moved_imag + weight * tap_values[1]
    half = pulses // 2
    freq = jnp.arange(half + 1, dtype=jnp.int32)
    shifted = ((freq + half) % pulses - half).astype(jnp.float32) / pulses
    phase = math.pi * (shifted * shifted)[:, None] / azimuth_rate[None, :]
    half_cos = jnp.cos(phase)
    half_sin = jnp.sin(phase)
    phase_cos = jnp.concatenate([half_cos, jnp.flip(half_cos[1:half], 0)], axis=0)
    phase_sin = jnp.concatenate([half_sin, jnp.flip(half_sin[1:half], 0)], axis=0)
    focus_real = (moved_real * phase_cos - moved_imag * phase_sin).astype(jnp.bfloat16)
    focus_imag = (moved_real * phase_sin + moved_imag * phase_cos).astype(jnp.bfloat16)
    image = pulse_transform(jnp.stack([focus_real, focus_imag]), PUL_DEV, 1)
    intensity = (image[0] * image[0] + image[1] * image[1]).astype(jnp.bfloat16)
    block_count = tile_owner.shape[1]
    block_rows = pulses // block_count
    blocks = intensity.reshape(block_count, block_rows * width)
    tiles = lax.axis_size("narrow")
    group = lax.axis_index("narrow")
    tile_ids = jnp.arange(tiles, dtype=jnp.int32)
    own_row = lax.dynamic_slice_in_dim(tile_owner, group, 1, 0)[0]
    member = (own_row[None, :] == tile_ids[:, None]).astype(jnp.bfloat16)
    counts = jnp.sum(
        (tile_owner[:, :, None] == tile_ids[None, None, :]).astype(jnp.int32), axis=(0, 1)
    )
    own_count = jnp.sum(jnp.where(tile_ids == group, counts, 0)).astype(jnp.float32)
    partial = jnp.dot(member, blocks, preferred_element_type=jnp.float32)
    partial = partial.reshape(tiles, block_rows, width)
    incoming = lax.all_to_all(partial, "narrow", split_axis=0, concat_axis=0, tiled=True)
    summed = jnp.sum(incoming, axis=0)[None]
    return summed / own_count


def solution(mesh):
    return jax.shard_map(
        per_device,
        mesh=mesh,
        in_specs=(P(None, "narrow", "wide", None), P(), P(), P("wide"), P("wide"), P()),
        out_specs=P("narrow", None, "wide"),
        check_vma=False,
    )
```
